32 devices in a mesh: survey: 2 (over y), xb: 4 (over z), yb: 2 (over x), tx: 2 (over core).
Axes of the slice: x: 2, y: 2, z: 4, core: 2. Of those that a mesh axis runs over, the one named last changes fastest.
Arguments:
- primaries: bfloat16 [64, 2, 3, 32, 16, 256], P(('survey', 'tx'), None, None, None, 'xb', 'yb'), parts along dimension 0, may hold values from -6 to 6
- conductivity: float32 [6, 32, 16, 256], P('survey', 'tx', 'xb', 'yb'), parts along dimension 0, may hold values from 0.3 to 3
- group_of: int32 [64], P('survey'), parts along dimension 0, may hold values from 0 to 1, as said below
- sign_of: int32 [64], P('survey'), parts along dimension 0, may hold values from -1 to 1, as said below
Outputs:
- secondary: float32 [4, 2, 3, 32, 16, 256], P(('survey', 'tx'), None, None, None, 'xb', 'yb'), parts along dimension 0
The draws below stay inside these ranges and needn't reach their ends.
There are 2 independent parts, one for each index of `survey`. The reference program is written for one: setup_inputs(seed, part) draws one part's arguments, and reference() takes and returns one part's arrays. A program takes and returns all parts, laid end to end along the dimension named above; each array names one. Nothing has to cross between parts.
Inputs may be any that keep to these rules, and one draw needn't show every extreme that they name: `group_of`: every supershot is joined by exactly 16 transmitters. `sign_of`: each weight is -1 or +1, never 0.
All inputs are finite; a program needn't handle non-finite values.
Results may differ from the reference program's by a relative error of at most 0.0003.
Values may be sent and summed in bfloat16 or wider, within the bound.
No kernel may reach another device: no remote copies, remote signals or barrier semaphores. Data moves between devices by JAX's collectives and lax.ppermute only.
A program may use at most 64 MiB of HBM per device.

```python
import math
import jax
import jax.numpy as jnp
from jax import lax

NZ = 32
SWEEPS = 2
NX = 16
NY = 256
NT = 32
NS = 2


def draw_group_of(key, part):
    order = jax.random.permutation(jax.random.fold_in(key, 11), NT)
    return (order % NS).astype(jnp.int32)


def draw_sign_of(key, part):
    bits = jax.random.randint(jax.random.fold_in(key, 23), (NT,), 0, 2)
    return (bits * 2 - 1).astype(jnp.int32)


def level_of(own_key, extent, split, low, high):
    loudness = 1.0
    for position, parts in split:
        draws = jax.random.uniform(jax.random.fold_in(jax.random.fold_in(own_key, 6), position), (parts,), jnp.float32, low / len(split), high / len(split))
        loudness = loudness * jnp.repeat(jnp.exp(draws), extent[position] // parts).reshape((-1,) + (1,) * (len(extent) - 1 - position))
    return loudness


def bell_draw(key, extent, width, bound, shards=(), held_as=jnp.bfloat16):
    values = jax.random.normal(key, extent, jnp.float32) * width
    if len(shards) > 0:
        values = level_of(key, extent, shards, -0.22, 0.18) * values
    return jnp.clip(values, min=-bound, max=bound).astype(held_as)


def setup_inputs(seed: int = 0, part: int = 0) -> dict:
    key_list = jax.random.split(jax.random.key(seed), 5)
    part_splits = jax.random.split(jax.random.fold_in(key_list[4], part), 5)
    primaries = bell_draw(part_splits[0], (NT, 2, 3, NZ, NX, NY), 1.0, 6.0, ((0, 2), (4, 4), (5, 2)))
    conductivity = jnp.clip(jnp.exp(math.log(3.0) - 2.3025851 * jax.random.uniform(part_splits[1], (3, NZ, NX, NY), jnp.float32) ** level_of(part_splits[1], (3, NZ, NX, NY), ((1, 2), (2, 4), (3, 2)), -0.2, 0.2)), 0.3, 3.0)
    group_of = draw_group_of(jax.random.fold_in(jax.random.fold_in(key_list[4], part), 71), part)
    sign_of = draw_sign_of(jax.random.fold_in(jax.random.fold_in(key_list[4], part), 71), part)
    return dict(primaries=primaries, conductivity=conductivity, group_of=group_of, sign_of=sign_of)


K_FREQ = 2.0
RELAX = 0.6


def inner(f):
    return f[..., :-1, :-1, :-1]


def fwd_z(f):
    return f[..., 1:, :-1, :-1] - inner(f)


def fwd_x(f):
    return f[..., :-1, 1:, :-1] - inner(f)


def fwd_y(f):
    return f[..., :-1, :-1, 1:] - inner(f)


def back_z(g):
    return g[..., 1:, 1:, 1:] - g[..., :-1, 1:, 1:]


def back_x(g):
    return g[..., 1:, 1:, 1:] - g[..., 1:, :-1, 1:]


def back_y(g):
    return g[..., 1:, 1:, 1:] - g[..., 1:, 1:, :-1]


def curl_curl(padded):
    e_x = padded[..., 0, :, :, :]
    e_y = padded[..., 1, :, :, :]
    e_z = padded[..., 2, :, :, :]
    h_x = fwd_y(e_z) - fwd_z(e_y)
    h_y = fwd_z(e_x) - fwd_x(e_z)
    h_z = fwd_x(e_y) - fwd_y(e_x)
    c_x = back_y(h_z) - back_z(h_y)
    c_y = back_z(h_x) - back_x(h_z)
    c_z = back_x(h_y) - back_y(h_x)
    return jnp.stack([c_x, c_y, c_z], axis=-4)


def apply_operator(field, padded, kappa):
    curled = curl_curl(padded)
    real_part = curled[..., 0, :, :, :, :] - kappa * field[..., 1, :, :, :, :]
    imag_part = curled[..., 1, :, :, :, :] + kappa * field[..., 0, :, :, :, :]
    return jnp.stack([real_part, imag_part], axis=-5)


def jacobi(resid, kappa):
    denom = 16.0 + kappa * kappa
    real_part = (4.0 * resid[..., 0, :, :, :, :] + kappa * resid[..., 1, :, :, :, :]) / denom
    imag_part = (4.0 * resid[..., 1, :, :, :, :] - kappa * resid[..., 0, :, :, :, :]) / denom
    return jnp.stack([real_part, imag_part], axis=-5)


def source_term(shot, delta):
    return jnp.stack([delta * shot[..., 1, :, :, :, :], -delta * shot[..., 0, :, :, :, :]], axis=-5)


def reference(primaries, conductivity, group_of, sign_of):
    rows = jnp.arange(NS, dtype=jnp.int32)
    weights = jnp.where(group_of[None, :] == rows[:, None], sign_of[None, :], 0).astype(jnp.float32).astype(jnp.bfloat16)
    flat = primaries.reshape(NT, -1)
    shots = jnp.dot(weights, flat, preferred_element_type=jnp.float32).reshape(NS, 2, 3, NZ, NX, NY)
    kappa = K_FREQ * conductivity
    delta = K_FREQ * (conductivity - 1.0)

    def solve_one(shot):
        rhs = source_term(shot, delta)
        field = jacobi(rhs, kappa)
        for sweep in range(SWEEPS):
            padded = jnp.pad(field, [(0, 0), (0, 0), (1, 1), (1, 1), (1, 1)])
            resid = rhs - apply_operator(field, padded, kappa)
            field = field + RELAX * jacobi(resid, kappa)
        return field

    return lax.map(solve_one, shots)
```

```python
import jax
import jax.numpy as jnp
from jax import lax
from jax.sharding import PartitionSpec as P

NS_DEV = 1
SWEEPS = 2


K_FREQ = 2.0
RELAX = 0.6


def inner(f):
    return f[..., :-1, :-1, :-1]


def fwd_z(f):
    return f[..., 1:, :-1, :-1] - inner(f)


def fwd_x(f):
    return f[..., :-1, 1:, :-1] - inner(f)


def fwd_y(f):
    return f[..., :-1, :-1, 1:] - inner(f)


def back_z(g):
    return g[..., 1:, 1:, 1:] - g[..., :-1, 1:, 1:]


def back_x(g):
    return g[..., 1:, 1:, 1:] - g[..., 1:, :-1, 1:]


def back_y(g):
    return g[..., 1:, 1:, 1:] - g[..., 1:, 1:, :-1]


def curl_curl(padded):
    e_x = padded[..., 0, :, :, :]
    e_y = padded[..., 1, :, :, :]
    e_z = padded[..., 2, :, :, :]
    h_x = fwd_y(e_z) - fwd_z(e_y)
    h_y = fwd_z(e_x) - fwd_x(e_z)
    h_z = fwd_x(e_y) - fwd_y(e_x)
    c_x = back_y(h_z) - back_z(h_y)
    c_y = back_z(h_x) - back_x(h_z)
    c_z = back_x(h_y) - back_y(h_x)
    return jnp.stack([c_x, c_y, c_z], axis=-4)


def jacobi(resid, kappa):
    denom = 16.0 + kappa * kappa
    real_part = (4.0 * resid[..., 0, :, :, :, :] + kappa * resid[..., 1, :, :, :, :]) / denom
    imag_part = (4.0 * resid[..., 1, :, :, :, :] - kappa * resid[..., 0, :, :, :, :]) / denom
    return jnp.stack([real_part, imag_part], axis=-5)


def source_term(shot, delta):
    return jnp.stack([delta * shot[..., 1, :, :, :, :], -delta * shot[..., 0, :, :, :, :]], axis=-5)


def shrink(f, ring):
    return f[..., ring:f.shape[-2] - ring, ring:f.shape[-1] - ring]


def pad_z(f):
    return jnp.pad(f, [(0, 0)] * (f.ndim - 3) + [(1, 1), (0, 0), (0, 0)])


def halo(cells, axis, dim, width):
    count = lax.axis_size(axis)
    size = cells.shape[dim]
    head = lax.slice_in_dim(cells, 0, width, axis=dim)
    tail = lax.slice_in_dim(cells, size - width, size, axis=dim)
    from_low = lax.ppermute(tail, axis, [(i, i + 1) for i in range(count - 1)])
    from_high = lax.ppermute(head, axis, [(i + 1, i) for i in range(count - 1)])
    return jnp.concatenate([from_low, cells, from_high], axis=dim)


def encode_weights(group_part, sign_part, rows):
    picked = group_part[None, :] == rows[:, None]
    return jnp.where(picked, sign_part[None, :], 0).astype(jnp.float32).astype(jnp.bfloat16)


def body(primaries, conductivity, group_of, sign_of):
    nt_local = primaries.shape[0]
    depth = primaries.shape[3]
    width_x = primaries.shape[4]
    width_y = primaries.shape[5]
    n_tx = lax.axis_size("tx")
    tx_index = lax.axis_index("tx")
    other = (tx_index + 1) % n_tx
    own_groups = lax.dynamic_slice_in_dim(group_of, tx_index * nt_local, nt_local, 0)
    own_signs = lax.dynamic_slice_in_dim(sign_of, tx_index * nt_local, nt_local, 0)
    rows = jnp.stack([other, tx_index]).astype(jnp.int32)
    weights = encode_weights(own_groups, own_signs, rows)
    partial = lax.dot_general(
        weights, primaries, (((1,), (0,)), ((), ())), preferred_element_type=jnp.float32
    )
    send = jnp.concatenate([partial[0].reshape(-1), conductivity.reshape(-1)])
    got = lax.ppermute(send, "tx", [(i, (i + 1) % n_tx) for i in range(n_tx)])
    shot_cells = partial[1].size
    shot = partial[1] + got[:shot_cells].reshape(partial[1].shape)
    sigma_other = got[shot_cells:].reshape(conductivity.shape)
    low_first = tx_index == 0
    sigma_all = jnp.where(
        low_first,
        jnp.concatenate([conductivity, sigma_other], axis=1),
        jnp.concatenate([sigma_other, conductivity], axis=1),
    )

    planes = jnp.concatenate([shot.reshape(-1, depth, width_x, width_y), sigma_all], axis=0)
    planes = halo(planes, "yb", 3, SWEEPS)
    planes = halo(planes, "xb", 2, SWEEPS)
    ext_x = width_x + 2 * SWEEPS
    ext_y = width_y + 2 * SWEEPS
    n_shot = shot.shape[0] * shot.shape[1]
    shot_ext = planes[:n_shot].reshape(shot.shape[:2] + (depth, ext_x, ext_y))
    sigma_ext = planes[n_shot:]

    gx = lax.axis_index("xb") * width_x - SWEEPS + lax.broadcasted_iota(jnp.int32, (ext_x, ext_y), 0)
    gy = lax.axis_index("yb") * width_y - SWEEPS + lax.broadcasted_iota(jnp.int32, (ext_x, ext_y), 1)
    inside = (gx >= 0) & (gx < width_x * lax.axis_size("xb")) & (gy >= 0) & (gy < width_y * lax.axis_size("yb"))

    kappa = K_FREQ * sigma_ext
    delta = K_FREQ * (sigma_ext - 1.0)
    rhs = source_term(shot_ext, delta)
    field = jacobi(rhs, kappa)
    for sweep in range(SWEEPS):
        curled = curl_curl(pad_z(field))
        field = shrink(field, 1)
        kappa = shrink(kappa, 1)
        rhs = shrink(rhs, 1)
        inside = shrink(inside, 1)
        real_part = curled[..., 0, :, :, :, :] - kappa * field[..., 1, :, :, :, :]
        imag_part = curled[..., 1, :, :, :, :] + kappa * field[..., 0, :, :, :, :]
        applied = jnp.stack([real_part, imag_part], axis=-5)
        field = field + RELAX * jacobi(rhs - applied, kappa)
        if sweep < SWEEPS - 1:
            field = jnp.where(inside, field, 0.0)
    return field[None]


def solution(mesh):
    in_specs = (
        P(("survey", "tx"), None, None, None, "xb", "yb"),
        P("survey", "tx", "xb", "yb"),
        P("survey"),
        P("survey"),
    )
    out_specs = P(("survey", "tx"), None, None, None, "xb", "yb")
    return jax.shard_map(body, mesh=mesh, in_specs=in_specs, out_specs=out_specs, check_vma=False)
```

```python
import jax
import jax.numpy as jnp
from jax import lax
from jax.sharding import PartitionSpec as P

NS_DEV = 1
SWEEPS = 2


K_FREQ = 2.0
RELAX = 0.6


def inner(f):
    return f[..., :-1, :-1, :-1]


def fwd_z(f):
    return f[..., 1:, :-1, :-1] - inner(f)


def fwd_x(f):
    return f[..., :-1, 1:, :-1] - inner(f)


def fwd_y(f):
    return f[..., :-1, :-1, 1:] - inner(f)


def back_z(g):
    return g[..., 1:, 1:, 1:] - g[..., :-1, 1:, 1:]


def back_x(g):
    return g[..., 1:, 1:, 1:] - g[..., 1:, :-1, 1:]


def back_y(g):
    return g[..., 1:, 1:, 1:] - g[..., 1:, 1:, :-1]


def curl_curl(padded):
    e_x = padded[..., 0, :, :, :]
    e_y = padded[..., 1, :, :, :]
    e_z = padded[..., 2, :, :, :]
    h_x = fwd_y(e_z) - fwd_z(e_y)
    h_y = fwd_z(e_x) - fwd_x(e_z)
    h_z = fwd_x(e_y) - fwd_y(e_x)
    c_x = back_y(h_z) - back_z(h_y)
    c_y = back_z(h_x) - back_x(h_z)
    c_z = back_x(h_y) - back_y(h_x)
    return jnp.stack([c_x, c_y, c_z], axis=-4)


def jacobi(resid, kappa):
    denom = 16.0 + kappa * kappa
    real_part = (4.0 * resid[..., 0, :, :, :, :] + kappa * resid[..., 1, :, :, :, :]) / denom
    imag_part = (4.0 * resid[..., 1, :, :, :, :] - kappa * resid[..., 0, :, :, :, :]) / denom
    return jnp.stack([real_part, imag_part], axis=-5)


def source_term(shot, delta):
    return jnp.stack([delta * shot[..., 1, :, :, :, :], -delta * shot[..., 0, :, :, :, :]], axis=-5)


def shrink(f, ring):
    return f[..., ring:f.shape[-2] - ring, ring:f.shape[-1] - ring]


def pad_z(f):
    return jnp.pad(f, [(0, 0)] * (f.ndim - 3) + [(1, 1), (0, 0), (0, 0)])


def halo(cells, axis, dim, width):
    count = lax.axis_size(axis)
    size = cells.shape[dim]
    head = lax.slice_in_dim(cells, 0, width, axis=dim)
    tail = lax.slice_in_dim(cells, size - width, size, axis=dim)
    from_low = lax.ppermute(tail, axis, [(i, i + 1) for i in range(count - 1)])
    from_high = lax.ppermute(head, axis, [(i + 1, i) for i in range(count - 1)])
    return jnp.concatenate([from_low, cells, from_high], axis=dim)


def encode_weights(group_part, sign_part, rows):
    picked = group_part[None, :] == rows[:, None]
    return jnp.where(picked, sign_part[None, :], 0).astype(jnp.float32).astype(jnp.bfloat16)


def body(primaries, conductivity, group_of, sign_of):
    nt_local = primaries.shape[0]
    depth = primaries.shape[3]
    width_x = primaries.shape[4]
    width_y = primaries.shape[5]
    n_tx = lax.axis_size("tx")
    tx_index = lax.axis_index("tx")
    other = (tx_index + 1) % n_tx
    mine = lax.broadcasted_iota(jnp.int32, (n_tx, nt_local), 0) == tx_index
    own_groups = jnp.sum(jnp.where(mine, group_of.reshape(n_tx, nt_local), 0), axis=0)
    own_signs = jnp.sum(jnp.where(mine, sign_of.reshape(n_tx, nt_local), 0), axis=0)
    rows = jnp.stack([other, tx_index]).astype(jnp.int32)
    weights = encode_weights(own_groups, own_signs, rows)
    partial = lax.dot_general(
        weights, primaries, (((1,), (0,)), ((), ())), preferred_element_type=jnp.float32
    )
    n_shot = partial.shape[1] * partial.shape[2]
    shot_planes = n_shot * depth
    partial = partial.reshape(2, shot_planes, width_x, width_y)
    sigma_planes = conductivity.reshape(-1, width_x, width_y)
    send = jnp.concatenate([partial[0], sigma_planes], axis=0)
    got = lax.ppermute(send, "tx", [(i, (i + 1) % n_tx) for i in range(n_tx)])
    shot = partial[1] + got[:shot_planes]
    sigma_other = got[shot_planes:].reshape(conductivity.shape)
    low_first = tx_index == 0
    sigma_all = jnp.where(
        low_first,
        jnp.concatenate([conductivity, sigma_other], axis=1),
        jnp.concatenate([sigma_other, conductivity], axis=1),
    )

    planes = jnp.concatenate([shot, sigma_all.reshape(-1, width_x, width_y)], axis=0)
    planes = halo(planes, "xb", 1, SWEEPS)
    planes = halo(planes, "yb", 2, SWEEPS)
    shot_shape = primaries.shape[1:3]
    ext_x = width_x + 2 * SWEEPS
    ext_y = width_y + 2 * SWEEPS
    shot_ext = planes[:shot_planes].reshape(shot_shape + (depth, ext_x, ext_y))
    sigma_ext = planes[shot_planes:].reshape(-1, depth, ext_x, ext_y)

    gx = lax.axis_index("xb") * width_x - SWEEPS + lax.broadcasted_iota(jnp.int32, (ext_x, ext_y), 0)
    gy = lax.axis_index("yb") * width_y - SWEEPS + lax.broadcasted_iota(jnp.int32, (ext_x, ext_y), 1)
    inside = (gx >= 0) & (gx < width_x * lax.axis_size("xb")) & (gy >= 0) & (gy < width_y * lax.axis_size("yb"))

    kappa = K_FREQ * sigma_ext
    delta = K_FREQ * (sigma_ext - 1.0)
    rhs = source_term(shot_ext, delta)
    field = jacobi(rhs, kappa)
    for sweep in range(SWEEPS):
        curled = curl_curl(pad_z(field))
        field = shrink(field, 1)
        kappa = shrink(kappa, 1)
        rhs = shrink(rhs, 1)
        inside = shrink(inside, 1)
        real_part = curled[..., 0, :, :, :, :] - kappa * field[..., 1, :, :, :, :]
        imag_part = curled[..., 1, :, :, :, :] + kappa * field[..., 0, :, :, :, :]
        applied = jnp.stack([real_part, imag_part], axis=-5)
        field = field + RELAX * jacobi(rhs - applied, kappa)
        if sweep < SWEEPS - 1:
            field = jnp.where(inside, field, 0.0)
    return field[None]


def solution(mesh):
    in_specs = (
        P(("survey", "tx"), None, None, None, "xb", "yb"),
        P("survey", "tx", "xb", "yb"),
        P("survey"),
        P("survey"),
    )
    out_specs = P(("survey", "tx"), None, None, None, "xb", "yb")
    return jax.shard_map(body, mesh=mesh, in_specs=in_specs, out_specs=out_specs, check_vma=False)
```

```python
import jax
import jax.numpy as jnp
from jax import lax
from jax.sharding import PartitionSpec as P

NS_DEV = 1
SWEEPS = 2


K_FREQ = 2.0
RELAX = 0.6


def inner(f):
    return f[..., :-1, :-1, :-1]


def fwd_z(f):
    return f[..., 1:, :-1, :-1] - inner(f)


def fwd_x(f):
    return f[..., :-1, 1:, :-1] - inner(f)


def fwd_y(f):
    return f[..., :-1, :-1, 1:] - inner(f)


def back_z(g):
    return g[..., 1:, 1:, 1:] - g[..., :-1, 1:, 1:]


def back_x(g):
    return g[..., 1:, 1:, 1:] - g[..., 1:, :-1, 1:]


def back_y(g):
    return g[..., 1:, 1:, 1:] - g[..., 1:, 1:, :-1]


def curl_curl(padded):
    e_x = padded[..., 0, :, :, :]
    e_y = padded[..., 1, :, :, :]
    e_z = padded[..., 2, :, :, :]
    h_x = fwd_y(e_z) - fwd_z(e_y)
    h_y = fwd_z(e_x) - fwd_x(e_z)
    h_z = fwd_x(e_y) - fwd_y(e_x)
    c_x = back_y(h_z) - back_z(h_y)
    c_y = back_z(h_x) - back_x(h_z)
    c_z = back_x(h_y) - back_y(h_x)
    return jnp.stack([c_x, c_y, c_z], axis=-4)


def jacobi(resid, kappa):
    denom = 16.0 + kappa * kappa
    real_part = (4.0 * resid[..., 0, :, :, :, :] + kappa * resid[..., 1, :, :, :, :]) / denom
    imag_part = (4.0 * resid[..., 1, :, :, :, :] - kappa * resid[..., 0, :, :, :, :]) / denom
    return jnp.stack([real_part, imag_part], axis=-5)


def source_term(shot, delta):
    return jnp.stack([delta * shot[..., 1, :, :, :, :], -delta * shot[..., 0, :, :, :, :]], axis=-5)


def shrink(f, ring):
    return f[..., ring:f.shape[-2] - ring, ring:f.shape[-1] - ring]


def pad_z(f):
    return jnp.pad(f, [(0, 0)] * (f.ndim - 3) + [(1, 1), (0, 0), (0, 0)])


def halo(cells, axis, dim, width):
    count = lax.axis_size(axis)
    size = cells.shape[dim]
    head = lax.slice_in_dim(cells, 0, width, axis=dim)
    tail = lax.slice_in_dim(cells, size - width, size, axis=dim)
    from_low = lax.ppermute(tail, axis, [(i, i + 1) for i in range(count - 1)])
    from_high = lax.ppermute(head, axis, [(i + 1, i) for i in range(count - 1)])
    return jnp.concatenate([from_low, cells, from_high], axis=dim)


def encode_weights(group_part, sign_part, rows):
    picked = group_part[None, :] == rows[:, None]
    return jnp.where(picked, sign_part[None, :], 0).astype(jnp.float32).astype(jnp.bfloat16)


def body(primaries, conductivity, group_of, sign_of):
    nt_local = primaries.shape[0]
    depth = primaries.shape[3]
    width_x = primaries.shape[4]
    width_y = primaries.shape[5]
    n_tx = lax.axis_size("tx")
    tx_index = lax.axis_index("tx")
    other = (tx_index + 1) % n_tx
    mine = lax.broadcasted_iota(jnp.int32, (n_tx, nt_local), 0) == tx_index
    own_groups = jnp.sum(jnp.where(mine, group_of.reshape(n_tx, nt_local), 0), axis=0)
    own_signs = jnp.sum(jnp.where(mine, sign_of.reshape(n_tx, nt_local), 0), axis=0)
    rows = jnp.stack([other, tx_index]).astype(jnp.int32)
    weights = encode_weights(own_groups, own_signs, rows)
    partial = lax.dot_general(
        weights, primaries, (((1,), (0,)), ((), ())), preferred_element_type=jnp.float32
    )
    sigma_half = halo(conductivity, "xb", 2, SWEEPS)
    tx_ring = [(i, (i + 1) % n_tx) for i in range(n_tx)]
    got = lax.ppermute(partial[0], "tx", tx_ring)
    shot = partial[1] + got
    sigma_other = lax.ppermute(sigma_half, "tx", tx_ring)
    low_first = tx_index == 0
    sigma_all = jnp.where(
        low_first,
        jnp.concatenate([sigma_half, sigma_other], axis=1),
        jnp.concatenate([sigma_other, sigma_half], axis=1),
    )
    shot = halo(shot, "xb", 3, SWEEPS)
    ext_x = width_x + 2 * SWEEPS
    ext_y = width_y + 2 * SWEEPS
    shot_planes = shot.shape[0] * shot.shape[1] * depth
    planes = jnp.concatenate(
        [shot.reshape(-1, ext_x, width_y), sigma_all.reshape(-1, ext_x, width_y)], axis=0
    )
    planes = halo(planes, "yb", 2, SWEEPS)
    shot_ext = planes[:shot_planes].reshape(shot.shape[:2] + (depth, ext_x, ext_y))
    sigma_ext = planes[shot_planes:].reshape(-1, depth, ext_x, ext_y)

    gx = lax.axis_index("xb") * width_x - SWEEPS + lax.broadcasted_iota(jnp.int32, (ext_x, ext_y), 0)
    gy = lax.axis_index("yb") * width_y - SWEEPS + lax.broadcasted_iota(jnp.int32, (ext_x, ext_y), 1)
    inside = (gx >= 0) & (gx < width_x * lax.axis_size("xb")) & (gy >= 0) & (gy < width_y * lax.axis_size("yb"))

    kappa = K_FREQ * sigma_ext
    delta = K_FREQ * (sigma_ext - 1.0)
    rhs = source_term(shot_ext, delta)
    field = jacobi(rhs, kappa)
    for sweep in range(SWEEPS):
        curled = curl_curl(pad_z(field))
        field = shrink(field, 1)
        kappa = shrink(kappa, 1)
        rhs = shrink(rhs, 1)
        inside = shrink(inside, 1)
        real_part = curled[..., 0, :, :, :, :] - kappa * field[..., 1, :, :, :, :]
        imag_part = curled[..., 1, :, :, :, :] + kappa * field[..., 0, :, :, :, :]
        applied = jnp.stack([real_part, imag_part], axis=-5)
        field = field + RELAX * jacobi(rhs - applied, kappa)
        if sweep < SWEEPS - 1:
            field = jnp.where(inside, field, 0.0)
    return field[None]


def solution(mesh):
    in_specs = (
        P(("survey", "tx"), None, None, None, "xb", "yb"),
        P("survey", "tx", "xb", "yb"),
        P("survey"),
        P("survey"),
    )
    out_specs = P(("survey", "tx"), None, None, None, "xb", "yb")
    return jax.shard_map(body, mesh=mesh, in_specs=in_specs, out_specs=out_specs, check_vma=False)
```

```python
import jax
import jax.numpy as jnp
from jax import lax
from jax.sharding import PartitionSpec as P

NS_DEV = 1
SWEEPS = 2


K_FREQ = 2.0
RELAX = 0.6


def inner(f):
    return f[..., :-1, :-1, :-1]


def fwd_z(f):
    return f[..., 1:, :-1, :-1] - inner(f)


def fwd_x(f):
    return f[..., :-1, 1:, :-1] - inner(f)


def fwd_y(f):
    return f[..., :-1, :-1, 1:] - inner(f)


def back_z(g):
    return g[..., 1:, 1:, 1:] - g[..., :-1, 1:, 1:]


def back_x(g):
    return g[..., 1:, 1:, 1:] - g[..., 1:, :-1, 1:]


def back_y(g):
    return g[..., 1:, 1:, 1:] - g[..., 1:, 1:, :-1]


def curl_curl(padded):
    e_x = padded[..., 0, :, :, :]
    e_y = padded[..., 1, :, :, :]
    e_z = padded[..., 2, :, :, :]
    h_x = fwd_y(e_z) - fwd_z(e_y)
    h_y = fwd_z(e_x) - fwd_x(e_z)
    h_z = fwd_x(e_y) - fwd_y(e_x)
    c_x = back_y(h_z) - back_z(h_y)
    c_y = back_z(h_x) - back_x(h_z)
    c_z = back_x(h_y) - back_y(h_x)
    return jnp.stack([c_x, c_y, c_z], axis=-4)


def jacobi(resid, kappa):
    denom = 16.0 + kappa * kappa
    real_part = (4.0 * resid[..., 0, :, :, :, :] + kappa * resid[..., 1, :, :, :, :]) / denom
    imag_part = (4.0 * resid[..., 1, :, :, :, :] - kappa * resid[..., 0, :, :, :, :]) / denom
    return jnp.stack([real_part, imag_part], axis=-5)


def source_term(shot, delta):
    return jnp.stack([delta * shot[..., 1, :, :, :, :], -delta * shot[..., 0, :, :, :, :]], axis=-5)


def shrink(f, ring):
    return f[..., ring:f.shape[-2] - ring, ring:f.shape[-1] - ring]


def pad_z(f):
    return jnp.pad(f, [(0, 0)] * (f.ndim - 3) + [(1, 1), (0, 0), (0, 0)])


def halo(cells, axis, dim, width):
    count = lax.axis_size(axis)
    size = cells.shape[dim]
    head = lax.slice_in_dim(cells, 0, width, axis=dim)
    tail = lax.slice_in_dim(cells, size - width, size, axis=dim)
    even = lax.axis_index(axis) % 2 == 0
    from_low = jnp.zeros_like(tail)
    from_high = jnp.zeros_like(head)
    for first in (0, 1):
        pairs = []
        for i in range(first, count - 1, 2):
            pairs += [(i, i + 1), (i + 1, i)]
        if not pairs:
            continue
        lower_is_even = first == 0
        send = jnp.where(even == lower_is_even, tail, head)
        got = lax.ppermute(send, axis, pairs)
        from_high = jnp.where(even == lower_is_even, got, from_high)
        from_low = jnp.where(even == lower_is_even, from_low, got)
    return jnp.concatenate([from_low, cells, from_high], axis=dim)


def encode_weights(group_part, sign_part, rows):
    picked = group_part[None, :] == rows[:, None]
    return jnp.where(picked, sign_part[None, :], 0).astype(jnp.float32).astype(jnp.bfloat16)


def body(primaries, conductivity, group_of, sign_of):
    nt_local = primaries.shape[0]
    depth = primaries.shape[3]
    width_x = primaries.shape[4]
    width_y = primaries.shape[5]
    n_tx = lax.axis_size("tx")
    tx_index = lax.axis_index("tx")
    other = (tx_index + 1) % n_tx
    mine = lax.broadcasted_iota(jnp.int32, (n_tx, nt_local), 0) == tx_index
    own_groups = jnp.sum(jnp.where(mine, group_of.reshape(n_tx, nt_local), 0), axis=0)
    own_signs = jnp.sum(jnp.where(mine, sign_of.reshape(n_tx, nt_local), 0), axis=0)
    rows = jnp.stack([other, tx_index]).astype(jnp.int32)
    weights = encode_weights(own_groups, own_signs, rows)
    partial = lax.dot_general(
        weights, primaries, (((1,), (0,)), ((), ())), preferred_element_type=jnp.float32
    )
    tx_ring = [(i, (i + 1) % n_tx) for i in range(n_tx)]
    got = lax.ppermute(partial[0], "tx", tx_ring)
    sigma_other = lax.ppermute(conductivity, "tx", tx_ring)
    shot = partial[1] + got
    low_first = tx_index == 0
    sigma_all = jnp.where(
        low_first,
        jnp.concatenate([conductivity, sigma_other], axis=1),
        jnp.concatenate([sigma_other, conductivity], axis=1),
    )
    ext_x = width_x + 2 * SWEEPS
    ext_y = width_y + 2 * SWEEPS
    shot_planes = shot.shape[0] * shot.shape[1] * depth
    planes = jnp.concatenate(
        [shot.reshape(-1, width_x, width_y), sigma_all.reshape(-1, width_x, width_y)], axis=0
    )
    planes = halo(planes, "xb", 1, SWEEPS)
    planes = halo(planes, "yb", 2, SWEEPS)
    shot_ext = planes[:shot_planes].reshape(shot.shape[:2] + (depth, ext_x, ext_y))
    sigma_ext = planes[shot_planes:].reshape(-1, depth, ext_x, ext_y)

    gx = lax.axis_index("xb") * width_x - SWEEPS + lax.broadcasted_iota(jnp.int32, (ext_x, ext_y), 0)
    gy = lax.axis_index("yb") * width_y - SWEEPS + lax.broadcasted_iota(jnp.int32, (ext_x, ext_y), 1)
    inside = (gx >= 0) & (gx < width_x * lax.axis_size("xb")) & (gy >= 0) & (gy < width_y * lax.axis_size("yb"))

    kappa = K_FREQ * sigma_ext
    delta = K_FREQ * (sigma_ext - 1.0)
    rhs = source_term(shot_ext, delta)
    field = jacobi(rhs, kappa)
    for sweep in range(SWEEPS):
        curled = curl_curl(pad_z(field))
        field = shrink(field, 1)
        kappa = shrink(kappa, 1)
        rhs = shrink(rhs, 1)
        inside = shrink(inside, 1)
        real_part = curled[..., 0, :, :, :, :] - kappa * field[..., 1, :, :, :, :]
        imag_part = curled[..., 1, :, :, :, :] + kappa * field[..., 0, :, :, :, :]
        applied = jnp.stack([real_part, imag_part], axis=-5)
        field = field + RELAX * jacobi(rhs - applied, kappa)
        if sweep < SWEEPS - 1:
            field = jnp.where(inside, field, 0.0)
    return field[None]


def solution(mesh):
    in_specs = (
        P(("survey", "tx"), None, None, None, "xb", "yb"),
        P("survey", "tx", "xb", "yb"),
        P("survey"),
        P("survey"),
    )
    out_specs = P(("survey", "tx"), None, None, None, "xb", "yb")
    return jax.shard_map(body, mesh=mesh, in_specs=in_specs, out_specs=out_specs, check_vma=False)
```

```python
import jax
import jax.numpy as jnp
from jax import lax
from jax.experimental.layout import Layout, with_layout_constraint
from jax.sharding import PartitionSpec as P

NS_DEV = 1
SWEEPS = 2


K_FREQ = 2.0
RELAX = 0.6


def inner(f):
    return f[..., :-1, :-1, :-1]


def fwd_z(f):
    return f[..., 1:, :-1, :-1] - inner(f)


def fwd_x(f):
    return f[..., :-1, 1:, :-1] - inner(f)


def fwd_y(f):
    return f[..., :-1, :-1, 1:] - inner(f)


def back_z(g):
    return g[..., 1:, 1:, 1:] - g[..., :-1, 1:, 1:]


def back_x(g):
    return g[..., 1:, 1:, 1:] - g[..., 1:, :-1, 1:]


def back_y(g):
    return g[..., 1:, 1:, 1:] - g[..., 1:, 1:, :-1]


def curl_curl(padded):
    e_x = padded[..., 0, :, :, :]
    e_y = padded[..., 1, :, :, :]
    e_z = padded[..., 2, :, :, :]
    h_x = fwd_y(e_z) - fwd_z(e_y)
    h_y = fwd_z(e_x) - fwd_x(e_z)
    h_z = fwd_x(e_y) - fwd_y(e_x)
    c_x = back_y(h_z) - back_z(h_y)
    c_y = back_z(h_x) - back_x(h_z)
    c_z = back_x(h_y) - back_y(h_x)
    return jnp.stack([c_x, c_y, c_z], axis=-4)


def jacobi(resid, kappa):
    denom = 16.0 + kappa * kappa
    real_part = (4.0 * resid[..., 0, :, :, :, :] + kappa * resid[..., 1, :, :, :, :]) / denom
    imag_part = (4.0 * resid[..., 1, :, :, :, :] - kappa * resid[..., 0, :, :, :, :]) / denom
    return jnp.stack([real_part, imag_part], axis=-5)


def source_term(shot, delta):
    return jnp.stack([delta * shot[..., 1, :, :, :, :], -delta * shot[..., 0, :, :, :, :]], axis=-5)


def shrink(f, ring):
    return f[..., ring:f.shape[-2] - ring, ring:f.shape[-1] - ring]


def pad_z(f):
    return jnp.pad(f, [(0, 0)] * (f.ndim - 3) + [(1, 1), (0, 0), (0, 0)])


def halo(cells, axis, dim, width):
    count = lax.axis_size(axis)
    size = cells.shape[dim]
    head = lax.slice_in_dim(cells, 0, width, axis=dim)
    tail = lax.slice_in_dim(cells, size - width, size, axis=dim)
    even = lax.axis_index(axis) % 2 == 0
    from_low = jnp.zeros_like(tail)
    from_high = jnp.zeros_like(head)
    for first in (0, 1):
        pairs = []
        for i in range(first, count - 1, 2):
            pairs += [(i, i + 1), (i + 1, i)]
        if not pairs:
            continue
        lower_is_even = first == 0
        send = jnp.where(even == lower_is_even, tail, head)
        got = lax.ppermute(send, axis, pairs)
        from_high = jnp.where(even == lower_is_even, got, from_high)
        from_low = jnp.where(even == lower_is_even, from_low, got)
    return jnp.concatenate([from_low, cells, from_high], axis=dim)


def row_major(x):
    return with_layout_constraint(x, Layout(major_to_minor=tuple(range(x.ndim))))


def encode_weights(group_part, sign_part, rows):
    picked = group_part[None, :] == rows[:, None]
    return jnp.where(picked, sign_part[None, :], 0).astype(jnp.float32).astype(jnp.bfloat16)


def body(primaries, conductivity, group_of, sign_of):
    nt_local = primaries.shape[0]
    depth = primaries.shape[3]
    width_x = primaries.shape[4]
    width_y = primaries.shape[5]
    n_tx = lax.axis_size("tx")
    tx_index = lax.axis_index("tx")
    other = (tx_index + 1) % n_tx
    mine = lax.broadcasted_iota(jnp.int32, (n_tx, nt_local), 0) == tx_index
    own_groups = jnp.sum(jnp.where(mine, group_of.reshape(n_tx, nt_local), 0), axis=0)
    own_signs = jnp.sum(jnp.where(mine, sign_of.reshape(n_tx, nt_local), 0), axis=0)
    rows = jnp.stack([other, tx_index]).astype(jnp.int32)
    weights = encode_weights(own_groups, own_signs, rows)
    partial = lax.dot_general(
        weights, primaries, (((1,), (0,)), ((), ())), preferred_element_type=jnp.float32
    )
    tx_ring = [(i, (i + 1) % n_tx) for i in range(n_tx)]
    got = lax.ppermute(partial[0], "tx", tx_ring)
    sigma_other = lax.ppermute(conductivity, "tx", tx_ring)
    shot = partial[1] + got
    low_first = tx_index == 0
    sigma_all = jnp.where(
        low_first,
        jnp.concatenate([conductivity, sigma_other], axis=1),
        jnp.concatenate([sigma_other, conductivity], axis=1),
    )
    ext_x = width_x + 2 * SWEEPS
    ext_y = width_y + 2 * SWEEPS
    shot_planes = shot.shape[0] * shot.shape[1] * depth
    planes = jnp.concatenate(
        [shot.reshape(-1, width_x, width_y), sigma_all.reshape(-1, width_x, width_y)], axis=0
    )
    planes = row_major(halo(row_major(planes), "xb", 1, SWEEPS))
    planes = row_major(halo(planes, "yb", 2, SWEEPS))
    shot_ext = planes[:shot_planes].reshape(shot.shape[:2] + (depth, ext_x, ext_y))
    sigma_ext = planes[shot_planes:].reshape(-1, depth, ext_x, ext_y)

    gx = lax.axis_index("xb") * width_x - SWEEPS + lax.broadcasted_iota(jnp.int32, (ext_x, ext_y), 0)
    gy = lax.axis_index("yb") * width_y - SWEEPS + lax.broadcasted_iota(jnp.int32, (ext_x, ext_y), 1)
    inside = (gx >= 0) & (gx < width_x * lax.axis_size("xb")) & (gy >= 0) & (gy < width_y * lax.axis_size("yb"))

    kappa = K_FREQ * sigma_ext
    delta = K_FREQ * (sigma_ext - 1.0)
    rhs = source_term(shot_ext, delta)
    field = jacobi(rhs, kappa)
    for sweep in range(SWEEPS):
        curled = curl_curl(pad_z(field))
        field = shrink(field, 1)
        kappa = shrink(kappa, 1)
        rhs = shrink(rhs, 1)
        inside = shrink(inside, 1)
        real_part = curled[..., 0, :, :, :, :] - kappa * field[..., 1, :, :, :, :]
        imag_part = curled[..., 1, :, :, :, :] + kappa * field[..., 0, :, :, :, :]
        applied = jnp.stack([real_part, imag_part], axis=-5)
        field = field + RELAX * jacobi(rhs - applied, kappa)
        if sweep < SWEEPS - 1:
            field = jnp.where(inside, field, 0.0)
    return field[None]


def solution(mesh):
    in_specs = (
        P(("survey", "tx"), None, None, None, "xb", "yb"),
        P("survey", "tx", "xb", "yb"),
        P("survey"),
        P("survey"),
    )
    out_specs = P(("survey", "tx"), None, None, None, "xb", "yb")
    return jax.shard_map(body, mesh=mesh, in_specs=in_specs, out_specs=out_specs, check_vma=False)
```

```python
import jax
import jax.numpy as jnp
from jax import lax
from jax.experimental.layout import Layout, with_layout_constraint
from jax.sharding import PartitionSpec as P

NS_DEV = 1
SWEEPS = 2


K_FREQ = 2.0
RELAX = 0.6


def inner(f):
    return f[..., :-1, :-1, :-1]


def fwd_z(f):
    return f[..., 1:, :-1, :-1] - inner(f)


def fwd_x(f):
    return f[..., :-1, 1:, :-1] - inner(f)


def fwd_y(f):
    return f[..., :-1, :-1, 1:] - inner(f)


def back_z(g):
    return g[..., 1:, 1:, 1:] - g[..., :-1, 1:, 1:]


def back_x(g):
    return g[..., 1:, 1:, 1:] - g[..., 1:, :-1, 1:]


def back_y(g):
    return g[..., 1:, 1:, 1:] - g[..., 1:, 1:, :-1]


def curl_curl(padded):
    e_x = padded[..., 0, :, :, :]
    e_y = padded[..., 1, :, :, :]
    e_z = padded[..., 2, :, :, :]
    h_x = fwd_y(e_z) - fwd_z(e_y)
    h_y = fwd_z(e_x) - fwd_x(e_z)
    h_z = fwd_x(e_y) - fwd_y(e_x)
    c_x = back_y(h_z) - back_z(h_y)
    c_y = back_z(h_x) - back_x(h_z)
    c_z = back_x(h_y) - back_y(h_x)
    return jnp.stack([c_x, c_y, c_z], axis=-4)


def jacobi(resid, kappa):
    denom = 16.0 + kappa * kappa
    real_part = (4.0 * resid[..., 0, :, :, :, :] + kappa * resid[..., 1, :, :, :, :]) / denom
    imag_part = (4.0 * resid[..., 1, :, :, :, :] - kappa * resid[..., 0, :, :, :, :]) / denom
    return jnp.stack([real_part, imag_part], axis=-5)


def source_term(shot, delta):
    return jnp.stack([delta * shot[..., 1, :, :, :, :], -delta * shot[..., 0, :, :, :, :]], axis=-5)


def shrink(f, ring):
    return f[..., ring:f.shape[-2] - ring, ring:f.shape[-1] - ring]


def pad_z(f):
    return jnp.pad(f, [(0, 0)] * (f.ndim - 3) + [(1, 1), (0, 0), (0, 0)])


def swap_rounds(axis):
    count = lax.axis_size(axis)
    even = lax.axis_index(axis) % 2 == 0
    for first in (0, 1):
        pairs = []
        for i in range(first, count - 1, 2):
            pairs += [(i, i + 1), (i + 1, i)]
        if pairs:
            yield pairs, even == (first == 0)


def halo_into(ext, head, tail, axis, corner, dim, low_at, high_at):
    for pairs, lower in swap_rounds(axis):
        got = lax.ppermute(row_major(jnp.where(lower, tail, head)), axis, pairs)
        start = list(corner)
        start[dim] = jnp.where(lower, high_at, low_at)
        ext = lax.dynamic_update_slice(ext, got, start)
    return ext


def row_major(x):
    return with_layout_constraint(x, Layout(major_to_minor=tuple(range(x.ndim))))


def encode_weights(group_part, sign_part, rows):
    picked = group_part[None, :] == rows[:, None]
    return jnp.where(picked, sign_part[None, :], 0).astype(jnp.float32).astype(jnp.bfloat16)


def body(primaries, conductivity, group_of, sign_of):
    nt_local = primaries.shape[0]
    depth = primaries.shape[3]
    width_x = primaries.shape[4]
    width_y = primaries.shape[5]
    n_tx = lax.axis_size("tx")
    tx_index = lax.axis_index("tx")
    other = (tx_index + 1) % n_tx
    own_groups = jnp.zeros((nt_local,), jnp.int32)
    own_signs = jnp.zeros((nt_local,), jnp.int32)
    for k in range(n_tx):
        own_groups = jnp.where(tx_index == k, group_of[k * nt_local:(k + 1) * nt_local], own_groups)
        own_signs = jnp.where(tx_index == k, sign_of[k * nt_local:(k + 1) * nt_local], own_signs)
    rows = jnp.stack([other, tx_index]).astype(jnp.int32)
    weights = encode_weights(own_groups, own_signs, rows)
    partial = lax.dot_general(
        weights, primaries, (((1,), (0,)), ((), ())), preferred_element_type=jnp.float32
    )
    tx_ring = [(i, (i + 1) % n_tx) for i in range(n_tx)]
    got = lax.ppermute(partial[0], "tx", tx_ring)
    sigma_other = lax.ppermute(conductivity, "tx", tx_ring)
    shot = partial[1] + got
    low_first = tx_index == 0
    sigma_all = jnp.where(
        low_first,
        jnp.concatenate([conductivity, sigma_other], axis=1),
        jnp.concatenate([sigma_other, conductivity], axis=1),
    )
    ext_x = width_x + 2 * SWEEPS
    ext_y = width_y + 2 * SWEEPS
    shot_planes = shot.shape[0] * shot.shape[1] * depth
    planes = jnp.concatenate(
        [shot.reshape(-1, width_x, width_y), sigma_all.reshape(-1, width_x, width_y)], axis=0
    )
    w = SWEEPS
    ext = row_major(jnp.pad(planes, [(0, 0), (w, w), (w, w)]))
    ext = halo_into(
        ext, planes[:, :w], planes[:, width_x - w:], "xb", (0, 0, w), 1, 0, w + width_x
    )
    ext = halo_into(
        ext, ext[:, :, w:2 * w], ext[:, :, width_y:width_y + w], "yb", (0, 0, 0), 2, 0, w + width_y
    )
    planes = row_major(ext)
    shot_ext = planes[:shot_planes].reshape(shot.shape[:2] + (depth, ext_x, ext_y))
    sigma_ext = planes[shot_planes:].reshape(-1, depth, ext_x, ext_y)

    gx = lax.axis_index("xb") * width_x - SWEEPS + lax.broadcasted_iota(jnp.int32, (ext_x, ext_y), 0)
    gy = lax.axis_index("yb") * width_y - SWEEPS + lax.broadcasted_iota(jnp.int32, (ext_x, ext_y), 1)
    inside = (gx >= 0) & (gx < width_x * lax.axis_size("xb")) & (gy >= 0) & (gy < width_y * lax.axis_size("yb"))

    kappa = K_FREQ * sigma_ext
    delta = K_FREQ * (sigma_ext - 1.0)
    rhs = source_term(shot_ext, delta)
    field = jacobi(rhs, kappa)
    for sweep in range(SWEEPS):
        curled = curl_curl(pad_z(field))
        field = shrink(field, 1)
        kappa = shrink(kappa, 1)
        rhs = shrink(rhs, 1)
        inside = shrink(inside, 1)
        real_part = curled[..., 0, :, :, :, :] - kappa * field[..., 1, :, :, :, :]
        imag_part = curled[..., 1, :, :, :, :] + kappa * field[..., 0, :, :, :, :]
        applied = jnp.stack([real_part, imag_part], axis=-5)
        field = field + RELAX * jacobi(rhs - applied, kappa)
        if sweep < SWEEPS - 1:
            field = jnp.where(inside, field, 0.0)
    return field[None]


def solution(mesh):
    in_specs = (
        P(("survey", "tx"), None, None, None, "xb", "yb"),
        P("survey", "tx", "xb", "yb"),
        P("survey"),
        P("survey"),
    )
    out_specs = P(("survey", "tx"), None, None, None, "xb", "yb")
    return jax.shard_map(body, mesh=mesh, in_specs=in_specs, out_specs=out_specs, check_vma=False)
```

```python
import jax
import jax.numpy as jnp
from jax import lax
from jax.experimental.layout import Layout, with_layout_constraint
from jax.sharding import PartitionSpec as P

NS_DEV = 1
SWEEPS = 2


K_FREQ = 2.0
RELAX = 0.6


def inner(f):
    return f[..., :-1, :-1, :-1]


def fwd_z(f):
    return f[..., 1:, :-1, :-1] - inner(f)


def fwd_x(f):
    return f[..., :-1, 1:, :-1] - inner(f)


def fwd_y(f):
    return f[..., :-1, :-1, 1:] - inner(f)


def back_z(g):
    return g[..., 1:, 1:, 1:] - g[..., :-1, 1:, 1:]


def back_x(g):
    return g[..., 1:, 1:, 1:] - g[..., 1:, :-1, 1:]


def back_y(g):
    return g[..., 1:, 1:, 1:] - g[..., 1:, 1:, :-1]


def curl_curl(padded):
    e_x = padded[..., 0, :, :, :]
    e_y = padded[..., 1, :, :, :]
    e_z = padded[..., 2, :, :, :]
    h_x = fwd_y(e_z) - fwd_z(e_y)
    h_y = fwd_z(e_x) - fwd_x(e_z)
    h_z = fwd_x(e_y) - fwd_y(e_x)
    c_x = back_y(h_z) - back_z(h_y)
    c_y = back_z(h_x) - back_x(h_z)
    c_z = back_x(h_y) - back_y(h_x)
    return jnp.stack([c_x, c_y, c_z], axis=-4)


def jacobi(resid, kappa):
    denom = 16.0 + kappa * kappa
    real_part = (4.0 * resid[..., 0, :, :, :, :] + kappa * resid[..., 1, :, :, :, :]) / denom
    imag_part = (4.0 * resid[..., 1, :, :, :, :] - kappa * resid[..., 0, :, :, :, :]) / denom
    return jnp.stack([real_part, imag_part], axis=-5)


def source_term(shot, delta):
    return jnp.stack([delta * shot[..., 1, :, :, :, :], -delta * shot[..., 0, :, :, :, :]], axis=-5)


def shrink(f, ring):
    return f[..., ring:f.shape[-2] - ring, ring:f.shape[-1] - ring]


def pad_z(f):
    return jnp.pad(f, [(0, 0)] * (f.ndim - 3) + [(1, 1), (0, 0), (0, 0)])


def halo(cells, axis, dim, width):
    count = lax.axis_size(axis)
    size = cells.shape[dim]
    head = lax.slice_in_dim(cells, 0, width, axis=dim)
    tail = lax.slice_in_dim(cells, size - width, size, axis=dim)
    even = lax.axis_index(axis) % 2 == 0
    from_low = jnp.zeros_like(tail)
    from_high = jnp.zeros_like(head)
    for first in (0, 1):
        pairs = []
        for i in range(first, count - 1, 2):
            pairs += [(i, i + 1), (i + 1, i)]
        if not pairs:
            continue
        lower_is_even = first == 0
        send = row_major(jnp.where(even == lower_is_even, tail, head))
        got = row_major(lax.ppermute(send, axis, pairs))
        from_high = jnp.where(even == lower_is_even, got, from_high)
        from_low = jnp.where(even == lower_is_even, from_low, got)
    return jnp.concatenate([from_low, cells, from_high], axis=dim)


def row_major(x):
    return with_layout_constraint(x, Layout(major_to_minor=tuple(range(x.ndim))))


def encode_weights(group_part, sign_part, rows):
    picked = group_part[None, :] == rows[:, None]
    return jnp.where(picked, sign_part[None, :], 0).astype(jnp.float32).astype(jnp.bfloat16)


def body(primaries, conductivity, group_of, sign_of):
    nt_local = primaries.shape[0]
    depth = primaries.shape[3]
    width_x = primaries.shape[4]
    width_y = primaries.shape[5]
    n_tx = lax.axis_size("tx")
    tx_index = lax.axis_index("tx")
    other = (tx_index + 1) % n_tx
    mine = lax.broadcasted_iota(jnp.int32, (n_tx, nt_local), 0) == tx_index
    own_groups = jnp.sum(jnp.where(mine, group_of.reshape(n_tx, nt_local), 0), axis=0)
    own_signs = jnp.sum(jnp.where(mine, sign_of.reshape(n_tx, nt_local), 0), axis=0)
    rows = jnp.stack([other, tx_index]).astype(jnp.int32)
    weights = encode_weights(own_groups, own_signs, rows)
    partial = lax.dot_general(
        weights, primaries, (((1,), (0,)), ((), ())), preferred_element_type=jnp.float32
    )
    tx_ring = [(i, (i + 1) % n_tx) for i in range(n_tx)]
    got = lax.ppermute(partial[0], "tx", tx_ring)
    sigma_other = lax.ppermute(conductivity, "tx", tx_ring)
    shot = partial[1] + got
    low_first = tx_index == 0
    sigma_all = jnp.where(
        low_first,
        jnp.concatenate([conductivity, sigma_other], axis=1),
        jnp.concatenate([sigma_other, conductivity], axis=1),
    )
    ext_x = width_x + 2 * SWEEPS
    ext_y = width_y + 2 * SWEEPS
    shot_planes = shot.shape[0] * shot.shape[1] * depth
    planes = jnp.concatenate(
        [shot.reshape(-1, width_x, width_y), sigma_all.reshape(-1, width_x, width_y)], axis=0
    )
    planes = row_major(halo(row_major(planes), "xb", 1, SWEEPS))
    planes = row_major(halo(planes, "yb", 2, SWEEPS))
    shot_ext = planes[:shot_planes].reshape(shot.shape[:2] + (depth, ext_x, ext_y))
    sigma_ext = planes[shot_planes:].reshape(-1, depth, ext_x, ext_y)

    gx = lax.axis_index("xb") * width_x - SWEEPS + lax.broadcasted_iota(jnp.int32, (ext_x, ext_y), 0)
    gy = lax.axis_index("yb") * width_y - SWEEPS + lax.broadcasted_iota(jnp.int32, (ext_x, ext_y), 1)
    inside = (gx >= 0) & (gx < width_x * lax.axis_size("xb")) & (gy >= 0) & (gy < width_y * lax.axis_size("yb"))

    kappa = K_FREQ * sigma_ext
    delta = K_FREQ * (sigma_ext - 1.0)
    rhs = source_term(shot_ext, delta)
    field = jacobi(rhs, kappa)
    for sweep in range(SWEEPS):
        curled = curl_curl(pad_z(field))
        field = shrink(field, 1)
        kappa = shrink(kappa, 1)
        rhs = shrink(rhs, 1)
        inside = shrink(inside, 1)
        real_part = curled[..., 0, :, :, :, :] - kappa * field[..., 1, :, :, :, :]
        imag_part = curled[..., 1, :, :, :, :] + kappa * field[..., 0, :, :, :, :]
        applied = jnp.stack([real_part, imag_part], axis=-5)
        field = field + RELAX * jacobi(rhs - applied, kappa)
        if sweep < SWEEPS - 1:
            field = jnp.where(inside, field, 0.0)
    return field[None]


def solution(mesh):
    in_specs = (
        P(("survey", "tx"), None, None, None, "xb", "yb"),
        P("survey", "tx", "xb", "yb"),
        P("survey"),
        P("survey"),
    )
    out_specs = P(("survey", "tx"), None, None, None, "xb", "yb")
    return jax.shard_map(body, mesh=mesh, in_specs=in_specs, out_specs=out_specs, check_vma=False)
```

```python
import jax
import jax.numpy as jnp
from jax import lax
from jax.experimental.layout import Layout, with_layout_constraint
from jax.sharding import PartitionSpec as P

NS_DEV = 1
SWEEPS = 2


K_FREQ = 2.0
RELAX = 0.6


def inner(f):
    return f[..., :-1, :-1, :-1]


def fwd_z(f):
    return f[..., 1:, :-1, :-1] - inner(f)


def fwd_x(f):
    return f[..., :-1, 1:, :-1] - inner(f)


def fwd_y(f):
    return f[..., :-1, :-1, 1:] - inner(f)


def back_z(g):
    return g[..., 1:, 1:, 1:] - g[..., :-1, 1:, 1:]


def back_x(g):
    return g[..., 1:, 1:, 1:] - g[..., 1:, :-1, 1:]


def back_y(g):
    return g[..., 1:, 1:, 1:] - g[..., 1:, 1:, :-1]


def curl_curl(padded):
    e_x = padded[..., 0, :, :, :]
    e_y = padded[..., 1, :, :, :]
    e_z = padded[..., 2, :, :, :]
    h_x = fwd_y(e_z) - fwd_z(e_y)
    h_y = fwd_z(e_x) - fwd_x(e_z)
    h_z = fwd_x(e_y) - fwd_y(e_x)
    c_x = back_y(h_z) - back_z(h_y)
    c_y = back_z(h_x) - back_x(h_z)
    c_z = back_x(h_y) - back_y(h_x)
    return jnp.stack([c_x, c_y, c_z], axis=-4)


def jacobi(resid, kappa):
    denom = 16.0 + kappa * kappa
    real_part = (4.0 * resid[..., 0, :, :, :, :] + kappa * resid[..., 1, :, :, :, :]) / denom
    imag_part = (4.0 * resid[..., 1, :, :, :, :] - kappa * resid[..., 0, :, :, :, :]) / denom
    return jnp.stack([real_part, imag_part], axis=-5)


def source_term(shot, delta):
    return jnp.stack([delta * shot[..., 1, :, :, :, :], -delta * shot[..., 0, :, :, :, :]], axis=-5)


def shrink(f, ring):
    return f[..., ring:f.shape[-2] - ring, ring:f.shape[-1] - ring]


def pad_z(f):
    return jnp.pad(f, [(0, 0)] * (f.ndim - 3) + [(1, 1), (0, 0), (0, 0)])


def halo(cells, axis, dim, width):
    count = lax.axis_size(axis)
    size = cells.shape[dim]
    head = lax.slice_in_dim(cells, 0, width, axis=dim)
    tail = lax.slice_in_dim(cells, size - width, size, axis=dim)
    if count == 2:
        send = row_major(jnp.concatenate([tail, head], axis=dim))
        got = row_major(lax.ppermute(send, axis, [(0, 1), (1, 0)]))
        return jnp.concatenate(
            [lax.slice_in_dim(got, 0, width, axis=dim), cells,
             lax.slice_in_dim(got, width, 2 * width, axis=dim)], axis=dim)
    even = lax.axis_index(axis) % 2 == 0
    from_low = tail
    from_high = head
    for first in (0, 1):
        pairs = []
        for i in range(first, count - 1, 2):
            pairs += [(i, i + 1), (i + 1, i)]
        lower_is_even = first == 0
        send = row_major(jnp.where(even == lower_is_even, tail, head))
        got = row_major(lax.ppermute(send, axis, pairs))
        from_high = jnp.where(even == lower_is_even, got, from_high)
        from_low = jnp.where(even == lower_is_even, from_low, got)
    return jnp.concatenate([from_low, cells, from_high], axis=dim)


def row_major(x):
    return with_layout_constraint(x, Layout(major_to_minor=tuple(range(x.ndim))))


def encode_weights(group_part, sign_part, rows):
    picked = group_part[None, :] == rows[:, None]
    return jnp.where(picked, sign_part[None, :], 0).astype(jnp.float32).astype(jnp.bfloat16)


def body(primaries, conductivity, group_of, sign_of):
    nt_local = primaries.shape[0]
    depth = primaries.shape[3]
    width_x = primaries.shape[4]
    width_y = primaries.shape[5]
    n_tx = lax.axis_size("tx")
    tx_index = lax.axis_index("tx")
    other = (tx_index + 1) % n_tx
    mine = lax.broadcasted_iota(jnp.int32, (n_tx, nt_local), 0) == tx_index
    own_groups = jnp.sum(jnp.where(mine, group_of.reshape(n_tx, nt_local), 0), axis=0)
    own_signs = jnp.sum(jnp.where(mine, sign_of.reshape(n_tx, nt_local), 0), axis=0)
    rows = jnp.stack([other, tx_index]).astype(jnp.int32)
    weights = encode_weights(own_groups, own_signs, rows)
    partial = lax.dot_general(
        weights, primaries, (((1,), (0,)), ((), ())), preferred_element_type=jnp.float32
    )
    tx_ring = [(i, (i + 1) % n_tx) for i in range(n_tx)]
    got = lax.ppermute(partial[0], "tx", tx_ring)
    sigma_other = lax.ppermute(conductivity, "tx", tx_ring)
    shot = partial[1] + got
    low_first = tx_index == 0
    sigma_all = jnp.where(
        low_first,
        jnp.concatenate([conductivity, sigma_other], axis=1),
        jnp.concatenate([sigma_other, conductivity], axis=1),
    )
    ext_x = width_x + 2 * SWEEPS
    ext_y = width_y + 2 * SWEEPS
    shot_planes = shot.shape[0] * shot.shape[1] * depth
    planes = jnp.concatenate(
        [shot.reshape(-1, width_x, width_y), sigma_all.reshape(-1, width_x, width_y)], axis=0
    )
    planes = row_major(halo(row_major(planes), "xb", 1, SWEEPS))
    planes = row_major(halo(planes, "yb", 2, SWEEPS))
    shot_ext = planes[:shot_planes].reshape(shot.shape[:2] + (depth, ext_x, ext_y))
    sigma_ext = planes[shot_planes:].reshape(-1, depth, ext_x, ext_y)

    gx = lax.axis_index("xb") * width_x - SWEEPS + lax.broadcasted_iota(jnp.int32, (ext_x, ext_y), 0)
    gy = lax.axis_index("yb") * width_y - SWEEPS + lax.broadcasted_iota(jnp.int32, (ext_x, ext_y), 1)
    inside = (gx >= 0) & (gx < width_x * lax.axis_size("xb")) & (gy >= 0) & (gy < width_y * lax.axis_size("yb"))

    kappa = K_FREQ * sigma_ext
    delta = K_FREQ * (sigma_ext - 1.0)
    rhs = source_term(shot_ext, delta)
    field = jnp.where(inside, jacobi(rhs, kappa), 0.0)
    for sweep in range(SWEEPS):
        curled = curl_curl(pad_z(field))
        field = shrink(field, 1)
        kappa = shrink(kappa, 1)
        rhs = shrink(rhs, 1)
        inside = shrink(inside, 1)
        real_part = curled[..., 0, :, :, :, :] - kappa * field[..., 1, :, :, :, :]
        imag_part = curled[..., 1, :, :, :, :] + kappa * field[..., 0, :, :, :, :]
        applied = jnp.stack([real_part, imag_part], axis=-5)
        field = field + RELAX * jacobi(rhs - applied, kappa)
        if sweep < SWEEPS - 1:
            field = jnp.where(inside, field, 0.0)
    return field[None]


def solution(mesh):
    in_specs = (
        P(("survey", "tx"), None, None, None, "xb", "yb"),
        P("survey", "tx", "xb", "yb"),
        P("survey"),
        P("survey"),
    )
    out_specs = P(("survey", "tx"), None, None, None, "xb", "yb")
    return jax.shard_map(body, mesh=mesh, in_specs=in_specs, out_specs=out_specs, check_vma=False)
```

```python
import jax
import jax.numpy as jnp
from jax import lax
from jax.experimental import pallas as pl
from jax.experimental.pallas import tpu as pltpu
from jax.experimental.layout import Layout, with_layout_constraint
from jax.sharding import PartitionSpec as P

NS_DEV = 1
SWEEPS = 2


K_FREQ = 2.0
RELAX = 0.6


def inner(f):
    return f[..., :-1, :-1, :-1]


def fwd_z(f):
    return f[..., 1:, :-1, :-1] - inner(f)


def fwd_x(f):
    return f[..., :-1, 1:, :-1] - inner(f)


def fwd_y(f):
    return f[..., :-1, :-1, 1:] - inner(f)


def back_z(g):
    return g[..., 1:, 1:, 1:] - g[..., :-1, 1:, 1:]


def back_x(g):
    return g[..., 1:, 1:, 1:] - g[..., 1:, :-1, 1:]


def back_y(g):
    return g[..., 1:, 1:, 1:] - g[..., 1:, 1:, :-1]


def curl_curl(padded):
    e_x = padded[..., 0, :, :, :]
    e_y = padded[..., 1, :, :, :]
    e_z = padded[..., 2, :, :, :]
    h_x = fwd_y(e_z) - fwd_z(e_y)
    h_y = fwd_z(e_x) - fwd_x(e_z)
    h_z = fwd_x(e_y) - fwd_y(e_x)
    c_x = back_y(h_z) - back_z(h_y)
    c_y = back_z(h_x) - back_x(h_z)
    c_z = back_x(h_y) - back_y(h_x)
    return jnp.stack([c_x, c_y, c_z], axis=-4)


def jacobi(resid, kappa):
    denom = 16.0 + kappa * kappa
    real_part = (4.0 * resid[..., 0, :, :, :, :] + kappa * resid[..., 1, :, :, :, :]) / denom
    imag_part = (4.0 * resid[..., 1, :, :, :, :] - kappa * resid[..., 0, :, :, :, :]) / denom
    return jnp.stack([real_part, imag_part], axis=-5)


def source_term(shot, delta):
    return jnp.stack([delta * shot[..., 1, :, :, :, :], -delta * shot[..., 0, :, :, :, :]], axis=-5)


def shrink(f, ring):
    return f[..., ring:f.shape[-2] - ring, ring:f.shape[-1] - ring]


def pad_z(f):
    return jnp.pad(f, [(0, 0)] * (f.ndim - 3) + [(1, 1), (0, 0), (0, 0)])


def halo(cells, axis, dim, width):
    count = lax.axis_size(axis)
    size = cells.shape[dim]
    head = lax.slice_in_dim(cells, 0, width, axis=dim)
    tail = lax.slice_in_dim(cells, size - width, size, axis=dim)
    even = lax.axis_index(axis) % 2 == 0
    from_low = jnp.zeros_like(tail)
    from_high = jnp.zeros_like(head)
    for first in (0, 1):
        pairs = []
        for i in range(first, count - 1, 2):
            pairs += [(i, i + 1), (i + 1, i)]
        if not pairs:
            continue
        lower_is_even = first == 0
        send = row_major(jnp.where(even == lower_is_even, tail, head))
        got = row_major(lax.ppermute(send, axis, pairs))
        from_high = jnp.where(even == lower_is_even, got, from_high)
        from_low = jnp.where(even == lower_is_even, from_low, got)
    return jnp.concatenate([from_low, cells, from_high], axis=dim)


def row_major(x):
    return with_layout_constraint(x, Layout(major_to_minor=tuple(range(x.ndim))))


def sweep_all(shot_ext, sigma_ext, inside):
    kappa = K_FREQ * sigma_ext
    delta = K_FREQ * (sigma_ext - 1.0)
    rhs = source_term(shot_ext, delta)
    field = jacobi(rhs, kappa)
    for sweep in range(SWEEPS):
        curled = curl_curl(pad_z(field))
        field = shrink(field, 1)
        kappa = shrink(kappa, 1)
        rhs = shrink(rhs, 1)
        inside = shrink(inside, 1)
        real_part = curled[..., 0, :, :, :, :] - kappa * field[..., 1, :, :, :, :]
        imag_part = curled[..., 1, :, :, :, :] + kappa * field[..., 0, :, :, :, :]
        applied = jnp.stack([real_part, imag_part], axis=-5)
        field = field + RELAX * jacobi(rhs - applied, kappa)
        if sweep < SWEEPS - 1:
            field = jnp.where(inside, field, 0.0)
    return field


def encode_weights(group_part, sign_part, rows):
    picked = group_part[None, :] == rows[:, None]
    return jnp.where(picked, sign_part[None, :], 0).astype(jnp.float32).astype(jnp.bfloat16)


def body(primaries, conductivity, group_of, sign_of):
    nt_local = primaries.shape[0]
    depth = primaries.shape[3]
    width_x = primaries.shape[4]
    width_y = primaries.shape[5]
    n_tx = lax.axis_size("tx")
    tx_index = lax.axis_index("tx")
    other = (tx_index + 1) % n_tx
    mine = lax.broadcasted_iota(jnp.int32, (n_tx, nt_local), 0) == tx_index
    own_groups = jnp.sum(jnp.where(mine, group_of.reshape(n_tx, nt_local), 0), axis=0)
    own_signs = jnp.sum(jnp.where(mine, sign_of.reshape(n_tx, nt_local), 0), axis=0)
    rows = jnp.stack([other, tx_index]).astype(jnp.int32)
    weights = encode_weights(own_groups, own_signs, rows)
    partial = lax.dot_general(
        weights, primaries, (((1,), (0,)), ((), ())), preferred_element_type=jnp.float32
    )
    tx_ring = [(i, (i + 1) % n_tx) for i in range(n_tx)]
    got = lax.ppermute(partial[0], "tx", tx_ring)
    sigma_other = lax.ppermute(conductivity, "tx", tx_ring)
    shot = partial[1] + got
    low_first = tx_index == 0
    sigma_all = jnp.where(
        low_first,
        jnp.concatenate([conductivity, sigma_other], axis=1),
        jnp.concatenate([sigma_other, conductivity], axis=1),
    )
    ext_x = width_x + 2 * SWEEPS
    ext_y = width_y + 2 * SWEEPS
    shot_planes = shot.shape[0] * shot.shape[1] * depth
    planes = jnp.concatenate(
        [shot.reshape(-1, width_x, width_y), sigma_all.reshape(-1, width_x, width_y)], axis=0
    )
    planes = row_major(halo(row_major(planes), "xb", 1, SWEEPS))
    planes = row_major(halo(planes, "yb", 2, SWEEPS))
    gx = lax.axis_index("xb") * width_x - SWEEPS + lax.broadcasted_iota(jnp.int32, (ext_x, ext_y), 0)
    gy = lax.axis_index("yb") * width_y - SWEEPS + lax.broadcasted_iota(jnp.int32, (ext_x, ext_y), 1)
    inside = (gx >= 0) & (gx < width_x * lax.axis_size("xb")) & (gy >= 0) & (gy < width_y * lax.axis_size("yb"))
    shot_shape = primaries.shape[1:3]
    out_shape = shot_shape + (depth, width_x, width_y)

    def sweeps_kernel(planes_ref, inside_ref, out_ref):
        ext = planes_ref[...]
        shot_ext = ext[:shot_planes].reshape(shot_shape + (depth, ext_x, ext_y))
        sigma_ext = ext[shot_planes:].reshape(-1, depth, ext_x, ext_y)
        keep = inside_ref[...] > 0.5
        out_ref[...] = sweep_all(shot_ext, sigma_ext, keep)

    field = pl.pallas_call(
        sweeps_kernel,
        out_shape=jax.ShapeDtypeStruct(out_shape, jnp.float32),
        in_specs=[pl.BlockSpec(memory_space=pltpu.VMEM)] * 2,
        out_specs=pl.BlockSpec(memory_space=pltpu.VMEM),
    )(planes, inside.astype(jnp.float32))
    return field[None]


def solution(mesh):
    in_specs = (
        P(("survey", "tx"), None, None, None, "xb", "yb"),
        P("survey", "tx", "xb", "yb"),
        P("survey"),
        P("survey"),
    )
    out_specs = P(("survey", "tx"), None, None, None, "xb", "yb")
    return jax.shard_map(body, mesh=mesh, in_specs=in_specs, out_specs=out_specs, check_vma=False)
```

```python
import jax
import jax.numpy as jnp
from jax import lax
from jax.experimental import pallas as pl
from jax.experimental.pallas import tpu as pltpu
from jax.experimental.layout import Layout, with_layout_constraint
from jax.sharding import PartitionSpec as P

NS_DEV = 1
SWEEPS = 2


K_FREQ = 2.0
RELAX = 0.6


def inner(f):
    return f[..., :-1, :-1, :-1]


def fwd_z(f):
    return f[..., 1:, :-1, :-1] - inner(f)


def fwd_x(f):
    return f[..., :-1, 1:, :-1] - inner(f)


def fwd_y(f):
    return f[..., :-1, :-1, 1:] - inner(f)


def back_z(g):
    return g[..., 1:, 1:, 1:] - g[..., :-1, 1:, 1:]


def back_x(g):
    return g[..., 1:, 1:, 1:] - g[..., 1:, :-1, 1:]


def back_y(g):
    return g[..., 1:, 1:, 1:] - g[..., 1:, 1:, :-1]


def curl_curl(padded):
    e_x = padded[..., 0, :, :, :]
    e_y = padded[..., 1, :, :, :]
    e_z = padded[..., 2, :, :, :]
    h_x = fwd_y(e_z) - fwd_z(e_y)
    h_y = fwd_z(e_x) - fwd_x(e_z)
    h_z = fwd_x(e_y) - fwd_y(e_x)
    c_x = back_y(h_z) - back_z(h_y)
    c_y = back_z(h_x) - back_x(h_z)
    c_z = back_x(h_y) - back_y(h_x)
    return jnp.stack([c_x, c_y, c_z], axis=-4)


def jacobi(resid, kappa):
    denom = 16.0 + kappa * kappa
    real_part = (4.0 * resid[..., 0, :, :, :, :] + kappa * resid[..., 1, :, :, :, :]) / denom
    imag_part = (4.0 * resid[..., 1, :, :, :, :] - kappa * resid[..., 0, :, :, :, :]) / denom
    return jnp.stack([real_part, imag_part], axis=-5)


def source_term(shot, delta):
    return jnp.stack([delta * shot[..., 1, :, :, :, :], -delta * shot[..., 0, :, :, :, :]], axis=-5)


def shrink(f, ring):
    return f[..., ring:f.shape[-2] - ring, ring:f.shape[-1] - ring]


def pad_z(f):
    return jnp.pad(f, [(0, 0)] * (f.ndim - 3) + [(1, 1), (0, 0), (0, 0)])


def halo_faces(cells, axis, dim, width):
    count = lax.axis_size(axis)
    size = cells.shape[dim]
    head = lax.slice_in_dim(cells, 0, width, axis=dim)
    tail = lax.slice_in_dim(cells, size - width, size, axis=dim)
    if count == 2:
        got = row_major(lax.ppermute(row_major(jnp.where(lax.axis_index(axis) == 0, tail, head)), axis, [(0, 1), (1, 0)]))
        return got, got
    even = lax.axis_index(axis) % 2 == 0
    from_low = jnp.zeros_like(tail)
    from_high = jnp.zeros_like(head)
    for first in (0, 1):
        pairs = []
        for i in range(first, count - 1, 2):
            pairs += [(i, i + 1), (i + 1, i)]
        lower_is_even = first == 0
        send = row_major(jnp.where(even == lower_is_even, tail, head))
        got = row_major(lax.ppermute(send, axis, pairs))
        from_high = jnp.where(even == lower_is_even, got, from_high)
        from_low = jnp.where(even == lower_is_even, from_low, got)
    return from_low, from_high


def halo(cells, axis, dim, width):
    count = lax.axis_size(axis)
    size = cells.shape[dim]
    head = lax.slice_in_dim(cells, 0, width, axis=dim)
    tail = lax.slice_in_dim(cells, size - width, size, axis=dim)
    even = lax.axis_index(axis) % 2 == 0
    from_low = jnp.zeros_like(tail)
    from_high = jnp.zeros_like(head)
    for first in (0, 1):
        pairs = []
        for i in range(first, count - 1, 2):
            pairs += [(i, i + 1), (i + 1, i)]
        if not pairs:
            continue
        lower_is_even = first == 0
        send = row_major(jnp.where(even == lower_is_even, tail, head))
        got = row_major(lax.ppermute(send, axis, pairs))
        from_high = jnp.where(even == lower_is_even, got, from_high)
        from_low = jnp.where(even == lower_is_even, from_low, got)
    return jnp.concatenate([from_low, cells, from_high], axis=dim)


def row_major(x):
    return with_layout_constraint(x, Layout(major_to_minor=tuple(range(x.ndim))))


def sweep_all(shot_ext, sigma_ext, inside):
    kappa = K_FREQ * sigma_ext
    delta = K_FREQ * (sigma_ext - 1.0)
    rhs = source_term(shot_ext, delta)
    field = jnp.where(inside, jacobi(rhs, kappa), 0.0)
    for sweep in range(SWEEPS):
        curled = curl_curl(pad_z(field))
        field = shrink(field, 1)
        kappa = shrink(kappa, 1)
        rhs = shrink(rhs, 1)
        inside = shrink(inside, 1)
        real_part = curled[..., 0, :, :, :, :] - kappa * field[..., 1, :, :, :, :]
        imag_part = curled[..., 1, :, :, :, :] + kappa * field[..., 0, :, :, :, :]
        applied = jnp.stack([real_part, imag_part], axis=-5)
        field = field + RELAX * jacobi(rhs - applied, kappa)
        if sweep < SWEEPS - 1:
            field = jnp.where(inside, field, 0.0)
    return field


def encode_weights(group_part, sign_part, rows):
    picked = group_part[None, :] == rows[:, None]
    return jnp.where(picked, sign_part[None, :], 0).astype(jnp.float32).astype(jnp.bfloat16)


def body(primaries, conductivity, group_of, sign_of):
    nt_local = primaries.shape[0]
    depth = primaries.shape[3]
    width_x = primaries.shape[4]
    width_y = primaries.shape[5]
    n_tx = lax.axis_size("tx")
    tx_index = lax.axis_index("tx")
    other = (tx_index + 1) % n_tx
    mine = lax.broadcasted_iota(jnp.int32, (n_tx, nt_local), 0) == tx_index
    own_groups = jnp.sum(jnp.where(mine, group_of.reshape(n_tx, nt_local), 0), axis=0)
    own_signs = jnp.sum(jnp.where(mine, sign_of.reshape(n_tx, nt_local), 0), axis=0)
    rows = jnp.stack([other, tx_index]).astype(jnp.int32)
    weights = encode_weights(own_groups, own_signs, rows)
    partial = lax.dot_general(
        weights, primaries, (((1,), (0,)), ((), ())), preferred_element_type=jnp.float32
    )
    tx_ring = [(i, (i + 1) % n_tx) for i in range(n_tx)]
    got = lax.ppermute(partial[0], "tx", tx_ring)
    sigma_other = lax.ppermute(conductivity, "tx", tx_ring)
    shot = partial[1] + got
    low_first = tx_index == 0
    sigma_all = jnp.where(
        low_first,
        jnp.concatenate([conductivity, sigma_other], axis=1),
        jnp.concatenate([sigma_other, conductivity], axis=1),
    )
    ext_x = width_x + 2 * SWEEPS
    ext_y = width_y + 2 * SWEEPS
    shot_planes = shot.shape[0] * shot.shape[1] * depth
    planes = jnp.concatenate(
        [shot.reshape(-1, width_x, width_y), sigma_all.reshape(-1, width_x, width_y)], axis=0
    )
    planes = row_major(halo(row_major(planes), "xb", 1, SWEEPS))
    y_low, y_high = halo_faces(planes, "yb", 2, SWEEPS)
    gx = lax.axis_index("xb") * width_x - SWEEPS + lax.broadcasted_iota(jnp.int32, (ext_x, ext_y), 0)
    gy = lax.axis_index("yb") * width_y - SWEEPS + lax.broadcasted_iota(jnp.int32, (ext_x, ext_y), 1)
    inside = (gx >= 0) & (gx < width_x * lax.axis_size("xb")) & (gy >= 0) & (gy < width_y * lax.axis_size("yb"))
    shot_shape = primaries.shape[1:3]
    out_shape = shot_shape + (depth, width_x, width_y)

    def sweeps_kernel(planes_ref, low_ref, high_ref, inside_ref, out_ref):
        ext = jnp.concatenate([low_ref[...], planes_ref[...], high_ref[...]], axis=2)
        shot_ext = ext[:shot_planes].reshape(shot_shape + (depth, ext_x, ext_y))
        sigma_ext = ext[shot_planes:].reshape(-1, depth, ext_x, ext_y)
        keep = inside_ref[...] > 0.5
        out_ref[...] = sweep_all(shot_ext, sigma_ext, keep)

    field = pl.pallas_call(
        sweeps_kernel,
        out_shape=jax.ShapeDtypeStruct(out_shape, jnp.float32),
        in_specs=[pl.BlockSpec(memory_space=pltpu.VMEM)] * 4,
        out_specs=pl.BlockSpec(memory_space=pltpu.VMEM),
    )(planes, y_low, y_high, inside.astype(jnp.float32))
    return field[None]


def solution(mesh):
    in_specs = (
        P(("survey", "tx"), None, None, None, "xb", "yb"),
        P("survey", "tx", "xb", "yb"),
        P("survey"),
        P("survey"),
    )
    out_specs = P(("survey", "tx"), None, None, None, "xb", "yb")
    return jax.shard_map(body, mesh=mesh, in_specs=in_specs, out_specs=out_specs, check_vma=False)
```

```python
import jax
import jax.numpy as jnp
from jax import lax
from jax.experimental import pallas as pl
from jax.experimental.pallas import tpu as pltpu
from jax.experimental.layout import Layout, with_layout_constraint
from jax.sharding import PartitionSpec as P

NS_DEV = 1
SWEEPS = 2


K_FREQ = 2.0
RELAX = 0.6


def inner(f):
    return f[..., :-1, :-1, :-1]


def fwd_z(f):
    return f[..., 1:, :-1, :-1] - inner(f)


def fwd_x(f):
    return f[..., :-1, 1:, :-1] - inner(f)


def fwd_y(f):
    return f[..., :-1, :-1, 1:] - inner(f)


def back_z(g):
    return g[..., 1:, 1:, 1:] - g[..., :-1, 1:, 1:]


def back_x(g):
    return g[..., 1:, 1:, 1:] - g[..., 1:, :-1, 1:]


def back_y(g):
    return g[..., 1:, 1:, 1:] - g[..., 1:, 1:, :-1]


def curl_curl(padded):
    e_x = padded[..., 0, :, :, :]
    e_y = padded[..., 1, :, :, :]
    e_z = padded[..., 2, :, :, :]
    h_x = fwd_y(e_z) - fwd_z(e_y)
    h_y = fwd_z(e_x) - fwd_x(e_z)
    h_z = fwd_x(e_y) - fwd_y(e_x)
    c_x = back_y(h_z) - back_z(h_y)
    c_y = back_z(h_x) - back_x(h_z)
    c_z = back_x(h_y) - back_y(h_x)
    return jnp.stack([c_x, c_y, c_z], axis=-4)


def jacobi(resid, kappa):
    denom = 16.0 + kappa * kappa
    real_part = (4.0 * resid[..., 0, :, :, :, :] + kappa * resid[..., 1, :, :, :, :]) / denom
    imag_part = (4.0 * resid[..., 1, :, :, :, :] - kappa * resid[..., 0, :, :, :, :]) / denom
    return jnp.stack([real_part, imag_part], axis=-5)


def source_term(shot, delta):
    return jnp.stack([delta * shot[..., 1, :, :, :, :], -delta * shot[..., 0, :, :, :, :]], axis=-5)


def shrink(f, ring):
    return f[..., ring:f.shape[-2] - ring, ring:f.shape[-1] - ring]


def pad_z(f):
    return jnp.pad(f, [(0, 0)] * (f.ndim - 3) + [(1, 1), (0, 0), (0, 0)])


def swap_rounds(axis):
    count = lax.axis_size(axis)
    even = lax.axis_index(axis) % 2 == 0
    for first in (0, 1):
        pairs = []
        for i in range(first, count - 1, 2):
            pairs += [(i, i + 1), (i + 1, i)]
        if pairs:
            yield pairs, even == (first == 0)


def halo_faces(cells, axis, dim, width):
    count = lax.axis_size(axis)
    size = cells.shape[dim]
    head = lax.slice_in_dim(cells, 0, width, axis=dim)
    tail = lax.slice_in_dim(cells, size - width, size, axis=dim)
    if count == 2:
        got = row_major(lax.ppermute(row_major(jnp.where(lax.axis_index(axis) == 0, tail, head)), axis, [(0, 1), (1, 0)]))
        return got, got
    even = lax.axis_index(axis) % 2 == 0
    from_low = jnp.zeros_like(tail)
    from_high = jnp.zeros_like(head)
    for first in (0, 1):
        pairs = []
        for i in range(first, count - 1, 2):
            pairs += [(i, i + 1), (i + 1, i)]
        lower_is_even = first == 0
        send = row_major(jnp.where(even == lower_is_even, tail, head))
        got = row_major(lax.ppermute(send, axis, pairs))
        from_high = jnp.where(even == lower_is_even, got, from_high)
        from_low = jnp.where(even == lower_is_even, from_low, got)
    return from_low, from_high


def halo(cells, axis, dim, width):
    count = lax.axis_size(axis)
    size = cells.shape[dim]
    head = lax.slice_in_dim(cells, 0, width, axis=dim)
    tail = lax.slice_in_dim(cells, size - width, size, axis=dim)
    even = lax.axis_index(axis) % 2 == 0
    from_low = jnp.zeros_like(tail)
    from_high = jnp.zeros_like(head)
    for first in (0, 1):
        pairs = []
        for i in range(first, count - 1, 2):
            pairs += [(i, i + 1), (i + 1, i)]
        if not pairs:
            continue
        lower_is_even = first == 0
        send = row_major(jnp.where(even == lower_is_even, tail, head))
        got = row_major(lax.ppermute(send, axis, pairs))
        from_high = jnp.where(even == lower_is_even, got, from_high)
        from_low = jnp.where(even == lower_is_even, from_low, got)
    return jnp.concatenate([from_low, cells, from_high], axis=dim)


def row_major(x):
    return with_layout_constraint(x, Layout(major_to_minor=tuple(range(x.ndim))))


def sweep_all(shot_ext, sigma_ext, inside):
    kappa = K_FREQ * sigma_ext
    delta = K_FREQ * (sigma_ext - 1.0)
    rhs = source_term(shot_ext, delta)
    field = jnp.where(inside, jacobi(rhs, kappa), 0.0)
    for sweep in range(SWEEPS):
        curled = curl_curl(pad_z(field))
        field = shrink(field, 1)
        kappa = shrink(kappa, 1)
        rhs = shrink(rhs, 1)
        inside = shrink(inside, 1)
        real_part = curled[..., 0, :, :, :, :] - kappa * field[..., 1, :, :, :, :]
        imag_part = curled[..., 1, :, :, :, :] + kappa * field[..., 0, :, :, :, :]
        applied = jnp.stack([real_part, imag_part], axis=-5)
        field = field + RELAX * jacobi(rhs - applied, kappa)
        if sweep < SWEEPS - 1:
            field = jnp.where(inside, field, 0.0)
    return field


def encode_weights(group_part, sign_part, rows):
    picked = group_part[None, :] == rows[:, None]
    return jnp.where(picked, sign_part[None, :], 0).astype(jnp.float32).astype(jnp.bfloat16)


def body(primaries, conductivity, group_of, sign_of):
    nt_local = primaries.shape[0]
    depth = primaries.shape[3]
    width_x = primaries.shape[4]
    width_y = primaries.shape[5]
    n_tx = lax.axis_size("tx")
    tx_index = lax.axis_index("tx")
    other = (tx_index + 1) % n_tx
    mine = lax.broadcasted_iota(jnp.int32, (n_tx, nt_local), 0) == tx_index
    own_groups = jnp.sum(jnp.where(mine, group_of.reshape(n_tx, nt_local), 0), axis=0)
    own_signs = jnp.sum(jnp.where(mine, sign_of.reshape(n_tx, nt_local), 0), axis=0)
    rows = jnp.stack([other, tx_index]).astype(jnp.int32)
    weights = encode_weights(own_groups, own_signs, rows)
    partial = lax.dot_general(
        weights, primaries, (((1,), (0,)), ((), ())), preferred_element_type=jnp.float32
    )
    tx_ring = [(i, (i + 1) % n_tx) for i in range(n_tx)]
    got = lax.ppermute(partial[0], "tx", tx_ring)
    sigma_other = lax.ppermute(conductivity, "tx", tx_ring)
    shot = partial[1] + got
    low_first = tx_index == 0
    sigma_all = jnp.where(
        low_first,
        jnp.concatenate([conductivity, sigma_other], axis=1),
        jnp.concatenate([sigma_other, conductivity], axis=1),
    )
    shot_planes = shot.shape[0] * shot.shape[1] * depth
    ext_x = width_x + 2 * SWEEPS
    ext_y = width_y + 2 * SWEEPS
    planes = jnp.concatenate(
        [shot.reshape(-1, width_x, width_y), sigma_all.reshape(-1, width_x, width_y)], axis=0
    )
    planes = row_major(planes)
    w = SWEEPS
    x_rounds = list(swap_rounds("xb"))
    y_rounds = list(swap_rounds("yb"))
    x_gots = []
    for pairs, lower in x_rounds:
        send = row_major(jnp.where(lower, planes[:, width_x - w:], planes[:, :w]))
        x_gots.append(row_major(lax.ppermute(send, "xb", pairs)))
    flags = jnp.stack(
        [(lax.axis_index("xb") % 2 == 0).astype(jnp.int32)]
        + [lower.astype(jnp.int32) for _, lower in y_rounds]
    )
    n_x = len(x_gots)
    n_y = len(y_rounds)
    face_shape = (planes.shape[0], ext_x, w)

    def x_kernel(flags_ref, planes_ref, *refs):
        got_refs = refs[:n_x]
        planes_x_ref = refs[n_x]
        send_refs = refs[n_x + 1:]
        if n_x == 1:
            low = high = got_refs[0][...]
        else:
            even = flags_ref[0] == 1
            high = jnp.where(even, got_refs[0][...], got_refs[1][...])
            low = jnp.where(even, got_refs[1][...], got_refs[0][...])
        cells = jnp.concatenate([low, planes_ref[...], high], axis=1)
        planes_x_ref[...] = cells
        head = cells[:, :, :w]
        tail = cells[:, :, width_y - w:]
        for k in range(n_y):
            send_refs[k][...] = jnp.where(flags_ref[1 + k] == 1, tail, head)

    outs = pl.pallas_call(
        x_kernel,
        out_shape=[jax.ShapeDtypeStruct((planes.shape[0], ext_x, width_y), jnp.float32)]
        + [jax.ShapeDtypeStruct(face_shape, jnp.float32)] * n_y,
        in_specs=[pl.BlockSpec(memory_space=pltpu.SMEM)]
        + [pl.BlockSpec(memory_space=pltpu.VMEM)] * (1 + n_x),
        out_specs=[pl.BlockSpec(memory_space=pltpu.VMEM)] * (1 + n_y),
    )(flags, planes, *x_gots)
    planes = outs[0]
    y_gots = [
        row_major(lax.ppermute(row_major(send), "yb", pairs))
        for send, (pairs, _) in zip(outs[1:], y_rounds)
    ]
    if n_y == 1:
        y_low = y_high = y_gots[0]
    else:
        even_y = lax.axis_index("yb") % 2 == 0
        y_high = jnp.where(even_y, y_gots[0], y_gots[1])
        y_low = jnp.where(even_y, y_gots[1], y_gots[0])
    gx = lax.axis_index("xb") * width_x - SWEEPS + lax.broadcasted_iota(jnp.int32, (ext_x, ext_y), 0)
    gy = lax.axis_index("yb") * width_y - SWEEPS + lax.broadcasted_iota(jnp.int32, (ext_x, ext_y), 1)
    inside = (gx >= 0) & (gx < width_x * lax.axis_size("xb")) & (gy >= 0) & (gy < width_y * lax.axis_size("yb"))
    shot_shape = primaries.shape[1:3]
    out_shape = shot_shape + (depth, width_x, width_y)

    def sweeps_kernel(planes_ref, low_ref, high_ref, inside_ref, out_ref):
        ext = jnp.concatenate([low_ref[...], planes_ref[...], high_ref[...]], axis=2)
        shot_ext = ext[:shot_planes].reshape(shot_shape + (depth, ext_x, ext_y))
        sigma_ext = ext[shot_planes:].reshape(-1, depth, ext_x, ext_y)
        keep = inside_ref[...] > 0.5
        out_ref[...] = sweep_all(shot_ext, sigma_ext, keep)

    field = pl.pallas_call(
        sweeps_kernel,
        out_shape=jax.ShapeDtypeStruct(out_shape, jnp.float32),
        in_specs=[pl.BlockSpec(memory_space=pltpu.VMEM)] * 4,
        out_specs=pl.BlockSpec(memory_space=pltpu.VMEM),
    )(planes, y_low, y_high, inside.astype(jnp.float32))
    return field[None]


def solution(mesh):
    in_specs = (
        P(("survey", "tx"), None, None, None, "xb", "yb"),
        P("survey", "tx", "xb", "yb"),
        P("survey"),
        P("survey"),
    )
    out_specs = P(("survey", "tx"), None, None, None, "xb", "yb")
    return jax.shard_map(body, mesh=mesh, in_specs=in_specs, out_specs=out_specs, check_vma=False)
```

```python
import jax
import jax.numpy as jnp
from jax import lax
from jax.experimental import pallas as pl
from jax.experimental.pallas import tpu as pltpu
from jax.experimental.layout import Layout, with_layout_constraint
from jax.sharding import PartitionSpec as P

NS_DEV = 1
SWEEPS = 2


K_FREQ = 2.0
RELAX = 0.6


def inner(f):
    return f[..., :-1, :-1, :-1]


def fwd_z(f):
    return f[..., 1:, :-1, :-1] - inner(f)


def fwd_x(f):
    return f[..., :-1, 1:, :-1] - inner(f)


def fwd_y(f):
    return f[..., :-1, :-1, 1:] - inner(f)


def back_z(g):
    return g[..., 1:, 1:, 1:] - g[..., :-1, 1:, 1:]


def back_x(g):
    return g[..., 1:, 1:, 1:] - g[..., 1:, :-1, 1:]


def back_y(g):
    return g[..., 1:, 1:, 1:] - g[..., 1:, 1:, :-1]


def curl_curl(padded):
    e_x = padded[..., 0, :, :, :]
    e_y = padded[..., 1, :, :, :]
    e_z = padded[..., 2, :, :, :]
    h_x = fwd_y(e_z) - fwd_z(e_y)
    h_y = fwd_z(e_x) - fwd_x(e_z)
    h_z = fwd_x(e_y) - fwd_y(e_x)
    c_x = back_y(h_z) - back_z(h_y)
    c_y = back_z(h_x) - back_x(h_z)
    c_z = back_x(h_y) - back_y(h_x)
    return jnp.stack([c_x, c_y, c_z], axis=-4)


def jacobi(resid, kappa):
    denom = 16.0 + kappa * kappa
    real_part = (4.0 * resid[..., 0, :, :, :, :] + kappa * resid[..., 1, :, :, :, :]) / denom
    imag_part = (4.0 * resid[..., 1, :, :, :, :] - kappa * resid[..., 0, :, :, :, :]) / denom
    return jnp.stack([real_part, imag_part], axis=-5)


def source_term(shot, delta):
    return jnp.stack([delta * shot[..., 1, :, :, :, :], -delta * shot[..., 0, :, :, :, :]], axis=-5)


def shrink(f, ring):
    return f[..., ring:f.shape[-2] - ring, ring:f.shape[-1] - ring]


def pad_z(f):
    return jnp.pad(f, [(0, 0)] * (f.ndim - 3) + [(1, 1), (0, 0), (0, 0)])


def swap_rounds(axis):
    count = lax.axis_size(axis)
    even = lax.axis_index(axis) % 2 == 0
    for first in (0, 1):
        pairs = []
        for i in range(first, count - 1, 2):
            pairs += [(i, i + 1), (i + 1, i)]
        if pairs:
            yield pairs, even == (first == 0)


def halo_faces(cells, axis, dim, width):
    count = lax.axis_size(axis)
    size = cells.shape[dim]
    head = lax.slice_in_dim(cells, 0, width, axis=dim)
    tail = lax.slice_in_dim(cells, size - width, size, axis=dim)
    if count == 2:
        got = row_major(lax.ppermute(row_major(jnp.where(lax.axis_index(axis) == 0, tail, head)), axis, [(0, 1), (1, 0)]))
        return got, got
    even = lax.axis_index(axis) % 2 == 0
    from_low = jnp.zeros_like(tail)
    from_high = jnp.zeros_like(head)
    for first in (0, 1):
        pairs = []
        for i in range(first, count - 1, 2):
            pairs += [(i, i + 1), (i + 1, i)]
        lower_is_even = first == 0
        send = row_major(jnp.where(even == lower_is_even, tail, head))
        got = row_major(lax.ppermute(send, axis, pairs))
        from_high = jnp.where(even == lower_is_even, got, from_high)
        from_low = jnp.where(even == lower_is_even, from_low, got)
    return from_low, from_high


def halo(cells, axis, dim, width):
    count = lax.axis_size(axis)
    size = cells.shape[dim]
    head = lax.slice_in_dim(cells, 0, width, axis=dim)
    tail = lax.slice_in_dim(cells, size - width, size, axis=dim)
    even = lax.axis_index(axis) % 2 == 0
    from_low = jnp.zeros_like(tail)
    from_high = jnp.zeros_like(head)
    for first in (0, 1):
        pairs = []
        for i in range(first, count - 1, 2):
            pairs += [(i, i + 1), (i + 1, i)]
        if not pairs:
            continue
        lower_is_even = first == 0
        send = row_major(jnp.where(even == lower_is_even, tail, head))
        got = row_major(lax.ppermute(send, axis, pairs))
        from_high = jnp.where(even == lower_is_even, got, from_high)
        from_low = jnp.where(even == lower_is_even, from_low, got)
    return jnp.concatenate([from_low, cells, from_high], axis=dim)


def row_major(x):
    return with_layout_constraint(x, Layout(major_to_minor=tuple(range(x.ndim))))


def sweep_all(shot_ext, sigma_ext, inside):
    kappa = K_FREQ * sigma_ext
    delta = K_FREQ * (sigma_ext - 1.0)
    rhs = source_term(shot_ext, delta)
    field = jnp.where(inside, jacobi(rhs, kappa), 0.0)
    for sweep in range(SWEEPS):
        curled = curl_curl(pad_z(field))
        field = shrink(field, 1)
        kappa = shrink(kappa, 1)
        rhs = shrink(rhs, 1)
        inside = shrink(inside, 1)
        real_part = curled[..., 0, :, :, :, :] - kappa * field[..., 1, :, :, :, :]
        imag_part = curled[..., 1, :, :, :, :] + kappa * field[..., 0, :, :, :, :]
        applied = jnp.stack([real_part, imag_part], axis=-5)
        field = field + RELAX * jacobi(rhs - applied, kappa)
        if sweep < SWEEPS - 1:
            field = jnp.where(inside, field, 0.0)
    return field


def encode_weights(group_part, sign_part, rows):
    picked = group_part[None, :] == rows[:, None]
    return jnp.where(picked, sign_part[None, :], 0).astype(jnp.float32).astype(jnp.bfloat16)


def body(primaries, conductivity, group_of, sign_of):
    nt_local = primaries.shape[0]
    depth = primaries.shape[3]
    width_x = primaries.shape[4]
    width_y = primaries.shape[5]
    n_tx = lax.axis_size("tx")
    tx_index = lax.axis_index("tx")
    other = (tx_index + 1) % n_tx
    mine = lax.broadcasted_iota(jnp.int32, (n_tx, nt_local), 0) == tx_index
    own_groups = jnp.sum(jnp.where(mine, group_of.reshape(n_tx, nt_local), 0), axis=0)
    own_signs = jnp.sum(jnp.where(mine, sign_of.reshape(n_tx, nt_local), 0), axis=0)
    rows = jnp.stack([other, tx_index]).astype(jnp.int32)
    weights = encode_weights(own_groups, own_signs, rows)
    partial = lax.dot_general(
        weights, primaries, (((1,), (0,)), ((), ())), preferred_element_type=jnp.float32
    )
    tx_ring = [(i, (i + 1) % n_tx) for i in range(n_tx)]
    got = lax.ppermute(partial[0], "tx", tx_ring)
    sigma_other = lax.ppermute(conductivity, "tx", tx_ring)
    shot = partial[1] + got
    low_first = tx_index == 0
    sigma_all = jnp.where(
        low_first,
        jnp.concatenate([conductivity, sigma_other], axis=1),
        jnp.concatenate([sigma_other, conductivity], axis=1),
    )
    shot_planes = shot.shape[0] * shot.shape[1] * depth
    ext_x = width_x + 2 * SWEEPS
    ext_y = width_y + 2 * SWEEPS
    planes = jnp.concatenate(
        [shot.reshape(-1, width_x, width_y), sigma_all.reshape(-1, width_x, width_y)], axis=0
    )
    planes = row_major(planes)
    w = SWEEPS
    x_rounds = list(swap_rounds("xb"))
    y_rounds = list(swap_rounds("yb"))
    x_gots = []

    def rows(lo, hi):
        shot_rows = partial[1][..., lo:hi, :] + got[..., lo:hi, :]
        sigma_rows = jnp.where(
            low_first,
            jnp.concatenate([conductivity[..., lo:hi, :], sigma_other[..., lo:hi, :]], axis=1),
            jnp.concatenate([sigma_other[..., lo:hi, :], conductivity[..., lo:hi, :]], axis=1),
        )
        return jnp.concatenate(
            [shot_rows.reshape(-1, hi - lo, width_y), sigma_rows.reshape(-1, hi - lo, width_y)], axis=0
        )

    head_x = rows(0, w)
    tail_x = rows(width_x - w, width_x)
    for pairs, lower in x_rounds:
        send = row_major(jnp.where(lower, tail_x, head_x))
        x_gots.append(row_major(lax.ppermute(send, "xb", pairs)))
    flags = jnp.stack(
        [(lax.axis_index("xb") % 2 == 0).astype(jnp.int32)]
        + [lower.astype(jnp.int32) for _, lower in y_rounds]
    )
    n_x = len(x_gots)
    n_y = len(y_rounds)
    face_shape = (planes.shape[0], ext_x, w)

    def x_kernel(flags_ref, planes_ref, *refs):
        got_refs = refs[:n_x]
        planes_x_ref = refs[n_x]
        send_refs = refs[n_x + 1:]
        if n_x == 1:
            low = high = got_refs[0][...]
        else:
            even = flags_ref[0] == 1
            high = jnp.where(even, got_refs[0][...], got_refs[1][...])
            low = jnp.where(even, got_refs[1][...], got_refs[0][...])
        cells = jnp.concatenate([low, planes_ref[...], high], axis=1)
        planes_x_ref[...] = cells
        head = cells[:, :, :w]
        tail = cells[:, :, width_y - w:]
        for k in range(n_y):
            send_refs[k][...] = jnp.where(flags_ref[1 + k] == 1, tail, head)

    outs = pl.pallas_call(
        x_kernel,
        out_shape=[jax.ShapeDtypeStruct((planes.shape[0], ext_x, width_y), jnp.float32)]
        + [jax.ShapeDtypeStruct(face_shape, jnp.float32)] * n_y,
        in_specs=[pl.BlockSpec(memory_space=pltpu.SMEM)]
        + [pl.BlockSpec(memory_space=pltpu.VMEM)] * (1 + n_x),
        out_specs=[pl.BlockSpec(memory_space=pltpu.VMEM)] * (1 + n_y),
    )(flags, planes, *x_gots)
    planes = outs[0]
    y_gots = [
        row_major(lax.ppermute(row_major(send), "yb", pairs))
        for send, (pairs, _) in zip(outs[1:], y_rounds)
    ]
    if n_y == 1:
        y_low = y_high = y_gots[0]
    else:
        even_y = lax.axis_index("yb") % 2 == 0
        y_high = jnp.where(even_y, y_gots[0], y_gots[1])
        y_low = jnp.where(even_y, y_gots[1], y_gots[0])
    gx = lax.axis_index("xb") * width_x - SWEEPS + lax.broadcasted_iota(jnp.int32, (ext_x, ext_y), 0)
    gy = lax.axis_index("yb") * width_y - SWEEPS + lax.broadcasted_iota(jnp.int32, (ext_x, ext_y), 1)
    inside = (gx >= 0) & (gx < width_x * lax.axis_size("xb")) & (gy >= 0) & (gy < width_y * lax.axis_size("yb"))
    shot_shape = primaries.shape[1:3]
    out_shape = shot_shape + (depth, width_x, width_y)

    def sweeps_kernel(planes_ref, low_ref, high_ref, inside_ref, out_ref):
        ext = jnp.concatenate([low_ref[...], planes_ref[...], high_ref[...]], axis=2)
        shot_ext = ext[:shot_planes].reshape(shot_shape + (depth, ext_x, ext_y))
        sigma_ext = ext[shot_planes:].reshape(-1, depth, ext_x, ext_y)
        keep = inside_ref[...] > 0.5
        out_ref[...] = sweep_all(shot_ext, sigma_ext, keep)

    field = pl.pallas_call(
        sweeps_kernel,
        out_shape=jax.ShapeDtypeStruct(out_shape, jnp.float32),
        in_specs=[pl.BlockSpec(memory_space=pltpu.VMEM)] * 4,
        out_specs=pl.BlockSpec(memory_space=pltpu.VMEM),
    )(planes, y_low, y_high, inside.astype(jnp.float32))
    return field[None]


def solution(mesh):
    in_specs = (
        P(("survey", "tx"), None, None, None, "xb", "yb"),
        P("survey", "tx", "xb", "yb"),
        P("survey"),
        P("survey"),
    )
    out_specs = P(("survey", "tx"), None, None, None, "xb", "yb")
    return jax.shard_map(body, mesh=mesh, in_specs=in_specs, out_specs=out_specs, check_vma=False)
```

```python
import jax
import jax.numpy as jnp
from jax import lax
from jax.experimental import pallas as pl
from jax.experimental.pallas import tpu as pltpu
from jax.experimental.layout import Layout, with_layout_constraint
from jax.sharding import PartitionSpec as P

NS_DEV = 1
SWEEPS = 2


K_FREQ = 2.0
RELAX = 0.6


def inner(f):
    return f[..., :-1, :-1, :-1]


def fwd_z(f):
    return f[..., 1:, :-1, :-1] - inner(f)


def fwd_x(f):
    return f[..., :-1, 1:, :-1] - inner(f)


def fwd_y(f):
    return f[..., :-1, :-1, 1:] - inner(f)


def back_z(g):
    return g[..., 1:, 1:, 1:] - g[..., :-1, 1:, 1:]


def back_x(g):
    return g[..., 1:, 1:, 1:] - g[..., 1:, :-1, 1:]


def back_y(g):
    return g[..., 1:, 1:, 1:] - g[..., 1:, 1:, :-1]


def curl_curl(padded):
    e_x = padded[..., 0, :, :, :]
    e_y = padded[..., 1, :, :, :]
    e_z = padded[..., 2, :, :, :]
    h_x = fwd_y(e_z) - fwd_z(e_y)
    h_y = fwd_z(e_x) - fwd_x(e_z)
    h_z = fwd_x(e_y) - fwd_y(e_x)
    c_x = back_y(h_z) - back_z(h_y)
    c_y = back_z(h_x) - back_x(h_z)
    c_z = back_x(h_y) - back_y(h_x)
    return jnp.stack([c_x, c_y, c_z], axis=-4)


def jacobi(resid, kappa):
    denom = 16.0 + kappa * kappa
    real_part = (4.0 * resid[..., 0, :, :, :, :] + kappa * resid[..., 1, :, :, :, :]) / denom
    imag_part = (4.0 * resid[..., 1, :, :, :, :] - kappa * resid[..., 0, :, :, :, :]) / denom
    return jnp.stack([real_part, imag_part], axis=-5)


def source_term(shot, delta):
    return jnp.stack([delta * shot[..., 1, :, :, :, :], -delta * shot[..., 0, :, :, :, :]], axis=-5)


def shrink(f, ring):
    return f[..., ring:f.shape[-2] - ring, ring:f.shape[-1] - ring]


def pad_z(f):
    return jnp.pad(f, [(0, 0)] * (f.ndim - 3) + [(1, 1), (0, 0), (0, 0)])


def swap_rounds(axis):
    count = lax.axis_size(axis)
    even = lax.axis_index(axis) % 2 == 0
    for first in (0, 1):
        pairs = []
        for i in range(first, count - 1, 2):
            pairs += [(i, i + 1), (i + 1, i)]
        if pairs:
            yield pairs, even == (first == 0)


def halo_faces(cells, axis, dim, width):
    count = lax.axis_size(axis)
    size = cells.shape[dim]
    head = lax.slice_in_dim(cells, 0, width, axis=dim)
    tail = lax.slice_in_dim(cells, size - width, size, axis=dim)
    if count == 2:
        got = row_major(lax.ppermute(row_major(jnp.where(lax.axis_index(axis) == 0, tail, head)), axis, [(0, 1), (1, 0)]))
        return got, got
    even = lax.axis_index(axis) % 2 == 0
    from_low = jnp.zeros_like(tail)
    from_high = jnp.zeros_like(head)
    for first in (0, 1):
        pairs = []
        for i in range(first, count - 1, 2):
            pairs += [(i, i + 1), (i + 1, i)]
        lower_is_even = first == 0
        send = row_major(jnp.where(even == lower_is_even, tail, head))
        got = row_major(lax.ppermute(send, axis, pairs))
        from_high = jnp.where(even == lower_is_even, got, from_high)
        from_low = jnp.where(even == lower_is_even, from_low, got)
    return from_low, from_high


def halo(cells, axis, dim, width):
    count = lax.axis_size(axis)
    size = cells.shape[dim]
    head = lax.slice_in_dim(cells, 0, width, axis=dim)
    tail = lax.slice_in_dim(cells, size - width, size, axis=dim)
    even = lax.axis_index(axis) % 2 == 0
    from_low = jnp.zeros_like(tail)
    from_high = jnp.zeros_like(head)
    for first in (0, 1):
        pairs = []
        for i in range(first, count - 1, 2):
            pairs += [(i, i + 1), (i + 1, i)]
        if not pairs:
            continue
        lower_is_even = first == 0
        send = row_major(jnp.where(even == lower_is_even, tail, head))
        got = row_major(lax.ppermute(send, axis, pairs))
        from_high = jnp.where(even == lower_is_even, got, from_high)
        from_low = jnp.where(even == lower_is_even, from_low, got)
    return jnp.concatenate([from_low, cells, from_high], axis=dim)


def row_major(x):
    return with_layout_constraint(x, Layout(major_to_minor=tuple(range(x.ndim))))


def sweep_all(shot_ext, sigma_ext, inside):
    kappa = K_FREQ * sigma_ext
    delta = K_FREQ * (sigma_ext - 1.0)
    rhs = source_term(shot_ext, delta)
    field = jnp.where(inside, jacobi(rhs, kappa), 0.0)
    for sweep in range(SWEEPS):
        curled = curl_curl(pad_z(field))
        field = shrink(field, 1)
        kappa = shrink(kappa, 1)
        rhs = shrink(rhs, 1)
        inside = shrink(inside, 1)
        real_part = curled[..., 0, :, :, :, :] - kappa * field[..., 1, :, :, :, :]
        imag_part = curled[..., 1, :, :, :, :] + kappa * field[..., 0, :, :, :, :]
        applied = jnp.stack([real_part, imag_part], axis=-5)
        field = field + RELAX * jacobi(rhs - applied, kappa)
        if sweep < SWEEPS - 1:
            field = jnp.where(inside, field, 0.0)
    return field


def encode_weights(group_part, sign_part, rows):
    picked = group_part[None, :] == rows[:, None]
    return jnp.where(picked, sign_part[None, :], 0).astype(jnp.float32).astype(jnp.bfloat16)


def body(primaries, conductivity, group_of, sign_of):
    nt_local = primaries.shape[0]
    depth = primaries.shape[3]
    width_x = primaries.shape[4]
    width_y = primaries.shape[5]
    n_tx = lax.axis_size("tx")
    tx_index = lax.axis_index("tx")
    other = (tx_index + 1) % n_tx
    mine = lax.broadcasted_iota(jnp.int32, (n_tx, nt_local), 0) == tx_index
    own_groups = jnp.sum(jnp.where(mine, group_of.reshape(n_tx, nt_local), 0), axis=0)
    own_signs = jnp.sum(jnp.where(mine, sign_of.reshape(n_tx, nt_local), 0), axis=0)
    rows = jnp.stack([other, tx_index]).astype(jnp.int32)
    weights = encode_weights(own_groups, own_signs, rows)
    partial = lax.dot_general(
        weights, primaries, (((1,), (0,)), ((), ())), preferred_element_type=jnp.float32
    )
    tx_ring = [(i, (i + 1) % n_tx) for i in range(n_tx)]
    got = lax.ppermute(partial[0], "tx", tx_ring)
    sigma_other = lax.ppermute(conductivity, "tx", tx_ring)
    shot_planes = partial.shape[1] * partial.shape[2] * depth
    ext_x = width_x + 2 * SWEEPS
    ext_y = width_y + 2 * SWEEPS
    w = SWEEPS
    x_rounds = list(swap_rounds("xb"))
    y_rounds = list(swap_rounds("yb"))
    n_x = len(x_rounds)
    n_y = len(y_rounds)
    flags = jnp.stack(
        [(tx_index == 0).astype(jnp.int32), (lax.axis_index("xb") % 2 == 0).astype(jnp.int32)]
        + [lower.astype(jnp.int32) for _, lower in x_rounds]
        + [lower.astype(jnp.int32) for _, lower in y_rounds]
    )
    pieces = (partial[1], got, conductivity, sigma_other)
    n_planes = shot_planes + 2 * conductivity.shape[0] * conductivity.shape[1]
    vmem = pl.BlockSpec(memory_space=pltpu.VMEM)
    smem = pl.BlockSpec(memory_space=pltpu.SMEM)

    def planes_of(flags_ref, own_ref, got_ref, sigma_ref, other_ref):
        shot = (own_ref[...] + got_ref[...]).reshape(shot_planes, width_x, width_y)
        mine = sigma_ref[...]
        theirs = other_ref[...]
        sigma = jnp.where(
            flags_ref[0] == 1,
            jnp.concatenate([mine, theirs], axis=1),
            jnp.concatenate([theirs, mine], axis=1),
        ).reshape(-1, width_x, width_y)
        return jnp.concatenate([shot, sigma], axis=0)

    def send_kernel(flags_ref, own_ref, got_ref, sigma_ref, other_ref, *send_refs):
        cells = planes_of(flags_ref, own_ref, got_ref, sigma_ref, other_ref)
        head = cells[:, :w]
        tail = cells[:, width_x - w:]
        for k in range(n_x):
            send_refs[k][...] = jnp.where(flags_ref[2 + k] == 1, tail, head)

    x_sends = pl.pallas_call(
        send_kernel,
        out_shape=[jax.ShapeDtypeStruct((n_planes, w, width_y), jnp.float32)] * n_x,
        in_specs=[smem] + [vmem] * 4,
        out_specs=[vmem] * n_x,
    )(flags, *pieces)
    x_gots = [
        row_major(lax.ppermute(row_major(send), "xb", pairs))
        for send, (pairs, _) in zip(x_sends, x_rounds)
    ]
    face_shape = (n_planes, ext_x, w)

    def x_kernel(flags_ref, own_ref, got_ref, sigma_ref, other_ref, *refs):
        got_refs = refs[:n_x]
        planes_x_ref = refs[n_x]
        send_refs = refs[n_x + 1:]
        if n_x == 1:
            low = high = got_refs[0][...]
        else:
            even = flags_ref[1] == 1
            high = jnp.where(even, got_refs[0][...], got_refs[1][...])
            low = jnp.where(even, got_refs[1][...], got_refs[0][...])
        middle = planes_of(flags_ref, own_ref, got_ref, sigma_ref, other_ref)
        cells = jnp.concatenate([low, middle, high], axis=1)
        planes_x_ref[...] = cells
        head = cells[:, :, :w]
        tail = cells[:, :, width_y - w:]
        for k in range(n_y):
            send_refs[k][...] = jnp.where(flags_ref[2 + n_x + k] == 1, tail, head)

    outs = pl.pallas_call(
        x_kernel,
        out_shape=[jax.ShapeDtypeStruct((n_planes, ext_x, width_y), jnp.float32)]
        + [jax.ShapeDtypeStruct(face_shape, jnp.float32)] * n_y,
        in_specs=[smem] + [vmem] * (4 + n_x),
        out_specs=[vmem] * (1 + n_y),
    )(flags, *pieces, *x_gots)
    planes = outs[0]
    y_gots = [
        row_major(lax.ppermute(row_major(send), "yb", pairs))
        for send, (pairs, _) in zip(outs[1:], y_rounds)
    ]
    if n_y == 1:
        y_low = y_high = y_gots[0]
    else:
        even_y = lax.axis_index("yb") % 2 == 0
        y_high = jnp.where(even_y, y_gots[0], y_gots[1])
        y_low = jnp.where(even_y, y_gots[1], y_gots[0])
    gx = lax.axis_index("xb") * width_x - SWEEPS + lax.broadcasted_iota(jnp.int32, (ext_x, ext_y), 0)
    gy = lax.axis_index("yb") * width_y - SWEEPS + lax.broadcasted_iota(jnp.int32, (ext_x, ext_y), 1)
    inside = (gx >= 0) & (gx < width_x * lax.axis_size("xb")) & (gy >= 0) & (gy < width_y * lax.axis_size("yb"))
    shot_shape = primaries.shape[1:3]
    out_shape = shot_shape + (depth, width_x, width_y)

    def sweeps_kernel(planes_ref, low_ref, high_ref, inside_ref, out_ref):
        ext = jnp.concatenate([low_ref[...], planes_ref[...], high_ref[...]], axis=2)
        shot_ext = ext[:shot_planes].reshape(shot_shape + (depth, ext_x, ext_y))
        sigma_ext = ext[shot_planes:].reshape(-1, depth, ext_x, ext_y)
        keep = inside_ref[...] > 0.5
        out_ref[...] = sweep_all(shot_ext, sigma_ext, keep)

    field = pl.pallas_call(
        sweeps_kernel,
        out_shape=jax.ShapeDtypeStruct(out_shape, jnp.float32),
        in_specs=[pl.BlockSpec(memory_space=pltpu.VMEM)] * 4,
        out_specs=pl.BlockSpec(memory_space=pltpu.VMEM),
    )(planes, y_low, y_high, inside.astype(jnp.float32))
    return field[None]


def solution(mesh):
    in_specs = (
        P(("survey", "tx"), None, None, None, "xb", "yb"),
        P("survey", "tx", "xb", "yb"),
        P("survey"),
        P("survey"),
    )
    out_specs = P(("survey", "tx"), None, None, None, "xb", "yb")
    return jax.shard_map(body, mesh=mesh, in_specs=in_specs, out_specs=out_specs, check_vma=False)
```

```python
import jax
import jax.numpy as jnp
from jax import lax
from jax.experimental import pallas as pl
from jax.experimental.pallas import tpu as pltpu
from jax.experimental.layout import Layout, with_layout_constraint
from jax.sharding import PartitionSpec as P

NS_DEV = 1
SWEEPS = 2


K_FREQ = 2.0
RELAX = 0.6


def inner(f):
    return f[..., :-1, :-1, :-1]


def fwd_z(f):
    return f[..., 1:, :-1, :-1] - inner(f)


def fwd_x(f):
    return f[..., :-1, 1:, :-1] - inner(f)


def fwd_y(f):
    return f[..., :-1, :-1, 1:] - inner(f)


def back_z(g):
    return g[..., 1:, 1:, 1:] - g[..., :-1, 1:, 1:]


def back_x(g):
    return g[..., 1:, 1:, 1:] - g[..., 1:, :-1, 1:]


def back_y(g):
    return g[..., 1:, 1:, 1:] - g[..., 1:, 1:, :-1]


def curl_curl(padded):
    e_x = padded[..., 0, :, :, :]
    e_y = padded[..., 1, :, :, :]
    e_z = padded[..., 2, :, :, :]
    h_x = fwd_y(e_z) - fwd_z(e_y)
    h_y = fwd_z(e_x) - fwd_x(e_z)
    h_z = fwd_x(e_y) - fwd_y(e_x)
    c_x = back_y(h_z) - back_z(h_y)
    c_y = back_z(h_x) - back_x(h_z)
    c_z = back_x(h_y) - back_y(h_x)
    return jnp.stack([c_x, c_y, c_z], axis=-4)


def jacobi(resid, kappa):
    denom = 16.0 + kappa * kappa
    real_part = (4.0 * resid[..., 0, :, :, :, :] + kappa * resid[..., 1, :, :, :, :]) / denom
    imag_part = (4.0 * resid[..., 1, :, :, :, :] - kappa * resid[..., 0, :, :, :, :]) / denom
    return jnp.stack([real_part, imag_part], axis=-5)


def source_term(shot, delta):
    return jnp.stack([delta * shot[..., 1, :, :, :, :], -delta * shot[..., 0, :, :, :, :]], axis=-5)


def shrink(f, ring):
    return f[..., ring:f.shape[-2] - ring, ring:f.shape[-1] - ring]


def pad_z(f):
    return jnp.pad(f, [(0, 0)] * (f.ndim - 3) + [(1, 1), (0, 0), (0, 0)])


def swap_rounds(axis):
    count = lax.axis_size(axis)
    even = lax.axis_index(axis) % 2 == 0
    for first in (0, 1):
        pairs = []
        for i in range(first, count - 1, 2):
            pairs += [(i, i + 1), (i + 1, i)]
        if pairs:
            yield pairs, even == (first == 0)


def halo_faces(cells, axis, dim, width):
    count = lax.axis_size(axis)
    size = cells.shape[dim]
    head = lax.slice_in_dim(cells, 0, width, axis=dim)
    tail = lax.slice_in_dim(cells, size - width, size, axis=dim)
    if count == 2:
        got = row_major(lax.ppermute(row_major(jnp.where(lax.axis_index(axis) == 0, tail, head)), axis, [(0, 1), (1, 0)]))
        return got, got
    even = lax.axis_index(axis) % 2 == 0
    from_low = jnp.zeros_like(tail)
    from_high = jnp.zeros_like(head)
    for first in (0, 1):
        pairs = []
        for i in range(first, count - 1, 2):
            pairs += [(i, i + 1), (i + 1, i)]
        lower_is_even = first == 0
        send = row_major(jnp.where(even == lower_is_even, tail, head))
        got = row_major(lax.ppermute(send, axis, pairs))
        from_high = jnp.where(even == lower_is_even, got, from_high)
        from_low = jnp.where(even == lower_is_even, from_low, got)
    return from_low, from_high


def halo(cells, axis, dim, width):
    count = lax.axis_size(axis)
    size = cells.shape[dim]
    head = lax.slice_in_dim(cells, 0, width, axis=dim)
    tail = lax.slice_in_dim(cells, size - width, size, axis=dim)
    even = lax.axis_index(axis) % 2 == 0
    from_low = jnp.zeros_like(tail)
    from_high = jnp.zeros_like(head)
    for first in (0, 1):
        pairs = []
        for i in range(first, count - 1, 2):
            pairs += [(i, i + 1), (i + 1, i)]
        if not pairs:
            continue
        lower_is_even = first == 0
        send = row_major(jnp.where(even == lower_is_even, tail, head))
        got = row_major(lax.ppermute(send, axis, pairs))
        from_high = jnp.where(even == lower_is_even, got, from_high)
        from_low = jnp.where(even == lower_is_even, from_low, got)
    return jnp.concatenate([from_low, cells, from_high], axis=dim)


def row_major(x):
    return with_layout_constraint(x, Layout(major_to_minor=tuple(range(x.ndim))))


def sweep_all(shot_ext, sigma_ext, inside):
    kappa = K_FREQ * sigma_ext
    delta = K_FREQ * (sigma_ext - 1.0)
    rhs = source_term(shot_ext, delta)
    field = jnp.where(inside, jacobi(rhs, kappa), 0.0)
    for sweep in range(SWEEPS):
        curled = curl_curl(pad_z(field))
        field = shrink(field, 1)
        kappa = shrink(kappa, 1)
        rhs = shrink(rhs, 1)
        inside = shrink(inside, 1)
        real_part = curled[..., 0, :, :, :, :] - kappa * field[..., 1, :, :, :, :]
        imag_part = curled[..., 1, :, :, :, :] + kappa * field[..., 0, :, :, :, :]
        applied = jnp.stack([real_part, imag_part], axis=-5)
        field = field + RELAX * jacobi(rhs - applied, kappa)
        if sweep < SWEEPS - 1:
            field = jnp.where(inside, field, 0.0)
    return field


def encode_weights(group_part, sign_part, rows):
    picked = group_part[None, :] == rows[:, None]
    return jnp.where(picked, sign_part[None, :], 0).astype(jnp.float32).astype(jnp.bfloat16)


def body(primaries, conductivity, group_of, sign_of):
    nt_local = primaries.shape[0]
    depth = primaries.shape[3]
    width_x = primaries.shape[4]
    width_y = primaries.shape[5]
    n_tx = lax.axis_size("tx")
    tx_index = lax.axis_index("tx")
    other = (tx_index + 1) % n_tx
    mine = lax.broadcasted_iota(jnp.int32, (n_tx, nt_local), 0) == tx_index
    own_groups = jnp.sum(jnp.where(mine, group_of.reshape(n_tx, nt_local), 0), axis=0)
    own_signs = jnp.sum(jnp.where(mine, sign_of.reshape(n_tx, nt_local), 0), axis=0)
    rows = jnp.stack([other, tx_index]).astype(jnp.int32)
    weights = encode_weights(own_groups, own_signs, rows)
    partial = lax.dot_general(
        weights, primaries, (((1,), (0,)), ((), ())), preferred_element_type=jnp.float32
    )
    tx_ring = [(i, (i + 1) % n_tx) for i in range(n_tx)]
    got = lax.ppermute(partial[0], "tx", tx_ring)
    sigma_other = lax.ppermute(conductivity, "tx", tx_ring)
    shot_planes = partial.shape[1] * partial.shape[2] * depth
    ext_x = width_x + 2 * SWEEPS
    ext_y = width_y + 2 * SWEEPS
    w = SWEEPS
    x_rounds = list(swap_rounds("xb"))
    y_rounds = list(swap_rounds("yb"))
    n_x = len(x_rounds)
    n_y = len(y_rounds)
    flags = jnp.stack(
        [(tx_index == 0).astype(jnp.int32), (lax.axis_index("xb") % 2 == 0).astype(jnp.int32)]
        + [lower.astype(jnp.int32) for _, lower in x_rounds]
        + [lower.astype(jnp.int32) for _, lower in y_rounds]
    )
    pieces = (partial[1], got, conductivity, sigma_other)
    n_planes = shot_planes + 2 * conductivity.shape[0] * conductivity.shape[1]
    vmem = pl.BlockSpec(memory_space=pltpu.VMEM)
    smem = pl.BlockSpec(memory_space=pltpu.SMEM)

    def planes_of(flags_ref, own_ref, got_ref, sigma_ref, other_ref):
        shot = (own_ref[...] + got_ref[...]).reshape(shot_planes, width_x, width_y)
        mine = sigma_ref[...]
        theirs = other_ref[...]
        sigma = jnp.where(
            flags_ref[0] == 1,
            jnp.concatenate([mine, theirs], axis=1),
            jnp.concatenate([theirs, mine], axis=1),
        ).reshape(-1, width_x, width_y)
        return jnp.concatenate([shot, sigma], axis=0)

    def send_kernel(flags_ref, own_ref, got_ref, sigma_ref, other_ref, *send_refs):
        def rows(lo, hi):
            shot = (own_ref[:, :, :, lo:hi, :] + got_ref[:, :, :, lo:hi, :]).reshape(-1, hi - lo, width_y)
            mine = sigma_ref[:, :, lo:hi, :]
            theirs = other_ref[:, :, lo:hi, :]
            sigma = jnp.where(
                flags_ref[0] == 1,
                jnp.concatenate([mine, theirs], axis=1),
                jnp.concatenate([theirs, mine], axis=1),
            ).reshape(-1, hi - lo, width_y)
            return jnp.concatenate([shot, sigma], axis=0)

        head = rows(0, w)
        tail = rows(width_x - w, width_x)
        for k in range(n_x):
            send_refs[k][...] = jnp.where(flags_ref[2 + k] == 1, tail, head)

    x_sends = pl.pallas_call(
        send_kernel,
        out_shape=[jax.ShapeDtypeStruct((n_planes, w, width_y), jnp.float32)] * n_x,
        in_specs=[smem] + [vmem] * 4,
        out_specs=[vmem] * n_x,
    )(flags, *pieces)
    x_gots = [
        row_major(lax.ppermute(row_major(send), "xb", pairs))
        for send, (pairs, _) in zip(x_sends, x_rounds)
    ]
    face_shape = (n_planes, ext_x, w)

    def x_kernel(flags_ref, own_ref, got_ref, sigma_ref, other_ref, *refs):
        got_refs = refs[:n_x]
        planes_x_ref = refs[n_x]
        send_refs = refs[n_x + 1:]
        if n_x == 1:
            low = high = got_refs[0][...]
        else:
            even = flags_ref[1] == 1
            high = jnp.where(even, got_refs[0][...], got_refs[1][...])
            low = jnp.where(even, got_refs[1][...], got_refs[0][...])
        middle = planes_of(flags_ref, own_ref, got_ref, sigma_ref, other_ref)
        cells = jnp.concatenate([low, middle, high], axis=1)
        planes_x_ref[...] = cells
        head = cells[:, :, :w]
        tail = cells[:, :, width_y - w:]
        for k in range(n_y):
            send_refs[k][...] = jnp.where(flags_ref[2 + n_x + k] == 1, tail, head)

    outs = pl.pallas_call(
        x_kernel,
        out_shape=[jax.ShapeDtypeStruct((n_planes, ext_x, width_y), jnp.float32)]
        + [jax.ShapeDtypeStruct(face_shape, jnp.float32)] * n_y,
        in_specs=[smem] + [vmem] * (4 + n_x),
        out_specs=[vmem] * (1 + n_y),
    )(flags, *pieces, *x_gots)
    planes = outs[0]
    y_gots = [
        row_major(lax.ppermute(row_major(send), "yb", pairs))
        for send, (pairs, _) in zip(outs[1:], y_rounds)
    ]
    if n_y == 1:
        y_low = y_high = y_gots[0]
    else:
        even_y = lax.axis_index("yb") % 2 == 0
        y_high = jnp.where(even_y, y_gots[0], y_gots[1])
        y_low = jnp.where(even_y, y_gots[1], y_gots[0])
    gx = lax.axis_index("xb") * width_x - SWEEPS + lax.broadcasted_iota(jnp.int32, (ext_x, ext_y), 0)
    gy = lax.axis_index("yb") * width_y - SWEEPS + lax.broadcasted_iota(jnp.int32, (ext_x, ext_y), 1)
    inside = (gx >= 0) & (gx < width_x * lax.axis_size("xb")) & (gy >= 0) & (gy < width_y * lax.axis_size("yb"))
    shot_shape = primaries.shape[1:3]
    out_shape = shot_shape + (depth, width_x, width_y)

    def sweeps_kernel(planes_ref, low_ref, high_ref, inside_ref, out_ref):
        ext = jnp.concatenate([low_ref[...], planes_ref[...], high_ref[...]], axis=2)
        shot_ext = ext[:shot_planes].reshape(shot_shape + (depth, ext_x, ext_y))
        sigma_ext = ext[shot_planes:].reshape(-1, depth, ext_x, ext_y)
        keep = inside_ref[...] > 0.5
        out_ref[...] = sweep_all(shot_ext, sigma_ext, keep)

    field = pl.pallas_call(
        sweeps_kernel,
        out_shape=jax.ShapeDtypeStruct(out_shape, jnp.float32),
        in_specs=[pl.BlockSpec(memory_space=pltpu.VMEM)] * 4,
        out_specs=pl.BlockSpec(memory_space=pltpu.VMEM),
    )(planes, y_low, y_high, inside.astype(jnp.float32))
    return field[None]


def solution(mesh):
    in_specs = (
        P(("survey", "tx"), None, None, None, "xb", "yb"),
        P("survey", "tx", "xb", "yb"),
        P("survey"),
        P("survey"),
    )
    out_specs = P(("survey", "tx"), None, None, None, "xb", "yb")
    return jax.shard_map(body, mesh=mesh, in_specs=in_specs, out_specs=out_specs, check_vma=False)
```

```python
import jax
import jax.numpy as jnp
from jax import lax
from jax.experimental import pallas as pl
from jax.experimental.pallas import tpu as pltpu
from jax.experimental.layout import Layout, with_layout_constraint
from jax.sharding import PartitionSpec as P

NS_DEV = 1
SWEEPS = 2


K_FREQ = 2.0
RELAX = 0.6


def inner(f):
    return f[..., :-1, :-1, :-1]


def fwd_z(f):
    return f[..., 1:, :-1, :-1] - inner(f)


def fwd_x(f):
    return f[..., :-1, 1:, :-1] - inner(f)


def fwd_y(f):
    return f[..., :-1, :-1, 1:] - inner(f)


def back_z(g):
    return g[..., 1:, 1:, 1:] - g[..., :-1, 1:, 1:]


def back_x(g):
    return g[..., 1:, 1:, 1:] - g[..., 1:, :-1, 1:]


def back_y(g):
    return g[..., 1:, 1:, 1:] - g[..., 1:, 1:, :-1]


def curl_curl(padded):
    e_x = padded[..., 0, :, :, :]
    e_y = padded[..., 1, :, :, :]
    e_z = padded[..., 2, :, :, :]
    h_x = fwd_y(e_z) - fwd_z(e_y)
    h_y = fwd_z(e_x) - fwd_x(e_z)
    h_z = fwd_x(e_y) - fwd_y(e_x)
    c_x = back_y(h_z) - back_z(h_y)
    c_y = back_z(h_x) - back_x(h_z)
    c_z = back_x(h_y) - back_y(h_x)
    return jnp.stack([c_x, c_y, c_z], axis=-4)


def jacobi(resid, kappa):
    denom = 16.0 + kappa * kappa
    real_part = (4.0 * resid[..., 0, :, :, :, :] + kappa * resid[..., 1, :, :, :, :]) / denom
    imag_part = (4.0 * resid[..., 1, :, :, :, :] - kappa * resid[..., 0, :, :, :, :]) / denom
    return jnp.stack([real_part, imag_part], axis=-5)


def source_term(shot, delta):
    return jnp.stack([delta * shot[..., 1, :, :, :, :], -delta * shot[..., 0, :, :, :, :]], axis=-5)


def shrink(f, ring):
    return f[..., ring:f.shape[-2] - ring, ring:f.shape[-1] - ring]


def pad_z(f):
    return jnp.pad(f, [(0, 0)] * (f.ndim - 3) + [(1, 1), (0, 0), (0, 0)])


def swap_rounds(axis):
    count = lax.axis_size(axis)
    even = lax.axis_index(axis) % 2 == 0
    for first in (0, 1):
        pairs = []
        for i in range(first, count - 1, 2):
            pairs += [(i, i + 1), (i + 1, i)]
        if pairs:
            yield pairs, even == (first == 0)


def halo_faces(cells, axis, dim, width):
    count = lax.axis_size(axis)
    size = cells.shape[dim]
    head = lax.slice_in_dim(cells, 0, width, axis=dim)
    tail = lax.slice_in_dim(cells, size - width, size, axis=dim)
    if count == 2:
        got = row_major(lax.ppermute(row_major(jnp.where(lax.axis_index(axis) == 0, tail, head)), axis, [(0, 1), (1, 0)]))
        return got, got
    even = lax.axis_index(axis) % 2 == 0
    from_low = jnp.zeros_like(tail)
    from_high = jnp.zeros_like(head)
    for first in (0, 1):
        pairs = []
        for i in range(first, count - 1, 2):
            pairs += [(i, i + 1), (i + 1, i)]
        lower_is_even = first == 0
        send = row_major(jnp.where(even == lower_is_even, tail, head))
        got = row_major(lax.ppermute(send, axis, pairs))
        from_high = jnp.where(even == lower_is_even, got, from_high)
        from_low = jnp.where(even == lower_is_even, from_low, got)
    return from_low, from_high


def halo(cells, axis, dim, width):
    count = lax.axis_size(axis)
    size = cells.shape[dim]
    head = lax.slice_in_dim(cells, 0, width, axis=dim)
    tail = lax.slice_in_dim(cells, size - width, size, axis=dim)
    even = lax.axis_index(axis) % 2 == 0
    from_low = jnp.zeros_like(tail)
    from_high = jnp.zeros_like(head)
    for first in (0, 1):
        pairs = []
        for i in range(first, count - 1, 2):
            pairs += [(i, i + 1), (i + 1, i)]
        if not pairs:
            continue
        lower_is_even = first == 0
        send = row_major(jnp.where(even == lower_is_even, tail, head))
        got = row_major(lax.ppermute(send, axis, pairs))
        from_high = jnp.where(even == lower_is_even, got, from_high)
        from_low = jnp.where(even == lower_is_even, from_low, got)
    return jnp.concatenate([from_low, cells, from_high], axis=dim)


def row_major(x):
    return with_layout_constraint(x, Layout(major_to_minor=tuple(range(x.ndim))))


def sweep_all(shot_ext, sigma_ext, inside):
    kappa = K_FREQ * sigma_ext
    delta = K_FREQ * (sigma_ext - 1.0)
    rhs = source_term(shot_ext, delta)
    field = jnp.where(inside, jacobi(rhs, kappa), 0.0)
    for sweep in range(SWEEPS):
        curled = curl_curl(pad_z(field))
        field = shrink(field, 1)
        kappa = shrink(kappa, 1)
        rhs = shrink(rhs, 1)
        inside = shrink(inside, 1)
        real_part = curled[..., 0, :, :, :, :] - kappa * field[..., 1, :, :, :, :]
        imag_part = curled[..., 1, :, :, :, :] + kappa * field[..., 0, :, :, :, :]
        applied = jnp.stack([real_part, imag_part], axis=-5)
        field = field + RELAX * jacobi(rhs - applied, kappa)
        if sweep < SWEEPS - 1:
            field = jnp.where(inside, field, 0.0)
    return field


def encode_weights(group_part, sign_part, rows):
    picked = group_part[None, :] == rows[:, None]
    return jnp.where(picked, sign_part[None, :], 0).astype(jnp.float32).astype(jnp.bfloat16)


def body(primaries, conductivity, group_of, sign_of):
    nt_local = primaries.shape[0]
    depth = primaries.shape[3]
    width_x = primaries.shape[4]
    width_y = primaries.shape[5]
    n_tx = lax.axis_size("tx")
    tx_index = lax.axis_index("tx")
    other = (tx_index + 1) % n_tx
    mine = lax.broadcasted_iota(jnp.int32, (n_tx, nt_local), 0) == tx_index
    own_groups = jnp.sum(jnp.where(mine, group_of.reshape(n_tx, nt_local), 0), axis=0)
    own_signs = jnp.sum(jnp.where(mine, sign_of.reshape(n_tx, nt_local), 0), axis=0)
    rows = jnp.stack([other, tx_index]).astype(jnp.int32)
    weights = encode_weights(own_groups, own_signs, rows)
    partial = lax.dot_general(
        weights, primaries, (((1,), (0,)), ((), ())), preferred_element_type=jnp.float32
    )
    tx_ring = [(i, (i + 1) % n_tx) for i in range(n_tx)]
    got = lax.ppermute(partial[0], "tx", tx_ring)
    sigma_other = lax.ppermute(conductivity, "tx", tx_ring)
    shot_planes = partial.shape[1] * partial.shape[2] * depth
    ext_x = width_x + 2 * SWEEPS
    ext_y = width_y + 2 * SWEEPS
    w = SWEEPS
    x_rounds = list(swap_rounds("xb"))
    y_rounds = list(swap_rounds("yb"))
    n_x = len(x_rounds)
    n_y = len(y_rounds)
    flags = jnp.stack(
        [(tx_index == 0).astype(jnp.int32), (lax.axis_index("xb") % 2 == 0).astype(jnp.int32)]
        + [lower.astype(jnp.int32) for _, lower in x_rounds]
        + [lower.astype(jnp.int32) for _, lower in y_rounds]
    )
    pieces = (partial[1], got, conductivity, sigma_other)
    n_planes = shot_planes + 2 * conductivity.shape[0] * conductivity.shape[1]
    vmem = pl.BlockSpec(memory_space=pltpu.VMEM)
    smem = pl.BlockSpec(memory_space=pltpu.SMEM)

    def planes_of(flags_ref, own_ref, got_ref, sigma_ref, other_ref):
        shot = (own_ref[...] + got_ref[...]).reshape(shot_planes, width_x, width_y)
        mine = sigma_ref[...]
        theirs = other_ref[...]
        sigma = jnp.where(
            flags_ref[0] == 1,
            jnp.concatenate([mine, theirs], axis=1),
            jnp.concatenate([theirs, mine], axis=1),
        ).reshape(-1, width_x, width_y)
        return jnp.concatenate([shot, sigma], axis=0)

    def send_kernel(flags_ref, own_ref, got_ref, sigma_ref, other_ref, *send_refs):
        cells = planes_of(flags_ref, own_ref, got_ref, sigma_ref, other_ref)
        head = cells[:, :w]
        tail = cells[:, width_x - w:]
        for k in range(n_x):
            send_refs[k][...] = jnp.where(flags_ref[2 + k] == 1, tail, head)

    x_sends = pl.pallas_call(
        send_kernel,
        out_shape=[jax.ShapeDtypeStruct((n_planes, w, width_y), jnp.float32)] * n_x,
        in_specs=[smem] + [vmem] * 4,
        out_specs=[vmem] * n_x,
    )(flags, *pieces)
    x_gots = [
        row_major(lax.ppermute(row_major(send), "xb", pairs))
        for send, (pairs, _) in zip(x_sends, x_rounds)
    ]
    face_shape = (w, n_planes * ext_x)

    def x_kernel(flags_ref, own_ref, got_ref, sigma_ref, other_ref, *refs):
        got_refs = refs[:n_x]
        planes_x_ref = refs[n_x]
        send_refs = refs[n_x + 1:]
        if n_x == 1:
            low = high = got_refs[0][...]
        else:
            even = flags_ref[1] == 1
            high = jnp.where(even, got_refs[0][...], got_refs[1][...])
            low = jnp.where(even, got_refs[1][...], got_refs[0][...])
        middle = planes_of(flags_ref, own_ref, got_ref, sigma_ref, other_ref)
        cells = jnp.concatenate([low, middle, high], axis=1)
        planes_x_ref[...] = cells
        columns = cells.reshape(n_planes * ext_x, width_y).T
        head = columns[:w]
        tail = columns[width_y - w:]
        for k in range(n_y):
            send_refs[k][...] = jnp.where(flags_ref[2 + n_x + k] == 1, tail, head)

    outs = pl.pallas_call(
        x_kernel,
        out_shape=[jax.ShapeDtypeStruct((n_planes, ext_x, width_y), jnp.float32)]
        + [jax.ShapeDtypeStruct(face_shape, jnp.float32)] * n_y,
        in_specs=[smem] + [vmem] * (4 + n_x),
        out_specs=[vmem] * (1 + n_y),
    )(flags, *pieces, *x_gots)
    planes = outs[0]
    y_gots = [
        row_major(lax.ppermute(row_major(send), "yb", pairs))
        for send, (pairs, _) in zip(outs[1:], y_rounds)
    ]
    if n_y == 1:
        y_low = y_high = y_gots[0]
    else:
        even_y = lax.axis_index("yb") % 2 == 0
        y_high = jnp.where(even_y, y_gots[0], y_gots[1])
        y_low = jnp.where(even_y, y_gots[1], y_gots[0])
    gx = lax.axis_index("xb") * width_x - SWEEPS + lax.broadcasted_iota(jnp.int32, (ext_x, ext_y), 0)
    gy = lax.axis_index("yb") * width_y - SWEEPS + lax.broadcasted_iota(jnp.int32, (ext_x, ext_y), 1)
    inside = (gx >= 0) & (gx < width_x * lax.axis_size("xb")) & (gy >= 0) & (gy < width_y * lax.axis_size("yb"))
    shot_shape = primaries.shape[1:3]
    out_shape = shot_shape + (depth, width_x, width_y)

    def unflip(face):
        filler = jnp.zeros((width_y - w, face.shape[1]), face.dtype)
        back = jnp.concatenate([face, filler], axis=0).T.reshape(n_planes, ext_x, width_y)
        return back[:, :, :w]

    def sweeps_kernel(planes_ref, low_ref, high_ref, inside_ref, out_ref):
        low = unflip(low_ref[...])
        high = low if n_y == 1 else unflip(high_ref[...])
        ext = jnp.concatenate([low, planes_ref[...], high], axis=2)
        shot_ext = ext[:shot_planes].reshape(shot_shape + (depth, ext_x, ext_y))
        sigma_ext = ext[shot_planes:].reshape(-1, depth, ext_x, ext_y)
        keep = inside_ref[...] > 0.5
        out_ref[...] = sweep_all(shot_ext, sigma_ext, keep)

    field = pl.pallas_call(
        sweeps_kernel,
        out_shape=jax.ShapeDtypeStruct(out_shape, jnp.float32),
        in_specs=[pl.BlockSpec(memory_space=pltpu.VMEM)] * 4,
        out_specs=pl.BlockSpec(memory_space=pltpu.VMEM),
    )(planes, y_low, y_high, inside.astype(jnp.float32))
    return field[None]


def solution(mesh):
    in_specs = (
        P(("survey", "tx"), None, None, None, "xb", "yb"),
        P("survey", "tx", "xb", "yb"),
        P("survey"),
        P("survey"),
    )
    out_specs = P(("survey", "tx"), None, None, None, "xb", "yb")
    return jax.shard_map(body, mesh=mesh, in_specs=in_specs, out_specs=out_specs, check_vma=False)
```

```python
import jax
import jax.numpy as jnp
from jax import lax
from jax.experimental import pallas as pl
from jax.experimental.pallas import tpu as pltpu
from jax.experimental.layout import Layout, with_layout_constraint
from jax.sharding import PartitionSpec as P

NS_DEV = 1
SWEEPS = 2


K_FREQ = 2.0
RELAX = 0.6


def inner(f):
    return f[..., :-1, :-1, :-1]


def fwd_z(f):
    return f[..., 1:, :-1, :-1] - inner(f)


def fwd_x(f):
    return f[..., :-1, 1:, :-1] - inner(f)


def fwd_y(f):
    return f[..., :-1, :-1, 1:] - inner(f)


def back_z(g):
    return g[..., 1:, 1:, 1:] - g[..., :-1, 1:, 1:]


def back_x(g):
    return g[..., 1:, 1:, 1:] - g[..., 1:, :-1, 1:]


def back_y(g):
    return g[..., 1:, 1:, 1:] - g[..., 1:, 1:, :-1]


def curl_curl(padded):
    e_x = padded[..., 0, :, :, :]
    e_y = padded[..., 1, :, :, :]
    e_z = padded[..., 2, :, :, :]
    h_x = fwd_y(e_z) - fwd_z(e_y)
    h_y = fwd_z(e_x) - fwd_x(e_z)
    h_z = fwd_x(e_y) - fwd_y(e_x)
    c_x = back_y(h_z) - back_z(h_y)
    c_y = back_z(h_x) - back_x(h_z)
    c_z = back_x(h_y) - back_y(h_x)
    return jnp.stack([c_x, c_y, c_z], axis=-4)


def jacobi(resid, kappa):
    denom = 16.0 + kappa * kappa
    real_part = (4.0 * resid[..., 0, :, :, :, :] + kappa * resid[..., 1, :, :, :, :]) / denom
    imag_part = (4.0 * resid[..., 1, :, :, :, :] - kappa * resid[..., 0, :, :, :, :]) / denom
    return jnp.stack([real_part, imag_part], axis=-5)


def source_term(shot, delta):
    return jnp.stack([delta * shot[..., 1, :, :, :, :], -delta * shot[..., 0, :, :, :, :]], axis=-5)


def shrink(f, ring):
    return f[..., ring:f.shape[-2] - ring, ring:f.shape[-1] - ring]


def pad_z(f):
    return jnp.pad(f, [(0, 0)] * (f.ndim - 3) + [(1, 1), (0, 0), (0, 0)])


def swap_rounds(axis):
    count = lax.axis_size(axis)
    even = lax.axis_index(axis) % 2 == 0
    for first in (0, 1):
        pairs = []
        for i in range(first, count - 1, 2):
            pairs += [(i, i + 1), (i + 1, i)]
        if pairs:
            yield pairs, even == (first == 0)


def halo_faces(cells, axis, dim, width):
    count = lax.axis_size(axis)
    size = cells.shape[dim]
    head = lax.slice_in_dim(cells, 0, width, axis=dim)
    tail = lax.slice_in_dim(cells, size - width, size, axis=dim)
    if count == 2:
        got = row_major(lax.ppermute(row_major(jnp.where(lax.axis_index(axis) == 0, tail, head)), axis, [(0, 1), (1, 0)]))
        return got, got
    even = lax.axis_index(axis) % 2 == 0
    from_low = jnp.zeros_like(tail)
    from_high = jnp.zeros_like(head)
    for first in (0, 1):
        pairs = []
        for i in range(first, count - 1, 2):
            pairs += [(i, i + 1), (i + 1, i)]
        lower_is_even = first == 0
        send = row_major(jnp.where(even == lower_is_even, tail, head))
        got = row_major(lax.ppermute(send, axis, pairs))
        from_high = jnp.where(even == lower_is_even, got, from_high)
        from_low = jnp.where(even == lower_is_even, from_low, got)
    return from_low, from_high


def halo(cells, axis, dim, width):
    count = lax.axis_size(axis)
    size = cells.shape[dim]
    head = lax.slice_in_dim(cells, 0, width, axis=dim)
    tail = lax.slice_in_dim(cells, size - width, size, axis=dim)
    even = lax.axis_index(axis) % 2 == 0
    from_low = jnp.zeros_like(tail)
    from_high = jnp.zeros_like(head)
    for first in (0, 1):
        pairs = []
        for i in range(first, count - 1, 2):
            pairs += [(i, i + 1), (i + 1, i)]
        if not pairs:
            continue
        lower_is_even = first == 0
        send = row_major(jnp.where(even == lower_is_even, tail, head))
        got = row_major(lax.ppermute(send, axis, pairs))
        from_high = jnp.where(even == lower_is_even, got, from_high)
        from_low = jnp.where(even == lower_is_even, from_low, got)
    return jnp.concatenate([from_low, cells, from_high], axis=dim)


def row_major(x):
    return with_layout_constraint(x, Layout(major_to_minor=tuple(range(x.ndim))))


def sweep_all(shot_ext, sigma_ext, inside):
    kappa = K_FREQ * sigma_ext
    delta = K_FREQ * (sigma_ext - 1.0)
    rhs = source_term(shot_ext, delta)
    field = jnp.where(inside, jacobi(rhs, kappa), 0.0)
    for sweep in range(SWEEPS):
        curled = curl_curl(pad_z(field))
        field = shrink(field, 1)
        kappa = shrink(kappa, 1)
        rhs = shrink(rhs, 1)
        inside = shrink(inside, 1)
        real_part = curled[..., 0, :, :, :, :] - kappa * field[..., 1, :, :, :, :]
        imag_part = curled[..., 1, :, :, :, :] + kappa * field[..., 0, :, :, :, :]
        applied = jnp.stack([real_part, imag_part], axis=-5)
        field = field + RELAX * jacobi(rhs - applied, kappa)
        if sweep < SWEEPS - 1:
            field = jnp.where(inside, field, 0.0)
    return field


def encode_weights(group_part, sign_part, rows):
    picked = group_part[None, :] == rows[:, None]
    return jnp.where(picked, sign_part[None, :], 0).astype(jnp.float32).astype(jnp.bfloat16)


def body(primaries, conductivity, group_of, sign_of):
    nt_local = primaries.shape[0]
    depth = primaries.shape[3]
    width_x = primaries.shape[4]
    width_y = primaries.shape[5]
    n_tx = lax.axis_size("tx")
    tx_index = lax.axis_index("tx")
    other = (tx_index + 1) % n_tx
    mine = lax.broadcasted_iota(jnp.int32, (n_tx, nt_local), 0) == tx_index
    own_groups = jnp.sum(jnp.where(mine, group_of.reshape(n_tx, nt_local), 0), axis=0)
    own_signs = jnp.sum(jnp.where(mine, sign_of.reshape(n_tx, nt_local), 0), axis=0)
    rows = jnp.stack([other, tx_index]).astype(jnp.int32)
    weights = encode_weights(own_groups, own_signs, rows)
    partial = lax.dot_general(
        weights, primaries, (((1,), (0,)), ((), ())), preferred_element_type=jnp.float32
    )
    tx_ring = [(i, (i + 1) % n_tx) for i in range(n_tx)]
    got = lax.ppermute(partial[0], "tx", tx_ring)
    sigma_other = lax.ppermute(conductivity, "tx", tx_ring)
    shot_planes = partial.shape[1] * partial.shape[2] * depth
    ext_x = width_x + 2 * SWEEPS
    ext_y = width_y + 2 * SWEEPS
    w = SWEEPS
    x_rounds = list(swap_rounds("xb"))
    y_rounds = list(swap_rounds("yb"))
    n_x = len(x_rounds)
    n_y = len(y_rounds)
    flags = jnp.stack(
        [(tx_index == 0).astype(jnp.int32), (lax.axis_index("xb") % 2 == 0).astype(jnp.int32)]
        + [lower.astype(jnp.int32) for _, lower in x_rounds]
        + [lower.astype(jnp.int32) for _, lower in y_rounds]
    )
    pieces = (partial[1], got, conductivity, sigma_other)
    n_planes = shot_planes + 2 * conductivity.shape[0] * conductivity.shape[1]
    vmem = pl.BlockSpec(memory_space=pltpu.VMEM)
    smem = pl.BlockSpec(memory_space=pltpu.SMEM)

    def planes_of(flags_ref, own_ref, got_ref, sigma_ref, other_ref):
        shot = (own_ref[...] + got_ref[...]).reshape(shot_planes, width_x, width_y)
        mine = sigma_ref[...]
        theirs = other_ref[...]
        sigma = jnp.where(
            flags_ref[0] == 1,
            jnp.concatenate([mine, theirs], axis=1),
            jnp.concatenate([theirs, mine], axis=1),
        ).reshape(-1, width_x, width_y)
        return jnp.concatenate([shot, sigma], axis=0)

    def send_kernel(flags_ref, own_ref, got_ref, sigma_ref, other_ref, *send_refs):
        cells = planes_of(flags_ref, own_ref, got_ref, sigma_ref, other_ref)
        head = cells[:, :w]
        tail = cells[:, width_x - w:]
        for k in range(n_x):
            send_refs[k][...] = jnp.where(flags_ref[2 + k] == 1, tail, head)

    x_sends = pl.pallas_call(
        send_kernel,
        out_shape=[jax.ShapeDtypeStruct((n_planes, w, width_y), jnp.float32)] * n_x,
        in_specs=[smem] + [vmem] * 4,
        out_specs=[vmem] * n_x,
    )(flags, *pieces)
    x_gots = [
        row_major(lax.ppermute(row_major(send), "xb", pairs))
        for send, (pairs, _) in zip(x_sends, x_rounds)
    ]
    face_shape = (w, n_planes * ext_x)

    def x_cells(flags_ref, own_ref, got_ref, sigma_ref, other_ref, got_refs):
        if n_x == 1:
            low = high = got_refs[0][...]
        else:
            even = flags_ref[1] == 1
            high = jnp.where(even, got_refs[0][...], got_refs[1][...])
            low = jnp.where(even, got_refs[1][...], got_refs[0][...])
        middle = planes_of(flags_ref, own_ref, got_ref, sigma_ref, other_ref)
        return jnp.concatenate([low, middle, high], axis=1)

    def x_kernel(flags_ref, own_ref, got_ref, sigma_ref, other_ref, *refs):
        got_refs = refs[:n_x]
        send_refs = refs[n_x:]
        cells = x_cells(flags_ref, own_ref, got_ref, sigma_ref, other_ref, got_refs)
        columns = cells.reshape(n_planes * ext_x, width_y).T
        head = columns[:w]
        tail = columns[width_y - w:]
        for k in range(n_y):
            send_refs[k][...] = jnp.where(flags_ref[2 + n_x + k] == 1, tail, head)

    y_sends = pl.pallas_call(
        x_kernel,
        out_shape=[jax.ShapeDtypeStruct(face_shape, jnp.float32)] * n_y,
        in_specs=[smem] + [vmem] * (4 + n_x),
        out_specs=[vmem] * n_y,
    )(flags, *pieces, *x_gots)
    y_gots = [
        row_major(lax.ppermute(row_major(send), "yb", pairs))
        for send, (pairs, _) in zip(y_sends, y_rounds)
    ]
    if n_y == 1:
        y_low = y_high = y_gots[0]
    else:
        even_y = lax.axis_index("yb") % 2 == 0
        y_high = jnp.where(even_y, y_gots[0], y_gots[1])
        y_low = jnp.where(even_y, y_gots[1], y_gots[0])
    gx = lax.axis_index("xb") * width_x - SWEEPS + lax.broadcasted_iota(jnp.int32, (ext_x, ext_y), 0)
    gy = lax.axis_index("yb") * width_y - SWEEPS + lax.broadcasted_iota(jnp.int32, (ext_x, ext_y), 1)
    inside = (gx >= 0) & (gx < width_x * lax.axis_size("xb")) & (gy >= 0) & (gy < width_y * lax.axis_size("yb"))
    shot_shape = primaries.shape[1:3]
    out_shape = shot_shape + (depth, width_x, width_y)

    def unflip(face):
        filler = jnp.zeros((width_y - w, face.shape[1]), face.dtype)
        back = jnp.concatenate([face, filler], axis=0).T.reshape(n_planes, ext_x, width_y)
        return back[:, :, :w]

    def sweeps_kernel(flags_ref, own_ref, got_ref, sigma_ref, other_ref, *refs):
        got_refs = refs[:n_x]
        low_ref, high_ref, inside_ref, out_ref = refs[n_x:]
        cells = x_cells(flags_ref, own_ref, got_ref, sigma_ref, other_ref, got_refs)
        low = unflip(low_ref[...])
        high = low if n_y == 1 else unflip(high_ref[...])
        ext = jnp.concatenate([low, cells, high], axis=2)
        shot_ext = ext[:shot_planes].reshape(shot_shape + (depth, ext_x, ext_y))
        sigma_ext = ext[shot_planes:].reshape(-1, depth, ext_x, ext_y)
        keep = inside_ref[...] > 0.5
        out_ref[...] = sweep_all(shot_ext, sigma_ext, keep)

    field = pl.pallas_call(
        sweeps_kernel,
        out_shape=jax.ShapeDtypeStruct(out_shape, jnp.float32),
        in_specs=[smem] + [vmem] * (4 + n_x + 3),
        out_specs=vmem,
    )(flags, *pieces, *x_gots, y_low, y_high, inside.astype(jnp.float32))
    return field[None]


def solution(mesh):
    in_specs = (
        P(("survey", "tx"), None, None, None, "xb", "yb"),
        P("survey", "tx", "xb", "yb"),
        P("survey"),
        P("survey"),
    )
    out_specs = P(("survey", "tx"), None, None, None, "xb", "yb")
    return jax.shard_map(body, mesh=mesh, in_specs=in_specs, out_specs=out_specs, check_vma=False)
```

```python
import jax
import jax.numpy as jnp
from jax import lax
from jax.experimental import pallas as pl
from jax.experimental.pallas import tpu as pltpu
from jax.experimental.layout import Layout, with_layout_constraint
from jax.sharding import PartitionSpec as P

NS_DEV = 1
SWEEPS = 2


K_FREQ = 2.0
RELAX = 0.6


def inner(f):
    return f[..., :-1, :-1, :-1]


def fwd_z(f):
    return f[..., 1:, :-1, :-1] - inner(f)


def fwd_x(f):
    return f[..., :-1, 1:, :-1] - inner(f)


def fwd_y(f):
    return f[..., :-1, :-1, 1:] - inner(f)


def back_z(g):
    return g[..., 1:, 1:, 1:] - g[..., :-1, 1:, 1:]


def back_x(g):
    return g[..., 1:, 1:, 1:] - g[..., 1:, :-1, 1:]


def back_y(g):
    return g[..., 1:, 1:, 1:] - g[..., 1:, 1:, :-1]


def curl_curl(padded):
    e_x = padded[..., 0, :, :, :]
    e_y = padded[..., 1, :, :, :]
    e_z = padded[..., 2, :, :, :]
    h_x = fwd_y(e_z) - fwd_z(e_y)
    h_y = fwd_z(e_x) - fwd_x(e_z)
    h_z = fwd_x(e_y) - fwd_y(e_x)
    c_x = back_y(h_z) - back_z(h_y)
    c_y = back_z(h_x) - back_x(h_z)
    c_z = back_x(h_y) - back_y(h_x)
    return jnp.stack([c_x, c_y, c_z], axis=-4)


def jacobi(resid, kappa):
    denom = 16.0 + kappa * kappa
    real_part = (4.0 * resid[..., 0, :, :, :, :] + kappa * resid[..., 1, :, :, :, :]) / denom
    imag_part = (4.0 * resid[..., 1, :, :, :, :] - kappa * resid[..., 0, :, :, :, :]) / denom
    return jnp.stack([real_part, imag_part], axis=-5)


def source_term(shot, delta):
    return jnp.stack([delta * shot[..., 1, :, :, :, :], -delta * shot[..., 0, :, :, :, :]], axis=-5)


def shrink(f, ring):
    return f[..., ring:f.shape[-2] - ring, ring:f.shape[-1] - ring]


def pad_z(f):
    return jnp.pad(f, [(0, 0)] * (f.ndim - 3) + [(1, 1), (0, 0), (0, 0)])


def swap_rounds(axis):
    count = lax.axis_size(axis)
    even = lax.axis_index(axis) % 2 == 0
    for first in (0, 1):
        pairs = []
        for i in range(first, count - 1, 2):
            pairs += [(i, i + 1), (i + 1, i)]
        if pairs:
            yield pairs, even == (first == 0)


def halo_faces(cells, axis, dim, width):
    count = lax.axis_size(axis)
    size = cells.shape[dim]
    head = lax.slice_in_dim(cells, 0, width, axis=dim)
    tail = lax.slice_in_dim(cells, size - width, size, axis=dim)
    if count == 2:
        got = row_major(lax.ppermute(row_major(jnp.where(lax.axis_index(axis) == 0, tail, head)), axis, [(0, 1), (1, 0)]))
        return got, got
    even = lax.axis_index(axis) % 2 == 0
    from_low = jnp.zeros_like(tail)
    from_high = jnp.zeros_like(head)
    for first in (0, 1):
        pairs = []
        for i in range(first, count - 1, 2):
            pairs += [(i, i + 1), (i + 1, i)]
        lower_is_even = first == 0
        send = row_major(jnp.where(even == lower_is_even, tail, head))
        got = row_major(lax.ppermute(send, axis, pairs))
        from_high = jnp.where(even == lower_is_even, got, from_high)
        from_low = jnp.where(even == lower_is_even, from_low, got)
    return from_low, from_high


def halo(cells, axis, dim, width):
    count = lax.axis_size(axis)
    size = cells.shape[dim]
    head = lax.slice_in_dim(cells, 0, width, axis=dim)
    tail = lax.slice_in_dim(cells, size - width, size, axis=dim)
    even = lax.axis_index(axis) % 2 == 0
    from_low = jnp.zeros_like(tail)
    from_high = jnp.zeros_like(head)
    for first in (0, 1):
        pairs = []
        for i in range(first, count - 1, 2):
            pairs += [(i, i + 1), (i + 1, i)]
        if not pairs:
            continue
        lower_is_even = first == 0
        send = row_major(jnp.where(even == lower_is_even, tail, head))
        got = row_major(lax.ppermute(send, axis, pairs))
        from_high = jnp.where(even == lower_is_even, got, from_high)
        from_low = jnp.where(even == lower_is_even, from_low, got)
    return jnp.concatenate([from_low, cells, from_high], axis=dim)


def row_major(x):
    return with_layout_constraint(x, Layout(major_to_minor=tuple(range(x.ndim))))


def sweep_all(shot_ext, sigma_ext, inside, outer):
    kappa = K_FREQ * sigma_ext
    delta = K_FREQ * (sigma_ext - 1.0)
    rhs = source_term(shot_ext, delta)
    field = jnp.where(inside, jnp.where(outer, shot_ext, jacobi(rhs, kappa)), 0.0)
    for sweep in range(SWEEPS):
        curled = curl_curl(pad_z(field))
        field = shrink(field, 1)
        kappa = shrink(kappa, 1)
        rhs = shrink(rhs, 1)
        inside = shrink(inside, 1)
        real_part = curled[..., 0, :, :, :, :] - kappa * field[..., 1, :, :, :, :]
        imag_part = curled[..., 1, :, :, :, :] + kappa * field[..., 0, :, :, :, :]
        applied = jnp.stack([real_part, imag_part], axis=-5)
        field = field + RELAX * jacobi(rhs - applied, kappa)
        if sweep < SWEEPS - 1:
            field = jnp.where(inside, field, 0.0)
    return field


def encode_weights(group_part, sign_part, rows):
    picked = group_part[None, :] == rows[:, None]
    return jnp.where(picked, sign_part[None, :], 0).astype(jnp.float32).astype(jnp.bfloat16)


def body(primaries, conductivity, group_of, sign_of):
    nt_local = primaries.shape[0]
    depth = primaries.shape[3]
    width_x = primaries.shape[4]
    width_y = primaries.shape[5]
    n_tx = lax.axis_size("tx")
    tx_index = lax.axis_index("tx")
    other = (tx_index + 1) % n_tx
    mine = lax.broadcasted_iota(jnp.int32, (n_tx, nt_local), 0) == tx_index
    own_groups = jnp.sum(jnp.where(mine, group_of.reshape(n_tx, nt_local), 0), axis=0)
    own_signs = jnp.sum(jnp.where(mine, sign_of.reshape(n_tx, nt_local), 0), axis=0)
    rows = jnp.stack([other, tx_index]).astype(jnp.int32)
    weights = encode_weights(own_groups, own_signs, rows)
    partial = lax.dot_general(
        weights, primaries, (((1,), (0,)), ((), ())), preferred_element_type=jnp.float32
    )
    tx_ring = [(i, (i + 1) % n_tx) for i in range(n_tx)]
    got = lax.ppermute(partial[0], "tx", tx_ring)
    sigma_other = lax.ppermute(conductivity, "tx", tx_ring)
    shot_planes = partial.shape[1] * partial.shape[2] * depth
    ext_x = width_x + 2 * SWEEPS
    ext_y = width_y + 2 * SWEEPS
    w = SWEEPS
    x_rounds = list(swap_rounds("xb"))
    y_rounds = list(swap_rounds("yb"))
    n_x = len(x_rounds)
    n_y = len(y_rounds)
    flags = jnp.stack(
        [(tx_index == 0).astype(jnp.int32), (lax.axis_index("xb") % 2 == 0).astype(jnp.int32)]
        + [lower.astype(jnp.int32) for _, lower in x_rounds]
        + [lower.astype(jnp.int32) for _, lower in y_rounds]
    )
    pieces = (partial[1], got, conductivity, sigma_other)
    n_planes = shot_planes + 2 * conductivity.shape[0] * conductivity.shape[1]
    vmem = pl.BlockSpec(memory_space=pltpu.VMEM)
    smem = pl.BlockSpec(memory_space=pltpu.SMEM)

    def planes_of(flags_ref, own_ref, got_ref, sigma_ref, other_ref):
        shot = (own_ref[...] + got_ref[...]).reshape(shot_planes, width_x, width_y)
        mine = sigma_ref[...]
        theirs = other_ref[...]
        sigma = jnp.where(
            flags_ref[0] == 1,
            jnp.concatenate([mine, theirs], axis=1),
            jnp.concatenate([theirs, mine], axis=1),
        ).reshape(-1, width_x, width_y)
        return jnp.concatenate([shot, sigma], axis=0)

    row_shot = primaries.shape[1:3] + (depth, 1, width_y)
    payload_planes = n_planes * (w - 1) + shot_planes

    def field0_row(row):
        shot = row[:shot_planes].reshape(row_shot)
        sigma = row[shot_planes:].reshape(-1, depth, 1, width_y)
        rhs = source_term(shot, K_FREQ * (sigma - 1.0))
        return jacobi(rhs, K_FREQ * sigma).reshape(shot_planes, 1, width_y)

    def send_kernel(flags_ref, own_ref, got_ref, sigma_ref, other_ref, *send_refs):
        cells = planes_of(flags_ref, own_ref, got_ref, sigma_ref, other_ref)

        def payload(inner_rows, outer_row):
            parts = [cells[:, r:r + 1] for r in inner_rows]
            parts.append(field0_row(cells[:, outer_row:outer_row + 1]))
            return jnp.concatenate(parts, axis=0)

        head = payload(range(0, w - 1), w - 1)
        tail = payload(range(width_x - w + 1, width_x), width_x - w)
        for k in range(n_x):
            send_refs[k][...] = jnp.where(flags_ref[2 + k] == 1, tail, head)

    x_sends = pl.pallas_call(
        send_kernel,
        out_shape=[jax.ShapeDtypeStruct((payload_planes, 1, width_y), jnp.float32)] * n_x,
        in_specs=[smem] + [vmem] * 4,
        out_specs=[vmem] * n_x,
    )(flags, *pieces)
    x_gots = [
        row_major(lax.ppermute(row_major(send), "xb", pairs))
        for send, (pairs, _) in zip(x_sends, x_rounds)
    ]
    face_shape = (w, n_planes * ext_x)

    def decode(payload, outer_first):
        inner = [payload[k * n_planes:(k + 1) * n_planes] for k in range(w - 1)]
        field0 = payload[n_planes * (w - 1):]
        filler = jnp.zeros((n_planes - shot_planes, 1, width_y), payload.dtype)
        outer = jnp.concatenate([field0, filler], axis=0)
        return jnp.concatenate([outer] + inner if outer_first else inner + [outer], axis=1)

    def x_cells(flags_ref, own_ref, got_ref, sigma_ref, other_ref, got_refs):
        if n_x == 1:
            low = high = got_refs[0][...]
        else:
            even = flags_ref[1] == 1
            high = jnp.where(even, got_refs[0][...], got_refs[1][...])
            low = jnp.where(even, got_refs[1][...], got_refs[0][...])
        low = decode(low, True)
        high = decode(high, False)
        middle = planes_of(flags_ref, own_ref, got_ref, sigma_ref, other_ref)
        return jnp.concatenate([low, middle, high], axis=1)

    def x_kernel(flags_ref, own_ref, got_ref, sigma_ref, other_ref, *refs):
        got_refs = refs[:n_x]
        send_refs = refs[n_x:]
        cells = x_cells(flags_ref, own_ref, got_ref, sigma_ref, other_ref, got_refs)
        columns = cells.reshape(n_planes * ext_x, width_y).T
        head = columns[:w]
        tail = columns[width_y - w:]
        for k in range(n_y):
            send_refs[k][...] = jnp.where(flags_ref[2 + n_x + k] == 1, tail, head)

    y_sends = pl.pallas_call(
        x_kernel,
        out_shape=[jax.ShapeDtypeStruct(face_shape, jnp.float32)] * n_y,
        in_specs=[smem] + [vmem] * (4 + n_x),
        out_specs=[vmem] * n_y,
    )(flags, *pieces, *x_gots)
    y_gots = [
        row_major(lax.ppermute(row_major(send), "yb", pairs))
        for send, (pairs, _) in zip(y_sends, y_rounds)
    ]
    if n_y == 1:
        y_low = y_high = y_gots[0]
    else:
        even_y = lax.axis_index("yb") % 2 == 0
        y_high = jnp.where(even_y, y_gots[0], y_gots[1])
        y_low = jnp.where(even_y, y_gots[1], y_gots[0])
    gx = lax.axis_index("xb") * width_x - SWEEPS + lax.broadcasted_iota(jnp.int32, (ext_x, ext_y), 0)
    gy = lax.axis_index("yb") * width_y - SWEEPS + lax.broadcasted_iota(jnp.int32, (ext_x, ext_y), 1)
    inside = (gx >= 0) & (gx < width_x * lax.axis_size("xb")) & (gy >= 0) & (gy < width_y * lax.axis_size("yb"))
    shot_shape = primaries.shape[1:3]
    out_shape = shot_shape + (depth, width_x, width_y)

    def unflip(face):
        filler = jnp.zeros((width_y - w, face.shape[1]), face.dtype)
        back = jnp.concatenate([face, filler], axis=0).T.reshape(n_planes, ext_x, width_y)
        return back[:, :, :w]

    def sweeps_kernel(flags_ref, own_ref, got_ref, sigma_ref, other_ref, *refs):
        got_refs = refs[:n_x]
        low_ref, high_ref, inside_ref, out_ref = refs[n_x:]
        cells = x_cells(flags_ref, own_ref, got_ref, sigma_ref, other_ref, got_refs)
        low = unflip(low_ref[...])
        high = low if n_y == 1 else unflip(high_ref[...])
        ext = jnp.concatenate([low, cells, high], axis=2)
        shot_ext = ext[:shot_planes].reshape(shot_shape + (depth, ext_x, ext_y))
        sigma_ext = ext[shot_planes:].reshape(-1, depth, ext_x, ext_y)
        keep = inside_ref[...] > 0.5
        row = lax.broadcasted_iota(jnp.int32, (ext_x, ext_y), 0)
        outer = (row == 0) | (row == ext_x - 1)
        out_ref[...] = sweep_all(shot_ext, sigma_ext, keep, outer)

    field = pl.pallas_call(
        sweeps_kernel,
        out_shape=jax.ShapeDtypeStruct(out_shape, jnp.float32),
        in_specs=[smem] + [vmem] * (4 + n_x + 3),
        out_specs=vmem,
    )(flags, *pieces, *x_gots, y_low, y_high, inside.astype(jnp.float32))
    return field[None]


def solution(mesh):
    in_specs = (
        P(("survey", "tx"), None, None, None, "xb", "yb"),
        P("survey", "tx", "xb", "yb"),
        P("survey"),
        P("survey"),
    )
    out_specs = P(("survey", "tx"), None, None, None, "xb", "yb")
    return jax.shard_map(body, mesh=mesh, in_specs=in_specs, out_specs=out_specs, check_vma=False)
```

```python
import jax
import jax.numpy as jnp
from jax import lax
from jax.experimental import pallas as pl
from jax.experimental.pallas import tpu as pltpu
from jax.experimental.layout import Layout, with_layout_constraint
from jax.sharding import PartitionSpec as P

NS_DEV = 1
SWEEPS = 2


K_FREQ = 2.0
RELAX = 0.6


def inner(f):
    return f[..., :-1, :-1, :-1]


def fwd_z(f):
    return f[..., 1:, :-1, :-1] - inner(f)


def fwd_x(f):
    return f[..., :-1, 1:, :-1] - inner(f)


def fwd_y(f):
    return f[..., :-1, :-1, 1:] - inner(f)


def back_z(g):
    return g[..., 1:, 1:, 1:] - g[..., :-1, 1:, 1:]


def back_x(g):
    return g[..., 1:, 1:, 1:] - g[..., 1:, :-1, 1:]


def back_y(g):
    return g[..., 1:, 1:, 1:] - g[..., 1:, 1:, :-1]


def curl_curl(padded):
    e_x = padded[..., 0, :, :, :]
    e_y = padded[..., 1, :, :, :]
    e_z = padded[..., 2, :, :, :]
    h_x = fwd_y(e_z) - fwd_z(e_y)
    h_y = fwd_z(e_x) - fwd_x(e_z)
    h_z = fwd_x(e_y) - fwd_y(e_x)
    c_x = back_y(h_z) - back_z(h_y)
    c_y = back_z(h_x) - back_x(h_z)
    c_z = back_x(h_y) - back_y(h_x)
    return jnp.stack([c_x, c_y, c_z], axis=-4)


def jacobi(resid, kappa):
    denom = 16.0 + kappa * kappa
    real_part = (4.0 * resid[..., 0, :, :, :, :] + kappa * resid[..., 1, :, :, :, :]) / denom
    imag_part = (4.0 * resid[..., 1, :, :, :, :] - kappa * resid[..., 0, :, :, :, :]) / denom
    return jnp.stack([real_part, imag_part], axis=-5)


def source_term(shot, delta):
    return jnp.stack([delta * shot[..., 1, :, :, :, :], -delta * shot[..., 0, :, :, :, :]], axis=-5)


def shrink(f, ring):
    return f[..., ring:f.shape[-2] - ring, ring:f.shape[-1] - ring]


def pad_z(f):
    return jnp.pad(f, [(0, 0)] * (f.ndim - 3) + [(1, 1), (0, 0), (0, 0)])


def swap_rounds(axis):
    count = lax.axis_size(axis)
    even = lax.axis_index(axis) % 2 == 0
    for first in (0, 1):
        pairs = []
        for i in range(first, count - 1, 2):
            pairs += [(i, i + 1), (i + 1, i)]
        if pairs:
            yield pairs, even == (first == 0)


def halo_faces(cells, axis, dim, width):
    count = lax.axis_size(axis)
    size = cells.shape[dim]
    head = lax.slice_in_dim(cells, 0, width, axis=dim)
    tail = lax.slice_in_dim(cells, size - width, size, axis=dim)
    if count == 2:
        got = row_major(lax.ppermute(row_major(jnp.where(lax.axis_index(axis) == 0, tail, head)), axis, [(0, 1), (1, 0)]))
        return got, got
    even = lax.axis_index(axis) % 2 == 0
    from_low = jnp.zeros_like(tail)
    from_high = jnp.zeros_like(head)
    for first in (0, 1):
        pairs = []
        for i in range(first, count - 1, 2):
            pairs += [(i, i + 1), (i + 1, i)]
        lower_is_even = first == 0
        send = row_major(jnp.where(even == lower_is_even, tail, head))
        got = row_major(lax.ppermute(send, axis, pairs))
        from_high = jnp.where(even == lower_is_even, got, from_high)
        from_low = jnp.where(even == lower_is_even, from_low, got)
    return from_low, from_high


def halo(cells, axis, dim, width):
    count = lax.axis_size(axis)
    size = cells.shape[dim]
    head = lax.slice_in_dim(cells, 0, width, axis=dim)
    tail = lax.slice_in_dim(cells, size - width, size, axis=dim)
    even = lax.axis_index(axis) % 2 == 0
    from_low = jnp.zeros_like(tail)
    from_high = jnp.zeros_like(head)
    for first in (0, 1):
        pairs = []
        for i in range(first, count - 1, 2):
            pairs += [(i, i + 1), (i + 1, i)]
        if not pairs:
            continue
        lower_is_even = first == 0
        send = row_major(jnp.where(even == lower_is_even, tail, head))
        got = row_major(lax.ppermute(send, axis, pairs))
        from_high = jnp.where(even == lower_is_even, got, from_high)
        from_low = jnp.where(even == lower_is_even, from_low, got)
    return jnp.concatenate([from_low, cells, from_high], axis=dim)


def row_major(x):
    return with_layout_constraint(x, Layout(major_to_minor=tuple(range(x.ndim))))


def sweep_all(shot_ext, sigma_ext, inside, outer):
    kappa = K_FREQ * sigma_ext
    delta = K_FREQ * (sigma_ext - 1.0)
    rhs = source_term(shot_ext, delta)
    field = jnp.where(inside, jnp.where(outer, shot_ext, jacobi(rhs, kappa)), 0.0)
    for sweep in range(SWEEPS):
        curled = curl_curl(pad_z(field))
        field = shrink(field, 1)
        kappa = shrink(kappa, 1)
        rhs = shrink(rhs, 1)
        inside = shrink(inside, 1)
        real_part = curled[..., 0, :, :, :, :] - kappa * field[..., 1, :, :, :, :]
        imag_part = curled[..., 1, :, :, :, :] + kappa * field[..., 0, :, :, :, :]
        applied = jnp.stack([real_part, imag_part], axis=-5)
        field = field + RELAX * jacobi(rhs - applied, kappa)
        if sweep < SWEEPS - 1:
            field = jnp.where(inside, field, 0.0)
    return field


def rolled_sweeps(shot_ext, sigma_ext, inside, outer, rows, lanes):
    def nxt(f, axis):
        return pltpu.roll(f, (lanes if axis == -1 else rows) - 1, axis=f.ndim + axis)

    def prv(f, axis):
        return pltpu.roll(f, 1, axis=f.ndim + axis)

    def curl(field):
        padded = pad_z(field)
        above = padded[..., 1:, :, :]
        here = padded[..., :-1, :, :]

        def dz(c):
            return above[..., c, :, :, :] - here[..., c, :, :, :]

        def dx(c):
            return nxt(here[..., c, :, :, :], -2) - here[..., c, :, :, :]

        def dy(c):
            return nxt(here[..., c, :, :, :], -1) - here[..., c, :, :, :]

        h_x = dy(2) - dz(1)
        h_y = dz(0) - dx(2)
        h_z = dx(1) - dy(0)

        def bz(g):
            return g[..., 1:, :, :] - g[..., :-1, :, :]

        def bx(g):
            return g[..., 1:, :, :] - prv(g[..., 1:, :, :], -2)

        def by(g):
            return g[..., 1:, :, :] - prv(g[..., 1:, :, :], -1)

        c_x = by(h_z) - bz(h_y)
        c_y = bz(h_x) - bx(h_z)
        c_z = bx(h_y) - by(h_x)
        return jnp.stack([c_x, c_y, c_z], axis=-4)

    kappa = K_FREQ * sigma_ext
    delta = K_FREQ * (sigma_ext - 1.0)
    rhs = source_term(shot_ext, delta)
    field = jnp.where(inside, jnp.where(outer, shot_ext, jacobi(rhs, kappa)), 0.0)
    for sweep in range(SWEEPS):
        curled = curl(field)
        real_part = curled[..., 0, :, :, :, :] - kappa * field[..., 1, :, :, :, :]
        imag_part = curled[..., 1, :, :, :, :] + kappa * field[..., 0, :, :, :, :]
        applied = jnp.stack([real_part, imag_part], axis=-5)
        field = field + RELAX * jacobi(rhs - applied, kappa)
        if sweep < SWEEPS - 1:
            field = jnp.where(inside, field, 0.0)
    return field


def encode_weights(group_part, sign_part, rows):
    picked = group_part[None, :] == rows[:, None]
    return jnp.where(picked, sign_part[None, :], 0).astype(jnp.float32).astype(jnp.bfloat16)


def body(primaries, conductivity, group_of, sign_of):
    nt_local = primaries.shape[0]
    depth = primaries.shape[3]
    width_x = primaries.shape[4]
    width_y = primaries.shape[5]
    n_tx = lax.axis_size("tx")
    tx_index = lax.axis_index("tx")
    other = (tx_index + 1) % n_tx
    mine = lax.broadcasted_iota(jnp.int32, (n_tx, nt_local), 0) == tx_index
    own_groups = jnp.sum(jnp.where(mine, group_of.reshape(n_tx, nt_local), 0), axis=0)
    own_signs = jnp.sum(jnp.where(mine, sign_of.reshape(n_tx, nt_local), 0), axis=0)
    rows = jnp.stack([other, tx_index]).astype(jnp.int32)
    weights = encode_weights(own_groups, own_signs, rows)
    partial = lax.dot_general(
        weights, primaries, (((1,), (0,)), ((), ())), preferred_element_type=jnp.float32
    )
    tx_ring = [(i, (i + 1) % n_tx) for i in range(n_tx)]
    got = lax.ppermute(partial[0], "tx", tx_ring)
    sigma_other = lax.ppermute(conductivity, "tx", tx_ring)
    shot_planes = partial.shape[1] * partial.shape[2] * depth
    ext_x = width_x + 2 * SWEEPS
    ext_y = width_y + 2 * SWEEPS
    w = SWEEPS
    x_rounds = list(swap_rounds("xb"))
    y_rounds = list(swap_rounds("yb"))
    n_x = len(x_rounds)
    n_y = len(y_rounds)
    flags = jnp.stack(
        [(tx_index == 0).astype(jnp.int32), (lax.axis_index("xb") % 2 == 0).astype(jnp.int32)]
        + [lower.astype(jnp.int32) for _, lower in x_rounds]
        + [lower.astype(jnp.int32) for _, lower in y_rounds]
    )
    pieces = (partial[1], got, conductivity, sigma_other)
    n_planes = shot_planes + 2 * conductivity.shape[0] * conductivity.shape[1]
    vmem = pl.BlockSpec(memory_space=pltpu.VMEM)
    smem = pl.BlockSpec(memory_space=pltpu.SMEM)

    def planes_of(flags_ref, own_ref, got_ref, sigma_ref, other_ref):
        shot = (own_ref[...] + got_ref[...]).reshape(shot_planes, width_x, width_y)
        mine = sigma_ref[...]
        theirs = other_ref[...]
        sigma = jnp.where(
            flags_ref[0] == 1,
            jnp.concatenate([mine, theirs], axis=1),
            jnp.concatenate([theirs, mine], axis=1),
        ).reshape(-1, width_x, width_y)
        return jnp.concatenate([shot, sigma], axis=0)

    row_shot = primaries.shape[1:3] + (depth, 1, width_y)
    payload_planes = n_planes * (w - 1) + shot_planes

    def field0_row(row):
        shot = row[:shot_planes].reshape(row_shot)
        sigma = row[shot_planes:].reshape(-1, depth, 1, width_y)
        rhs = source_term(shot, K_FREQ * (sigma - 1.0))
        return jacobi(rhs, K_FREQ * sigma).reshape(shot_planes, 1, width_y)

    def send_kernel(flags_ref, own_ref, got_ref, sigma_ref, other_ref, *send_refs):
        cells = planes_of(flags_ref, own_ref, got_ref, sigma_ref, other_ref)

        def payload(inner_rows, outer_row):
            parts = [cells[:, r:r + 1] for r in inner_rows]
            parts.append(field0_row(cells[:, outer_row:outer_row + 1]))
            return jnp.concatenate(parts, axis=0)

        head = payload(range(0, w - 1), w - 1)
        tail = payload(range(width_x - w + 1, width_x), width_x - w)
        for k in range(n_x):
            send_refs[k][...] = jnp.where(flags_ref[2 + k] == 1, tail, head)

    x_sends = pl.pallas_call(
        send_kernel,
        out_shape=[jax.ShapeDtypeStruct((payload_planes, 1, width_y), jnp.float32)] * n_x,
        in_specs=[smem] + [vmem] * 4,
        out_specs=[vmem] * n_x,
    )(flags, *pieces)
    x_gots = [
        row_major(lax.ppermute(row_major(send), "xb", pairs))
        for send, (pairs, _) in zip(x_sends, x_rounds)
    ]
    face_shape = (w, n_planes * ext_x)

    def decode(payload, outer_first):
        inner = [payload[k * n_planes:(k + 1) * n_planes] for k in range(w - 1)]
        field0 = payload[n_planes * (w - 1):]
        filler = jnp.zeros((n_planes - shot_planes, 1, width_y), payload.dtype)
        outer = jnp.concatenate([field0, filler], axis=0)
        return jnp.concatenate([outer] + inner if outer_first else inner + [outer], axis=1)

    def x_cells(flags_ref, own_ref, got_ref, sigma_ref, other_ref, got_refs):
        if n_x == 1:
            low = high = got_refs[0][...]
        else:
            even = flags_ref[1] == 1
            high = jnp.where(even, got_refs[0][...], got_refs[1][...])
            low = jnp.where(even, got_refs[1][...], got_refs[0][...])
        low = decode(low, True)
        high = decode(high, False)
        middle = planes_of(flags_ref, own_ref, got_ref, sigma_ref, other_ref)
        return jnp.concatenate([low, middle, high], axis=1)

    def x_kernel(flags_ref, own_ref, got_ref, sigma_ref, other_ref, *refs):
        got_refs = refs[:n_x]
        send_refs = refs[n_x:]
        cells = x_cells(flags_ref, own_ref, got_ref, sigma_ref, other_ref, got_refs)
        columns = cells.reshape(n_planes * ext_x, width_y).T
        head = columns[:w]
        tail = columns[width_y - w:]
        for k in range(n_y):
            send_refs[k][...] = jnp.where(flags_ref[2 + n_x + k] == 1, tail, head)

    y_sends = pl.pallas_call(
        x_kernel,
        out_shape=[jax.ShapeDtypeStruct(face_shape, jnp.float32)] * n_y,
        in_specs=[smem] + [vmem] * (4 + n_x),
        out_specs=[vmem] * n_y,
    )(flags, *pieces, *x_gots)
    y_gots = [
        row_major(lax.ppermute(row_major(send), "yb", pairs))
        for send, (pairs, _) in zip(y_sends, y_rounds)
    ]
    if n_y == 1:
        y_low = y_high = y_gots[0]
    else:
        even_y = lax.axis_index("yb") % 2 == 0
        y_high = jnp.where(even_y, y_gots[0], y_gots[1])
        y_low = jnp.where(even_y, y_gots[1], y_gots[0])
    lanes = 2 * width_y
    gx = lax.axis_index("xb") * width_x - SWEEPS + lax.broadcasted_iota(jnp.int32, (ext_x, lanes), 0)
    lane = lax.broadcasted_iota(jnp.int32, (ext_x, lanes), 1)
    local_y = jnp.where(lane >= lanes - SWEEPS, lane - lanes, lane)
    gy = lax.axis_index("yb") * width_y + local_y
    inside = (gx >= 0) & (gx < width_x * lax.axis_size("xb")) & (gy >= 0) & (gy < width_y * lax.axis_size("yb"))
    inside = inside & (local_y < width_y + SWEEPS)
    shot_shape = primaries.shape[1:3]
    out_shape = shot_shape + (depth, width_x, width_y)

    def unflip(face):
        filler = jnp.zeros((width_y - w, face.shape[1]), face.dtype)
        back = jnp.concatenate([face, filler], axis=0).T.reshape(n_planes, ext_x, width_y)
        return back[:, :, :w]

    def sweeps_kernel(flags_ref, own_ref, got_ref, sigma_ref, other_ref, *refs):
        got_refs = refs[:n_x]
        low_ref, high_ref, inside_ref, out_ref = refs[n_x:]
        cells = x_cells(flags_ref, own_ref, got_ref, sigma_ref, other_ref, got_refs)
        low = unflip(low_ref[...])
        high = low if n_y == 1 else unflip(high_ref[...])
        gap = jnp.zeros((n_planes, ext_x, lanes - width_y - 2 * w), jnp.float32)
        ext = jnp.concatenate([cells, high, gap, low], axis=2)
        shot_ext = ext[:shot_planes].reshape(shot_shape + (depth, ext_x, lanes))
        sigma_ext = ext[shot_planes:].reshape(-1, depth, ext_x, lanes)
        keep = inside_ref[...] > 0.5
        row = lax.broadcasted_iota(jnp.int32, (ext_x, lanes), 0)
        outer = (row == 0) | (row == ext_x - 1)
        field = rolled_sweeps(shot_ext, sigma_ext, keep, outer, ext_x, lanes)
        out_ref[...] = field[..., w:w + width_x, :width_y]

    field = pl.pallas_call(
        sweeps_kernel,
        out_shape=jax.ShapeDtypeStruct(out_shape, jnp.float32),
        in_specs=[smem] + [vmem] * (4 + n_x + 3),
        out_specs=vmem,
    )(flags, *pieces, *x_gots, y_low, y_high, inside.astype(jnp.float32))
    return field[None]


def solution(mesh):
    in_specs = (
        P(("survey", "tx"), None, None, None, "xb", "yb"),
        P("survey", "tx", "xb", "yb"),
        P("survey"),
        P("survey"),
    )
    out_specs = P(("survey", "tx"), None, None, None, "xb", "yb")
    return jax.shard_map(body, mesh=mesh, in_specs=in_specs, out_specs=out_specs, check_vma=False)
```

```python
import jax
import jax.numpy as jnp
from jax import lax
from jax.experimental import pallas as pl
from jax.experimental.pallas import tpu as pltpu
from jax.experimental.layout import Layout, with_layout_constraint
from jax.sharding import PartitionSpec as P

NS_DEV = 1
SWEEPS = 2


K_FREQ = 2.0
RELAX = 0.6


def inner(f):
    return f[..., :-1, :-1, :-1]


def fwd_z(f):
    return f[..., 1:, :-1, :-1] - inner(f)


def fwd_x(f):
    return f[..., :-1, 1:, :-1] - inner(f)


def fwd_y(f):
    return f[..., :-1, :-1, 1:] - inner(f)


def back_z(g):
    return g[..., 1:, 1:, 1:] - g[..., :-1, 1:, 1:]


def back_x(g):
    return g[..., 1:, 1:, 1:] - g[..., 1:, :-1, 1:]


def back_y(g):
    return g[..., 1:, 1:, 1:] - g[..., 1:, 1:, :-1]


def curl_curl(padded):
    e_x = padded[..., 0, :, :, :]
    e_y = padded[..., 1, :, :, :]
    e_z = padded[..., 2, :, :, :]
    h_x = fwd_y(e_z) - fwd_z(e_y)
    h_y = fwd_z(e_x) - fwd_x(e_z)
    h_z = fwd_x(e_y) - fwd_y(e_x)
    c_x = back_y(h_z) - back_z(h_y)
    c_y = back_z(h_x) - back_x(h_z)
    c_z = back_x(h_y) - back_y(h_x)
    return jnp.stack([c_x, c_y, c_z], axis=-4)


def jacobi(resid, kappa):
    denom = 16.0 + kappa * kappa
    real_part = (4.0 * resid[..., 0, :, :, :, :] + kappa * resid[..., 1, :, :, :, :]) / denom
    imag_part = (4.0 * resid[..., 1, :, :, :, :] - kappa * resid[..., 0, :, :, :, :]) / denom
    return jnp.stack([real_part, imag_part], axis=-5)


def source_term(shot, delta):
    return jnp.stack([delta * shot[..., 1, :, :, :, :], -delta * shot[..., 0, :, :, :, :]], axis=-5)


def shrink(f, ring):
    return f[..., ring:f.shape[-2] - ring, ring:f.shape[-1] - ring]


def pad_z(f):
    return jnp.pad(f, [(0, 0)] * (f.ndim - 3) + [(1, 1), (0, 0), (0, 0)])


def swap_rounds(axis):
    count = lax.axis_size(axis)
    even = lax.axis_index(axis) % 2 == 0
    for first in (0, 1):
        pairs = []
        for i in range(first, count - 1, 2):
            pairs += [(i, i + 1), (i + 1, i)]
        if pairs:
            yield pairs, even == (first == 0)


def halo_faces(cells, axis, dim, width):
    count = lax.axis_size(axis)
    size = cells.shape[dim]
    head = lax.slice_in_dim(cells, 0, width, axis=dim)
    tail = lax.slice_in_dim(cells, size - width, size, axis=dim)
    if count == 2:
        got = row_major(lax.ppermute(row_major(jnp.where(lax.axis_index(axis) == 0, tail, head)), axis, [(0, 1), (1, 0)]))
        return got, got
    even = lax.axis_index(axis) % 2 == 0
    from_low = jnp.zeros_like(tail)
    from_high = jnp.zeros_like(head)
    for first in (0, 1):
        pairs = []
        for i in range(first, count - 1, 2):
            pairs += [(i, i + 1), (i + 1, i)]
        lower_is_even = first == 0
        send = row_major(jnp.where(even == lower_is_even, tail, head))
        got = row_major(lax.ppermute(send, axis, pairs))
        from_high = jnp.where(even == lower_is_even, got, from_high)
        from_low = jnp.where(even == lower_is_even, from_low, got)
    return from_low, from_high


def halo(cells, axis, dim, width):
    count = lax.axis_size(axis)
    size = cells.shape[dim]
    head = lax.slice_in_dim(cells, 0, width, axis=dim)
    tail = lax.slice_in_dim(cells, size - width, size, axis=dim)
    even = lax.axis_index(axis) % 2 == 0
    from_low = jnp.zeros_like(tail)
    from_high = jnp.zeros_like(head)
    for first in (0, 1):
        pairs = []
        for i in range(first, count - 1, 2):
            pairs += [(i, i + 1), (i + 1, i)]
        if not pairs:
            continue
        lower_is_even = first == 0
        send = row_major(jnp.where(even == lower_is_even, tail, head))
        got = row_major(lax.ppermute(send, axis, pairs))
        from_high = jnp.where(even == lower_is_even, got, from_high)
        from_low = jnp.where(even == lower_is_even, from_low, got)
    return jnp.concatenate([from_low, cells, from_high], axis=dim)


def row_major(x):
    return with_layout_constraint(x, Layout(major_to_minor=tuple(range(x.ndim))))


def sweep_all(shot_ext, sigma_ext, inside, outer):
    kappa = K_FREQ * sigma_ext
    delta = K_FREQ * (sigma_ext - 1.0)
    rhs = source_term(shot_ext, delta)
    field = jnp.where(inside, jnp.where(outer, shot_ext, jacobi(rhs, kappa)), 0.0)
    for sweep in range(SWEEPS):
        curled = curl_curl(pad_z(field))
        field = shrink(field, 1)
        kappa = shrink(kappa, 1)
        rhs = shrink(rhs, 1)
        inside = shrink(inside, 1)
        real_part = curled[..., 0, :, :, :, :] - kappa * field[..., 1, :, :, :, :]
        imag_part = curled[..., 1, :, :, :, :] + kappa * field[..., 0, :, :, :, :]
        applied = jnp.stack([real_part, imag_part], axis=-5)
        field = field + RELAX * jacobi(rhs - applied, kappa)
        if sweep < SWEEPS - 1:
            field = jnp.where(inside, field, 0.0)
    return field


def rolled_sweeps(shot_ext, sigma_ext, inside, outer, rows, lanes):
    def nxt(f, axis):
        return pltpu.roll(f, (lanes if axis == -1 else rows) - 1, axis=f.ndim + axis)

    def prv(f, axis):
        return pltpu.roll(f, 1, axis=f.ndim + axis)

    def curl(field):
        padded = pad_z(field)
        above = padded[..., 1:, :, :]
        here = padded[..., :-1, :, :]

        def dz(c):
            return above[..., c, :, :, :] - here[..., c, :, :, :]

        def dx(c):
            return nxt(here[..., c, :, :, :], -2) - here[..., c, :, :, :]

        def dy(c):
            return nxt(here[..., c, :, :, :], -1) - here[..., c, :, :, :]

        h_x = dy(2) - dz(1)
        h_y = dz(0) - dx(2)
        h_z = dx(1) - dy(0)

        def bz(g):
            return g[..., 1:, :, :] - g[..., :-1, :, :]

        def bx(g):
            return g[..., 1:, :, :] - prv(g[..., 1:, :, :], -2)

        def by(g):
            return g[..., 1:, :, :] - prv(g[..., 1:, :, :], -1)

        c_x = by(h_z) - bz(h_y)
        c_y = bz(h_x) - bx(h_z)
        c_z = bx(h_y) - by(h_x)
        return jnp.stack([c_x, c_y, c_z], axis=-4)

    kappa = K_FREQ * sigma_ext
    delta = K_FREQ * (sigma_ext - 1.0)
    rhs = source_term(shot_ext, delta)
    field = jnp.where(inside, jnp.where(outer, shot_ext, jacobi(rhs, kappa)), 0.0)
    for sweep in range(SWEEPS):
        curled = curl(field)
        real_part = curled[..., 0, :, :, :, :] - kappa * field[..., 1, :, :, :, :]
        imag_part = curled[..., 1, :, :, :, :] + kappa * field[..., 0, :, :, :, :]
        applied = jnp.stack([real_part, imag_part], axis=-5)
        field = field + RELAX * jacobi(rhs - applied, kappa)
        if sweep < SWEEPS - 1:
            field = jnp.where(inside, field, 0.0)
    return field


def encode_weights(group_part, sign_part, rows):
    picked = group_part[None, :] == rows[:, None]
    return jnp.where(picked, sign_part[None, :], 0).astype(jnp.float32).astype(jnp.bfloat16)


def body(primaries, conductivity, group_of, sign_of):
    nt_local = primaries.shape[0]
    depth = primaries.shape[3]
    width_x = primaries.shape[4]
    width_y = primaries.shape[5]
    n_tx = lax.axis_size("tx")
    tx_index = lax.axis_index("tx")
    other = (tx_index + 1) % n_tx
    mine = lax.broadcasted_iota(jnp.int32, (n_tx, nt_local), 0) == tx_index
    own_groups = jnp.sum(jnp.where(mine, group_of.reshape(n_tx, nt_local), 0), axis=0)
    own_signs = jnp.sum(jnp.where(mine, sign_of.reshape(n_tx, nt_local), 0), axis=0)
    rows = jnp.stack([other, tx_index]).astype(jnp.int32)
    weights = encode_weights(own_groups, own_signs, rows)
    partial = lax.dot_general(
        weights, primaries, (((1,), (0,)), ((), ())), preferred_element_type=jnp.float32
    )
    tx_ring = [(i, (i + 1) % n_tx) for i in range(n_tx)]
    got = lax.ppermute(partial[0], "tx", tx_ring)
    sigma_other = lax.ppermute(conductivity, "tx", tx_ring)
    shot_planes = partial.shape[1] * partial.shape[2] * depth
    ext_x = width_x + 2 * SWEEPS
    ext_y = width_y + 2 * SWEEPS
    w = SWEEPS
    x_rounds = list(swap_rounds("xb"))
    y_rounds = list(swap_rounds("yb"))
    n_x = len(x_rounds)
    n_y = len(y_rounds)
    flags = jnp.stack(
        [(tx_index == 0).astype(jnp.int32), (lax.axis_index("xb") % 2 == 0).astype(jnp.int32)]
        + [lower.astype(jnp.int32) for _, lower in x_rounds]
        + [lower.astype(jnp.int32) for _, lower in y_rounds]
    )
    pieces = (partial[1], got, conductivity, sigma_other)
    n_planes = shot_planes + 2 * conductivity.shape[0] * conductivity.shape[1]
    vmem = pl.BlockSpec(memory_space=pltpu.VMEM)
    smem = pl.BlockSpec(memory_space=pltpu.SMEM)

    def planes_of(flags_ref, own_ref, got_ref, sigma_ref, other_ref):
        shot = (own_ref[...] + got_ref[...]).reshape(shot_planes, width_x, width_y)
        mine = sigma_ref[...]
        theirs = other_ref[...]
        sigma = jnp.where(
            flags_ref[0] == 1,
            jnp.concatenate([mine, theirs], axis=1),
            jnp.concatenate([theirs, mine], axis=1),
        ).reshape(-1, width_x, width_y)
        return jnp.concatenate([shot, sigma], axis=0)

    row_shot = primaries.shape[1:3] + (depth, 1, width_y)
    payload_planes = n_planes * (w - 1) + shot_planes

    def field0_row(row):
        shot = row[:shot_planes].reshape(row_shot)
        sigma = row[shot_planes:].reshape(-1, depth, 1, width_y)
        rhs = source_term(shot, K_FREQ * (sigma - 1.0))
        return jacobi(rhs, K_FREQ * sigma).reshape(shot_planes, 1, width_y)

    def send_kernel(flags_ref, own_ref, got_ref, sigma_ref, other_ref, *send_refs):
        cells = planes_of(flags_ref, own_ref, got_ref, sigma_ref, other_ref)

        def payload(inner_rows, outer_row):
            parts = [cells[:, r:r + 1] for r in inner_rows]
            parts.append(field0_row(cells[:, outer_row:outer_row + 1]))
            return jnp.concatenate(parts, axis=0)

        head = payload(range(0, w - 1), w - 1)
        tail = payload(range(width_x - w + 1, width_x), width_x - w)
        for k in range(n_x):
            send_refs[k][...] = jnp.where(flags_ref[2 + k] == 1, tail, head)

    x_sends = pl.pallas_call(
        send_kernel,
        out_shape=[jax.ShapeDtypeStruct((payload_planes, 1, width_y), jnp.float32)] * n_x,
        in_specs=[smem] + [vmem] * 4,
        out_specs=[vmem] * n_x,
    )(flags, *pieces)
    x_gots = [
        row_major(lax.ppermute(row_major(send), "xb", pairs))
        for send, (pairs, _) in zip(x_sends, x_rounds)
    ]
    face_shape = (w, n_planes * ext_x)

    def decode(payload, outer_first):
        inner = [payload[k * n_planes:(k + 1) * n_planes] for k in range(w - 1)]
        field0 = payload[n_planes * (w - 1):]
        filler = jnp.zeros((n_planes - shot_planes, 1, width_y), payload.dtype)
        outer = jnp.concatenate([field0, filler], axis=0)
        return jnp.concatenate([outer] + inner if outer_first else inner + [outer], axis=1)

    def x_cells(flags_ref, own_ref, got_ref, sigma_ref, other_ref, got_refs):
        if n_x == 1:
            low = high = got_refs[0][...]
        else:
            even = flags_ref[1] == 1
            high = jnp.where(even, got_refs[0][...], got_refs[1][...])
            low = jnp.where(even, got_refs[1][...], got_refs[0][...])
        low = decode(low, True)
        high = decode(high, False)
        middle = planes_of(flags_ref, own_ref, got_ref, sigma_ref, other_ref)
        return jnp.concatenate([low, middle, high], axis=1)

    def x_kernel(flags_ref, own_ref, got_ref, sigma_ref, other_ref, *refs):
        got_refs = refs[:n_x]
        send_refs = refs[n_x:]
        cells = x_cells(flags_ref, own_ref, got_ref, sigma_ref, other_ref, got_refs)
        columns = cells.reshape(n_planes * ext_x, width_y).T
        head = columns[:w]
        tail = columns[width_y - w:]
        for k in range(n_y):
            send_refs[k][...] = jnp.where(flags_ref[2 + n_x + k] == 1, tail, head)

    y_sends = pl.pallas_call(
        x_kernel,
        out_shape=[jax.ShapeDtypeStruct(face_shape, jnp.float32)] * n_y,
        in_specs=[smem] + [vmem] * (4 + n_x),
        out_specs=[vmem] * n_y,
    )(flags, *pieces, *x_gots)
    y_gots = [
        row_major(lax.ppermute(row_major(send), "yb", pairs))
        for send, (pairs, _) in zip(y_sends, y_rounds)
    ]
    if n_y == 1:
        y_low = y_high = y_gots[0]
    else:
        even_y = lax.axis_index("yb") % 2 == 0
        y_high = jnp.where(even_y, y_gots[0], y_gots[1])
        y_low = jnp.where(even_y, y_gots[1], y_gots[0])
    lanes = 2 * width_y
    gx = lax.axis_index("xb") * width_x - SWEEPS + lax.broadcasted_iota(jnp.int32, (ext_x, lanes), 0)
    lane = lax.broadcasted_iota(jnp.int32, (ext_x, lanes), 1)
    local_y = jnp.where(lane >= lanes - SWEEPS, lane - lanes, lane)
    gy = lax.axis_index("yb") * width_y + local_y
    inside = (gx >= 0) & (gx < width_x * lax.axis_size("xb")) & (gy >= 0) & (gy < width_y * lax.axis_size("yb"))
    inside = inside & (local_y < width_y + SWEEPS)
    shot_shape = primaries.shape[1:3]
    out_shape = shot_shape + (depth, width_x, width_y)

    def unflip(face):
        filler = jnp.zeros((width_y - w, face.shape[1]), face.dtype)
        back = jnp.concatenate([face, filler], axis=0).T.reshape(n_planes, ext_x, width_y)
        return back[:, :, :w]

    def sweeps_kernel(flags_ref, own_ref, got_ref, sigma_ref, other_ref, *refs):
        got_refs = refs[:n_x]
        low_ref, high_ref, inside_ref, out_ref = refs[n_x:]
        cells = x_cells(flags_ref, own_ref, got_ref, sigma_ref, other_ref, got_refs)
        gap = jnp.zeros((lanes - width_y - 2 * w, n_planes * ext_x), jnp.float32)
        upper = jnp.concatenate([high_ref[...], gap, low_ref[...]], axis=0)
        upper = upper.T.reshape(n_planes, ext_x, lanes - width_y)
        ext = jnp.concatenate([cells, upper], axis=2)
        shot_ext = ext[:shot_planes].reshape(shot_shape + (depth, ext_x, lanes))
        sigma_ext = ext[shot_planes:].reshape(-1, depth, ext_x, lanes)
        keep = inside_ref[...] > 0.5
        row = lax.broadcasted_iota(jnp.int32, (ext_x, lanes), 0)
        outer = (row == 0) | (row == ext_x - 1)
        field = rolled_sweeps(shot_ext, sigma_ext, keep, outer, ext_x, lanes)
        out_ref[...] = field[..., w:w + width_x, :width_y]

    field = pl.pallas_call(
        sweeps_kernel,
        out_shape=jax.ShapeDtypeStruct(out_shape, jnp.float32),
        in_specs=[smem] + [vmem] * (4 + n_x + 3),
        out_specs=vmem,
    )(flags, *pieces, *x_gots, y_low, y_high, inside.astype(jnp.float32))
    return field[None]


def solution(mesh):
    in_specs = (
        P(("survey", "tx"), None, None, None, "xb", "yb"),
        P("survey", "tx", "xb", "yb"),
        P("survey"),
        P("survey"),
    )
    out_specs = P(("survey", "tx"), None, None, None, "xb", "yb")
    return jax.shard_map(body, mesh=mesh, in_specs=in_specs, out_specs=out_specs, check_vma=False)
```

```python
import jax
import jax.numpy as jnp
from jax import lax
from jax.experimental import pallas as pl
from jax.experimental.pallas import tpu as pltpu
from jax.experimental.layout import Layout, with_layout_constraint
from jax.sharding import PartitionSpec as P

NS_DEV = 1
SWEEPS = 2


K_FREQ = 2.0
RELAX = 0.6


def inner(f):
    return f[..., :-1, :-1, :-1]


def fwd_z(f):
    return f[..., 1:, :-1, :-1] - inner(f)


def fwd_x(f):
    return f[..., :-1, 1:, :-1] - inner(f)


def fwd_y(f):
    return f[..., :-1, :-1, 1:] - inner(f)


def back_z(g):
    return g[..., 1:, 1:, 1:] - g[..., :-1, 1:, 1:]


def back_x(g):
    return g[..., 1:, 1:, 1:] - g[..., 1:, :-1, 1:]


def back_y(g):
    return g[..., 1:, 1:, 1:] - g[..., 1:, 1:, :-1]


def curl_curl(padded):
    e_x = padded[..., 0, :, :, :]
    e_y = padded[..., 1, :, :, :]
    e_z = padded[..., 2, :, :, :]
    h_x = fwd_y(e_z) - fwd_z(e_y)
    h_y = fwd_z(e_x) - fwd_x(e_z)
    h_z = fwd_x(e_y) - fwd_y(e_x)
    c_x = back_y(h_z) - back_z(h_y)
    c_y = back_z(h_x) - back_x(h_z)
    c_z = back_x(h_y) - back_y(h_x)
    return jnp.stack([c_x, c_y, c_z], axis=-4)


def jacobi(resid, kappa):
    denom = 16.0 + kappa * kappa
    real_part = (4.0 * resid[..., 0, :, :, :, :] + kappa * resid[..., 1, :, :, :, :]) / denom
    imag_part = (4.0 * resid[..., 1, :, :, :, :] - kappa * resid[..., 0, :, :, :, :]) / denom
    return jnp.stack([real_part, imag_part], axis=-5)


def source_term(shot, delta):
    return jnp.stack([delta * shot[..., 1, :, :, :, :], -delta * shot[..., 0, :, :, :, :]], axis=-5)


def shrink(f, ring):
    return f[..., ring:f.shape[-2] - ring, ring:f.shape[-1] - ring]


def pad_z(f):
    return jnp.pad(f, [(0, 0)] * (f.ndim - 3) + [(1, 1), (0, 0), (0, 0)])


def swap_rounds(axis):
    count = lax.axis_size(axis)
    even = lax.axis_index(axis) % 2 == 0
    for first in (0, 1):
        pairs = []
        for i in range(first, count - 1, 2):
            pairs += [(i, i + 1), (i + 1, i)]
        if pairs:
            yield pairs, even == (first == 0)


def halo_faces(cells, axis, dim, width):
    count = lax.axis_size(axis)
    size = cells.shape[dim]
    head = lax.slice_in_dim(cells, 0, width, axis=dim)
    tail = lax.slice_in_dim(cells, size - width, size, axis=dim)
    if count == 2:
        got = row_major(lax.ppermute(row_major(jnp.where(lax.axis_index(axis) == 0, tail, head)), axis, [(0, 1), (1, 0)]))
        return got, got
    even = lax.axis_index(axis) % 2 == 0
    from_low = jnp.zeros_like(tail)
    from_high = jnp.zeros_like(head)
    for first in (0, 1):
        pairs = []
        for i in range(first, count - 1, 2):
            pairs += [(i, i + 1), (i + 1, i)]
        lower_is_even = first == 0
        send = row_major(jnp.where(even == lower_is_even, tail, head))
        got = row_major(lax.ppermute(send, axis, pairs))
        from_high = jnp.where(even == lower_is_even, got, from_high)
        from_low = jnp.where(even == lower_is_even, from_low, got)
    return from_low, from_high


def halo(cells, axis, dim, width):
    count = lax.axis_size(axis)
    size = cells.shape[dim]
    head = lax.slice_in_dim(cells, 0, width, axis=dim)
    tail = lax.slice_in_dim(cells, size - width, size, axis=dim)
    even = lax.axis_index(axis) % 2 == 0
    from_low = jnp.zeros_like(tail)
    from_high = jnp.zeros_like(head)
    for first in (0, 1):
        pairs = []
        for i in range(first, count - 1, 2):
            pairs += [(i, i + 1), (i + 1, i)]
        if not pairs:
            continue
        lower_is_even = first == 0
        send = row_major(jnp.where(even == lower_is_even, tail, head))
        got = row_major(lax.ppermute(send, axis, pairs))
        from_high = jnp.where(even == lower_is_even, got, from_high)
        from_low = jnp.where(even == lower_is_even, from_low, got)
    return jnp.concatenate([from_low, cells, from_high], axis=dim)


def row_major(x):
    return with_layout_constraint(x, Layout(major_to_minor=tuple(range(x.ndim))))


def sweep_all(shot_ext, sigma_ext, inside, outer):
    kappa = K_FREQ * sigma_ext
    delta = K_FREQ * (sigma_ext - 1.0)
    rhs = source_term(shot_ext, delta)
    field = jnp.where(inside, jnp.where(outer, shot_ext, jacobi(rhs, kappa)), 0.0)
    for sweep in range(SWEEPS):
        curled = curl_curl(pad_z(field))
        field = shrink(field, 1)
        kappa = shrink(kappa, 1)
        rhs = shrink(rhs, 1)
        inside = shrink(inside, 1)
        real_part = curled[..., 0, :, :, :, :] - kappa * field[..., 1, :, :, :, :]
        imag_part = curled[..., 1, :, :, :, :] + kappa * field[..., 0, :, :, :, :]
        applied = jnp.stack([real_part, imag_part], axis=-5)
        field = field + RELAX * jacobi(rhs - applied, kappa)
        if sweep < SWEEPS - 1:
            field = jnp.where(inside, field, 0.0)
    return field


def rolled_sweeps(shot_ext, sigma_ext, inside, outer, rows, lanes):
    def nxt(f, axis):
        return pltpu.roll(f, (lanes if axis == -1 else rows) - 1, axis=f.ndim + axis)

    def prv(f, axis):
        return pltpu.roll(f, 1, axis=f.ndim + axis)

    def curl(field):
        def comp(c):
            return field[..., c, :, :, :]

        def dz(c):
            e = comp(c)
            return jnp.concatenate([e[..., 1:, :, :] - e[..., :-1, :, :], 0.0 - e[..., -1:, :, :]], axis=-3)

        def dx(c):
            return nxt(comp(c), -2) - comp(c)

        def dy(c):
            return nxt(comp(c), -1) - comp(c)

        h_x = dy(2) - dz(1)
        h_y = dz(0) - dx(2)
        h_z = dx(1) - dy(0)
        below_x = 0.0 - comp(1)[..., :1, :, :]
        below_y = comp(0)[..., :1, :, :] - 0.0

        def bz(g, below):
            return jnp.concatenate([g[..., :1, :, :] - below, g[..., 1:, :, :] - g[..., :-1, :, :]], axis=-3)

        def bx(g):
            return g - prv(g, -2)

        def by(g):
            return g - prv(g, -1)

        c_x = by(h_z) - bz(h_y, below_y)
        c_y = bz(h_x, below_x) - bx(h_z)
        c_z = bx(h_y) - by(h_x)
        return jnp.stack([c_x, c_y, c_z], axis=-4)

    kappa = K_FREQ * sigma_ext
    delta = K_FREQ * (sigma_ext - 1.0)
    rhs = source_term(shot_ext, delta)
    field = jnp.where(inside, jnp.where(outer, shot_ext, jacobi(rhs, kappa)), 0.0)
    for sweep in range(SWEEPS):
        curled = curl(field)
        real_part = curled[..., 0, :, :, :, :] - kappa * field[..., 1, :, :, :, :]
        imag_part = curled[..., 1, :, :, :, :] + kappa * field[..., 0, :, :, :, :]
        applied = jnp.stack([real_part, imag_part], axis=-5)
        field = field + RELAX * jacobi(rhs - applied, kappa)
        if sweep < SWEEPS - 1:
            field = jnp.where(inside, field, 0.0)
    return field


def encode_weights(group_part, sign_part, rows):
    picked = group_part[None, :] == rows[:, None]
    return jnp.where(picked, sign_part[None, :], 0).astype(jnp.float32).astype(jnp.bfloat16)


def body(primaries, conductivity, group_of, sign_of):
    nt_local = primaries.shape[0]
    depth = primaries.shape[3]
    width_x = primaries.shape[4]
    width_y = primaries.shape[5]
    n_tx = lax.axis_size("tx")
    tx_index = lax.axis_index("tx")
    other = (tx_index + 1) % n_tx
    mine = lax.broadcasted_iota(jnp.int32, (n_tx, nt_local), 0) == tx_index
    own_groups = jnp.sum(jnp.where(mine, group_of.reshape(n_tx, nt_local), 0), axis=0)
    own_signs = jnp.sum(jnp.where(mine, sign_of.reshape(n_tx, nt_local), 0), axis=0)
    rows = jnp.stack([other, tx_index]).astype(jnp.int32)
    weights = encode_weights(own_groups, own_signs, rows)
    partial = lax.dot_general(
        weights, primaries, (((1,), (0,)), ((), ())), preferred_element_type=jnp.float32
    )
    tx_ring = [(i, (i + 1) % n_tx) for i in range(n_tx)]
    got = lax.ppermute(partial[0], "tx", tx_ring)
    sigma_other = lax.ppermute(conductivity, "tx", tx_ring)
    shot_planes = partial.shape[1] * partial.shape[2] * depth
    ext_x = width_x + 2 * SWEEPS
    ext_y = width_y + 2 * SWEEPS
    w = SWEEPS
    x_rounds = list(swap_rounds("xb"))
    y_rounds = list(swap_rounds("yb"))
    n_x = len(x_rounds)
    n_y = len(y_rounds)
    flags = jnp.stack(
        [(tx_index == 0).astype(jnp.int32), (lax.axis_index("xb") % 2 == 0).astype(jnp.int32)]
        + [lower.astype(jnp.int32) for _, lower in x_rounds]
        + [lower.astype(jnp.int32) for _, lower in y_rounds]
    )
    pieces = (partial[1], got, conductivity, sigma_other)
    n_planes = shot_planes + 2 * conductivity.shape[0] * conductivity.shape[1]
    vmem = pl.BlockSpec(memory_space=pltpu.VMEM)
    smem = pl.BlockSpec(memory_space=pltpu.SMEM)

    def planes_of(flags_ref, own_ref, got_ref, sigma_ref, other_ref):
        shot = (own_ref[...] + got_ref[...]).reshape(shot_planes, width_x, width_y)
        mine = sigma_ref[...]
        theirs = other_ref[...]
        sigma = jnp.where(
            flags_ref[0] == 1,
            jnp.concatenate([mine, theirs], axis=1),
            jnp.concatenate([theirs, mine], axis=1),
        ).reshape(-1, width_x, width_y)
        return jnp.concatenate([shot, sigma], axis=0)

    row_shot = primaries.shape[1:3] + (depth, 1, width_y)
    payload_planes = n_planes * (w - 1) + shot_planes

    def field0_row(row):
        shot = row[:shot_planes].reshape(row_shot)
        sigma = row[shot_planes:].reshape(-1, depth, 1, width_y)
        rhs = source_term(shot, K_FREQ * (sigma - 1.0))
        return jacobi(rhs, K_FREQ * sigma).reshape(shot_planes, 1, width_y)

    def send_kernel(flags_ref, own_ref, got_ref, sigma_ref, other_ref, *send_refs):
        cells = planes_of(flags_ref, own_ref, got_ref, sigma_ref, other_ref)

        def payload(inner_rows, outer_row):
            parts = [cells[:, r:r + 1] for r in inner_rows]
            parts.append(field0_row(cells[:, outer_row:outer_row + 1]))
            return jnp.concatenate(parts, axis=0)

        head = payload(range(0, w - 1), w - 1)
        tail = payload(range(width_x - w + 1, width_x), width_x - w)
        for k in range(n_x):
            send_refs[k][...] = jnp.where(flags_ref[2 + k] == 1, tail, head)

    x_sends = pl.pallas_call(
        send_kernel,
        out_shape=[jax.ShapeDtypeStruct((payload_planes, 1, width_y), jnp.float32)] * n_x,
        in_specs=[smem] + [vmem] * 4,
        out_specs=[vmem] * n_x,
    )(flags, *pieces)
    x_gots = [
        row_major(lax.ppermute(row_major(send), "xb", pairs))
        for send, (pairs, _) in zip(x_sends, x_rounds)
    ]
    face_shape = (w, n_planes * ext_x)

    def decode(payload, outer_first):
        inner = [payload[k * n_planes:(k + 1) * n_planes] for k in range(w - 1)]
        field0 = payload[n_planes * (w - 1):]
        filler = jnp.zeros((n_planes - shot_planes, 1, width_y), payload.dtype)
        outer = jnp.concatenate([field0, filler], axis=0)
        return jnp.concatenate([outer] + inner if outer_first else inner + [outer], axis=1)

    def x_cells(flags_ref, own_ref, got_ref, sigma_ref, other_ref, got_refs):
        if n_x == 1:
            low = high = got_refs[0][...]
        else:
            even = flags_ref[1] == 1
            high = jnp.where(even, got_refs[0][...], got_refs[1][...])
            low = jnp.where(even, got_refs[1][...], got_refs[0][...])
        low = decode(low, True)
        high = decode(high, False)
        middle = planes_of(flags_ref, own_ref, got_ref, sigma_ref, other_ref)
        return jnp.concatenate([low, middle, high], axis=1)

    def x_kernel(flags_ref, own_ref, got_ref, sigma_ref, other_ref, *refs):
        got_refs = refs[:n_x]
        send_refs = refs[n_x:]
        cells = x_cells(flags_ref, own_ref, got_ref, sigma_ref, other_ref, got_refs)
        columns = cells.reshape(n_planes * ext_x, width_y).T
        head = columns[:w]
        tail = columns[width_y - w:]
        for k in range(n_y):
            send_refs[k][...] = jnp.where(flags_ref[2 + n_x + k] == 1, tail, head)

    y_sends = pl.pallas_call(
        x_kernel,
        out_shape=[jax.ShapeDtypeStruct(face_shape, jnp.float32)] * n_y,
        in_specs=[smem] + [vmem] * (4 + n_x),
        out_specs=[vmem] * n_y,
    )(flags, *pieces, *x_gots)
    y_gots = [
        row_major(lax.ppermute(row_major(send), "yb", pairs))
        for send, (pairs, _) in zip(y_sends, y_rounds)
    ]
    if n_y == 1:
        y_low = y_high = y_gots[0]
    else:
        even_y = lax.axis_index("yb") % 2 == 0
        y_high = jnp.where(even_y, y_gots[0], y_gots[1])
        y_low = jnp.where(even_y, y_gots[1], y_gots[0])
    lanes = 2 * width_y
    gx = lax.axis_index("xb") * width_x - SWEEPS + lax.broadcasted_iota(jnp.int32, (ext_x, lanes), 0)
    lane = lax.broadcasted_iota(jnp.int32, (ext_x, lanes), 1)
    local_y = jnp.where(lane >= lanes - SWEEPS, lane - lanes, lane)
    gy = lax.axis_index("yb") * width_y + local_y
    inside = (gx >= 0) & (gx < width_x * lax.axis_size("xb")) & (gy >= 0) & (gy < width_y * lax.axis_size("yb"))
    inside = inside & (local_y < width_y + SWEEPS)
    shot_shape = primaries.shape[1:3]
    out_shape = shot_shape + (depth, width_x, width_y)

    def unflip(face):
        filler = jnp.zeros((width_y - w, face.shape[1]), face.dtype)
        back = jnp.concatenate([face, filler], axis=0).T.reshape(n_planes, ext_x, width_y)
        return back[:, :, :w]

    def sweeps_kernel(flags_ref, own_ref, got_ref, sigma_ref, other_ref, *refs):
        got_refs = refs[:n_x]
        low_ref, high_ref, inside_ref, out_ref = refs[n_x:]
        cells = x_cells(flags_ref, own_ref, got_ref, sigma_ref, other_ref, got_refs)
        gap = jnp.zeros((lanes - width_y - 2 * w, n_planes * ext_x), jnp.float32)
        upper = jnp.concatenate([high_ref[...], gap, low_ref[...]], axis=0)
        upper = upper.T.reshape(n_planes, ext_x, lanes - width_y)
        ext = jnp.concatenate([cells, upper], axis=2)
        shot_ext = ext[:shot_planes].reshape(shot_shape + (depth, ext_x, lanes))
        sigma_ext = ext[shot_planes:].reshape(-1, depth, ext_x, lanes)
        keep = inside_ref[...] > 0.5
        row = lax.broadcasted_iota(jnp.int32, (ext_x, lanes), 0)
        outer = (row == 0) | (row == ext_x - 1)
        field = rolled_sweeps(shot_ext, sigma_ext, keep, outer, ext_x, lanes)
        out_ref[...] = field[..., w:w + width_x, :width_y]

    field = pl.pallas_call(
        sweeps_kernel,
        out_shape=jax.ShapeDtypeStruct(out_shape, jnp.float32),
        in_specs=[smem] + [vmem] * (4 + n_x + 3),
        out_specs=vmem,
    )(flags, *pieces, *x_gots, y_low, y_high, inside.astype(jnp.float32))
    return field[None]


def solution(mesh):
    in_specs = (
        P(("survey", "tx"), None, None, None, "xb", "yb"),
        P("survey", "tx", "xb", "yb"),
        P("survey"),
        P("survey"),
    )
    out_specs = P(("survey", "tx"), None, None, None, "xb", "yb")
    return jax.shard_map(body, mesh=mesh, in_specs=in_specs, out_specs=out_specs, check_vma=False)
```

```python
import jax
import jax.numpy as jnp
from jax import lax
from jax.experimental import pallas as pl
from jax.experimental.pallas import tpu as pltpu
from jax.experimental.layout import Layout, with_layout_constraint
from jax.sharding import PartitionSpec as P

NS_DEV = 1
SWEEPS = 2


K_FREQ = 2.0
RELAX = 0.6


def inner(f):
    return f[..., :-1, :-1, :-1]


def fwd_z(f):
    return f[..., 1:, :-1, :-1] - inner(f)


def fwd_x(f):
    return f[..., :-1, 1:, :-1] - inner(f)


def fwd_y(f):
    return f[..., :-1, :-1, 1:] - inner(f)


def back_z(g):
    return g[..., 1:, 1:, 1:] - g[..., :-1, 1:, 1:]


def back_x(g):
    return g[..., 1:, 1:, 1:] - g[..., 1:, :-1, 1:]


def back_y(g):
    return g[..., 1:, 1:, 1:] - g[..., 1:, 1:, :-1]


def curl_curl(padded):
    e_x = padded[..., 0, :, :, :]
    e_y = padded[..., 1, :, :, :]
    e_z = padded[..., 2, :, :, :]
    h_x = fwd_y(e_z) - fwd_z(e_y)
    h_y = fwd_z(e_x) - fwd_x(e_z)
    h_z = fwd_x(e_y) - fwd_y(e_x)
    c_x = back_y(h_z) - back_z(h_y)
    c_y = back_z(h_x) - back_x(h_z)
    c_z = back_x(h_y) - back_y(h_x)
    return jnp.stack([c_x, c_y, c_z], axis=-4)


def jacobi(resid, kappa):
    denom = 16.0 + kappa * kappa
    real_part = (4.0 * resid[..., 0, :, :, :, :] + kappa * resid[..., 1, :, :, :, :]) / denom
    imag_part = (4.0 * resid[..., 1, :, :, :, :] - kappa * resid[..., 0, :, :, :, :]) / denom
    return jnp.stack([real_part, imag_part], axis=-5)


def source_term(shot, delta):
    return jnp.stack([delta * shot[..., 1, :, :, :, :], -delta * shot[..., 0, :, :, :, :]], axis=-5)


def shrink(f, ring):
    return f[..., ring:f.shape[-2] - ring, ring:f.shape[-1] - ring]


def pad_z(f):
    return jnp.pad(f, [(0, 0)] * (f.ndim - 3) + [(1, 1), (0, 0), (0, 0)])


def swap_rounds(axis):
    count = lax.axis_size(axis)
    even = lax.axis_index(axis) % 2 == 0
    for first in (0, 1):
        pairs = []
        for i in range(first, count - 1, 2):
            pairs += [(i, i + 1), (i + 1, i)]
        if pairs:
            yield pairs, even == (first == 0)


def halo_faces(cells, axis, dim, width):
    count = lax.axis_size(axis)
    size = cells.shape[dim]
    head = lax.slice_in_dim(cells, 0, width, axis=dim)
    tail = lax.slice_in_dim(cells, size - width, size, axis=dim)
    if count == 2:
        got = row_major(lax.ppermute(row_major(jnp.where(lax.axis_index(axis) == 0, tail, head)), axis, [(0, 1), (1, 0)]))
        return got, got
    even = lax.axis_index(axis) % 2 == 0
    from_low = jnp.zeros_like(tail)
    from_high = jnp.zeros_like(head)
    for first in (0, 1):
        pairs = []
        for i in range(first, count - 1, 2):
            pairs += [(i, i + 1), (i + 1, i)]
        lower_is_even = first == 0
        send = row_major(jnp.where(even == lower_is_even, tail, head))
        got = row_major(lax.ppermute(send, axis, pairs))
        from_high = jnp.where(even == lower_is_even, got, from_high)
        from_low = jnp.where(even == lower_is_even, from_low, got)
    return from_low, from_high


def halo(cells, axis, dim, width):
    count = lax.axis_size(axis)
    size = cells.shape[dim]
    head = lax.slice_in_dim(cells, 0, width, axis=dim)
    tail = lax.slice_in_dim(cells, size - width, size, axis=dim)
    even = lax.axis_index(axis) % 2 == 0
    from_low = jnp.zeros_like(tail)
    from_high = jnp.zeros_like(head)
    for first in (0, 1):
        pairs = []
        for i in range(first, count - 1, 2):
            pairs += [(i, i + 1), (i + 1, i)]
        if not pairs:
            continue
        lower_is_even = first == 0
        send = row_major(jnp.where(even == lower_is_even, tail, head))
        got = row_major(lax.ppermute(send, axis, pairs))
        from_high = jnp.where(even == lower_is_even, got, from_high)
        from_low = jnp.where(even == lower_is_even, from_low, got)
    return jnp.concatenate([from_low, cells, from_high], axis=dim)


def row_major(x):
    return with_layout_constraint(x, Layout(major_to_minor=tuple(range(x.ndim))))


def sweep_all(shot_ext, sigma_ext, inside, outer):
    kappa = K_FREQ * sigma_ext
    delta = K_FREQ * (sigma_ext - 1.0)
    rhs = source_term(shot_ext, delta)
    field = jnp.where(inside, jnp.where(outer, shot_ext, jacobi(rhs, kappa)), 0.0)
    for sweep in range(SWEEPS):
        curled = curl_curl(pad_z(field))
        field = shrink(field, 1)
        kappa = shrink(kappa, 1)
        rhs = shrink(rhs, 1)
        inside = shrink(inside, 1)
        real_part = curled[..., 0, :, :, :, :] - kappa * field[..., 1, :, :, :, :]
        imag_part = curled[..., 1, :, :, :, :] + kappa * field[..., 0, :, :, :, :]
        applied = jnp.stack([real_part, imag_part], axis=-5)
        field = field + RELAX * jacobi(rhs - applied, kappa)
        if sweep < SWEEPS - 1:
            field = jnp.where(inside, field, 0.0)
    return field


def rolled_sweeps(shot_ext, sigma_ext, inside, outer, rows, lanes):
    def nxt(f, axis):
        return pltpu.roll(f, (lanes if axis == -1 else rows) - 1, axis=f.ndim + axis)

    def prv(f, axis):
        return pltpu.roll(f, 1, axis=f.ndim + axis)

    def curl(field):
        padded = pad_z(field)
        above = padded[..., 1:, :, :]
        here = padded[..., :-1, :, :]

        def dz(c):
            return above[..., c, :, :, :] - here[..., c, :, :, :]

        def dx(c):
            return nxt(here[..., c, :, :, :], -2) - here[..., c, :, :, :]

        def dy(c):
            return nxt(here[..., c, :, :, :], -1) - here[..., c, :, :, :]

        h_x = dy(2) - dz(1)
        h_y = dz(0) - dx(2)
        h_z = dx(1) - dy(0)

        def bz(g):
            return g[..., 1:, :, :] - g[..., :-1, :, :]

        def bx(g):
            return g[..., 1:, :, :] - prv(g[..., 1:, :, :], -2)

        def by(g):
            return g[..., 1:, :, :] - prv(g[..., 1:, :, :], -1)

        c_x = by(h_z) - bz(h_y)
        c_y = bz(h_x) - bx(h_z)
        c_z = bx(h_y) - by(h_x)
        return jnp.stack([c_x, c_y, c_z], axis=-4)

    kappa = K_FREQ * sigma_ext
    delta = K_FREQ * (sigma_ext - 1.0)
    inverse = 1.0 / (16.0 + kappa * kappa)

    def jac(resid):
        real_part = (4.0 * resid[..., 0, :, :, :, :] + kappa * resid[..., 1, :, :, :, :]) * inverse
        imag_part = (4.0 * resid[..., 1, :, :, :, :] - kappa * resid[..., 0, :, :, :, :]) * inverse
        return jnp.stack([real_part, imag_part], axis=-5)

    rhs = source_term(shot_ext, delta)
    field = jnp.where(inside, jnp.where(outer, shot_ext, jac(rhs)), 0.0)
    for sweep in range(SWEEPS):
        curled = curl(field)
        real_part = curled[..., 0, :, :, :, :] - kappa * field[..., 1, :, :, :, :]
        imag_part = curled[..., 1, :, :, :, :] + kappa * field[..., 0, :, :, :, :]
        applied = jnp.stack([real_part, imag_part], axis=-5)
        field = field + RELAX * jac(rhs - applied)
        if sweep < SWEEPS - 1:
            field = jnp.where(inside, field, 0.0)
    return field


def encode_weights(group_part, sign_part, rows):
    picked = group_part[None, :] == rows[:, None]
    return jnp.where(picked, sign_part[None, :], 0).astype(jnp.float32).astype(jnp.bfloat16)


def body(primaries, conductivity, group_of, sign_of):
    nt_local = primaries.shape[0]
    depth = primaries.shape[3]
    width_x = primaries.shape[4]
    width_y = primaries.shape[5]
    n_tx = lax.axis_size("tx")
    tx_index = lax.axis_index("tx")
    other = (tx_index + 1) % n_tx
    mine = lax.broadcasted_iota(jnp.int32, (n_tx, nt_local), 0) == tx_index
    own_groups = jnp.sum(jnp.where(mine, group_of.reshape(n_tx, nt_local), 0), axis=0)
    own_signs = jnp.sum(jnp.where(mine, sign_of.reshape(n_tx, nt_local), 0), axis=0)
    rows = jnp.stack([other, tx_index]).astype(jnp.int32)
    weights = encode_weights(own_groups, own_signs, rows)
    partial = lax.dot_general(
        weights, primaries, (((1,), (0,)), ((), ())), preferred_element_type=jnp.float32
    )
    tx_ring = [(i, (i + 1) % n_tx) for i in range(n_tx)]
    got = lax.ppermute(partial[0], "tx", tx_ring)
    sigma_other = lax.ppermute(conductivity, "tx", tx_ring)
    shot_planes = partial.shape[1] * partial.shape[2] * depth
    ext_x = width_x + 2 * SWEEPS
    ext_y = width_y + 2 * SWEEPS
    w = SWEEPS
    x_rounds = list(swap_rounds("xb"))
    y_rounds = list(swap_rounds("yb"))
    n_x = len(x_rounds)
    n_y = len(y_rounds)
    flags = jnp.stack(
        [(tx_index == 0).astype(jnp.int32), (lax.axis_index("xb") % 2 == 0).astype(jnp.int32)]
        + [lower.astype(jnp.int32) for _, lower in x_rounds]
        + [lower.astype(jnp.int32) for _, lower in y_rounds]
    )
    pieces = (partial[1], got, conductivity, sigma_other)
    n_planes = shot_planes + 2 * conductivity.shape[0] * conductivity.shape[1]
    vmem = pl.BlockSpec(memory_space=pltpu.VMEM)
    smem = pl.BlockSpec(memory_space=pltpu.SMEM)

    def planes_of(flags_ref, own_ref, got_ref, sigma_ref, other_ref):
        shot = (own_ref[...] + got_ref[...]).reshape(shot_planes, width_x, width_y)
        mine = sigma_ref[...]
        theirs = other_ref[...]
        sigma = jnp.where(
            flags_ref[0] == 1,
            jnp.concatenate([mine, theirs], axis=1),
            jnp.concatenate([theirs, mine], axis=1),
        ).reshape(-1, width_x, width_y)
        return jnp.concatenate([shot, sigma], axis=0)

    row_shot = primaries.shape[1:3] + (depth, 1, width_y)
    payload_planes = n_planes * (w - 1) + shot_planes

    def field0_row(row):
        shot = row[:shot_planes].reshape(row_shot)
        sigma = row[shot_planes:].reshape(-1, depth, 1, width_y)
        rhs = source_term(shot, K_FREQ * (sigma - 1.0))
        return jacobi(rhs, K_FREQ * sigma).reshape(shot_planes, 1, width_y)

    def send_kernel(flags_ref, own_ref, got_ref, sigma_ref, other_ref, *send_refs):
        cells = planes_of(flags_ref, own_ref, got_ref, sigma_ref, other_ref)

        def payload(inner_rows, outer_row):
            parts = [cells[:, r:r + 1] for r in inner_rows]
            parts.append(field0_row(cells[:, outer_row:outer_row + 1]))
            return jnp.concatenate(parts, axis=0)

        head = payload(range(0, w - 1), w - 1)
        tail = payload(range(width_x - w + 1, width_x), width_x - w)
        for k in range(n_x):
            send_refs[k][...] = jnp.where(flags_ref[2 + k] == 1, tail, head)

    x_sends = pl.pallas_call(
        send_kernel,
        out_shape=[jax.ShapeDtypeStruct((payload_planes, 1, width_y), jnp.float32)] * n_x,
        in_specs=[smem] + [vmem] * 4,
        out_specs=[vmem] * n_x,
    )(flags, *pieces)
    x_gots = [
        row_major(lax.ppermute(row_major(send), "xb", pairs))
        for send, (pairs, _) in zip(x_sends, x_rounds)
    ]
    face_shape = (w, n_planes * ext_x)

    def decode(payload, outer_first):
        inner = [payload[k * n_planes:(k + 1) * n_planes] for k in range(w - 1)]
        field0 = payload[n_planes * (w - 1):]
        filler = jnp.zeros((n_planes - shot_planes, 1, width_y), payload.dtype)
        outer = jnp.concatenate([field0, filler], axis=0)
        return jnp.concatenate([outer] + inner if outer_first else inner + [outer], axis=1)

    def x_cells(flags_ref, own_ref, got_ref, sigma_ref, other_ref, got_refs):
        if n_x == 1:
            low = high = got_refs[0][...]
        else:
            even = flags_ref[1] == 1
            high = jnp.where(even, got_refs[0][...], got_refs[1][...])
            low = jnp.where(even, got_refs[1][...], got_refs[0][...])
        low = decode(low, True)
        high = decode(high, False)
        middle = planes_of(flags_ref, own_ref, got_ref, sigma_ref, other_ref)
        return jnp.concatenate([low, middle, high], axis=1)

    def x_kernel(flags_ref, own_ref, got_ref, sigma_ref, other_ref, *refs):
        got_refs = refs[:n_x]
        send_refs = refs[n_x:]
        cells = x_cells(flags_ref, own_ref, got_ref, sigma_ref, other_ref, got_refs)
        columns = cells.reshape(n_planes * ext_x, width_y).T
        head = columns[:w]
        tail = columns[width_y - w:]
        for k in range(n_y):
            send_refs[k][...] = jnp.where(flags_ref[2 + n_x + k] == 1, tail, head)

    y_sends = pl.pallas_call(
        x_kernel,
        out_shape=[jax.ShapeDtypeStruct(face_shape, jnp.float32)] * n_y,
        in_specs=[smem] + [vmem] * (4 + n_x),
        out_specs=[vmem] * n_y,
    )(flags, *pieces, *x_gots)
    y_gots = [
        row_major(lax.ppermute(row_major(send), "yb", pairs))
        for send, (pairs, _) in zip(y_sends, y_rounds)
    ]
    if n_y == 1:
        y_low = y_high = y_gots[0]
    else:
        even_y = lax.axis_index("yb") % 2 == 0
        y_high = jnp.where(even_y, y_gots[0], y_gots[1])
        y_low = jnp.where(even_y, y_gots[1], y_gots[0])
    lanes = 2 * width_y
    gx = lax.axis_index("xb") * width_x - SWEEPS + lax.broadcasted_iota(jnp.int32, (ext_x, lanes), 0)
    lane = lax.broadcasted_iota(jnp.int32, (ext_x, lanes), 1)
    local_y = jnp.where(lane >= lanes - SWEEPS, lane - lanes, lane)
    gy = lax.axis_index("yb") * width_y + local_y
    inside = (gx >= 0) & (gx < width_x * lax.axis_size("xb")) & (gy >= 0) & (gy < width_y * lax.axis_size("yb"))
    inside = inside & (local_y < width_y + SWEEPS)
    shot_shape = primaries.shape[1:3]
    out_shape = shot_shape + (depth, width_x, width_y)

    def unflip(face):
        filler = jnp.zeros((width_y - w, face.shape[1]), face.dtype)
        back = jnp.concatenate([face, filler], axis=0).T.reshape(n_planes, ext_x, width_y)
        return back[:, :, :w]

    def sweeps_kernel(flags_ref, own_ref, got_ref, sigma_ref, other_ref, *refs):
        got_refs = refs[:n_x]
        low_ref, high_ref, inside_ref, out_ref = refs[n_x:]
        cells = x_cells(flags_ref, own_ref, got_ref, sigma_ref, other_ref, got_refs)
        gap = jnp.zeros((lanes - width_y - 2 * w, n_planes * ext_x), jnp.float32)
        upper = jnp.concatenate([high_ref[...], gap, low_ref[...]], axis=0)
        upper = upper.T.reshape(n_planes, ext_x, lanes - width_y)
        ext = jnp.concatenate([cells, upper], axis=2)
        shot_ext = ext[:shot_planes].reshape(shot_shape + (depth, ext_x, lanes))
        sigma_ext = ext[shot_planes:].reshape(-1, depth, ext_x, lanes)
        keep = inside_ref[...] > 0.5
        row = lax.broadcasted_iota(jnp.int32, (ext_x, lanes), 0)
        outer = (row == 0) | (row == ext_x - 1)
        field = rolled_sweeps(shot_ext, sigma_ext, keep, outer, ext_x, lanes)
        out_ref[...] = field[..., w:w + width_x, :width_y]

    field = pl.pallas_call(
        sweeps_kernel,
        out_shape=jax.ShapeDtypeStruct(out_shape, jnp.float32),
        in_specs=[smem] + [vmem] * (4 + n_x + 3),
        out_specs=vmem,
    )(flags, *pieces, *x_gots, y_low, y_high, inside.astype(jnp.float32))
    return field[None]


def solution(mesh):
    in_specs = (
        P(("survey", "tx"), None, None, None, "xb", "yb"),
        P("survey", "tx", "xb", "yb"),
        P("survey"),
        P("survey"),
    )
    out_specs = P(("survey", "tx"), None, None, None, "xb", "yb")
    return jax.shard_map(body, mesh=mesh, in_specs=in_specs, out_specs=out_specs, check_vma=False)
```

```python
import jax
import jax.numpy as jnp
from jax import lax
from jax.experimental import pallas as pl
from jax.experimental.pallas import tpu as pltpu
from jax.experimental.layout import Layout, with_layout_constraint
from jax.sharding import PartitionSpec as P

NS_DEV = 1
SWEEPS = 2


K_FREQ = 2.0
RELAX = 0.6


def inner(f):
    return f[..., :-1, :-1, :-1]


def fwd_z(f):
    return f[..., 1:, :-1, :-1] - inner(f)


def fwd_x(f):
    return f[..., :-1, 1:, :-1] - inner(f)


def fwd_y(f):
    return f[..., :-1, :-1, 1:] - inner(f)


def back_z(g):
    return g[..., 1:, 1:, 1:] - g[..., :-1, 1:, 1:]


def back_x(g):
    return g[..., 1:, 1:, 1:] - g[..., 1:, :-1, 1:]


def back_y(g):
    return g[..., 1:, 1:, 1:] - g[..., 1:, 1:, :-1]


def curl_curl(padded):
    e_x = padded[..., 0, :, :, :]
    e_y = padded[..., 1, :, :, :]
    e_z = padded[..., 2, :, :, :]
    h_x = fwd_y(e_z) - fwd_z(e_y)
    h_y = fwd_z(e_x) - fwd_x(e_z)
    h_z = fwd_x(e_y) - fwd_y(e_x)
    c_x = back_y(h_z) - back_z(h_y)
    c_y = back_z(h_x) - back_x(h_z)
    c_z = back_x(h_y) - back_y(h_x)
    return jnp.stack([c_x, c_y, c_z], axis=-4)


def jacobi(resid, kappa):
    denom = 16.0 + kappa * kappa
    real_part = (4.0 * resid[..., 0, :, :, :, :] + kappa * resid[..., 1, :, :, :, :]) / denom
    imag_part = (4.0 * resid[..., 1, :, :, :, :] - kappa * resid[..., 0, :, :, :, :]) / denom
    return jnp.stack([real_part, imag_part], axis=-5)


def source_term(shot, delta):
    return jnp.stack([delta * shot[..., 1, :, :, :, :], -delta * shot[..., 0, :, :, :, :]], axis=-5)


def shrink(f, ring):
    return f[..., ring:f.shape[-2] - ring, ring:f.shape[-1] - ring]


def pad_z(f):
    return jnp.pad(f, [(0, 0)] * (f.ndim - 3) + [(1, 1), (0, 0), (0, 0)])


def swap_rounds(axis):
    count = lax.axis_size(axis)
    even = lax.axis_index(axis) % 2 == 0
    for first in (0, 1):
        pairs = []
        for i in range(first, count - 1, 2):
            pairs += [(i, i + 1), (i + 1, i)]
        if pairs:
            yield pairs, even == (first == 0)


def halo_faces(cells, axis, dim, width):
    count = lax.axis_size(axis)
    size = cells.shape[dim]
    head = lax.slice_in_dim(cells, 0, width, axis=dim)
    tail = lax.slice_in_dim(cells, size - width, size, axis=dim)
    if count == 2:
        got = row_major(lax.ppermute(row_major(jnp.where(lax.axis_index(axis) == 0, tail, head)), axis, [(0, 1), (1, 0)]))
        return got, got
    even = lax.axis_index(axis) % 2 == 0
    from_low = jnp.zeros_like(tail)
    from_high = jnp.zeros_like(head)
    for first in (0, 1):
        pairs = []
        for i in range(first, count - 1, 2):
            pairs += [(i, i + 1), (i + 1, i)]
        lower_is_even = first == 0
        send = row_major(jnp.where(even == lower_is_even, tail, head))
        got = row_major(lax.ppermute(send, axis, pairs))
        from_high = jnp.where(even == lower_is_even, got, from_high)
        from_low = jnp.where(even == lower_is_even, from_low, got)
    return from_low, from_high


def halo(cells, axis, dim, width):
    count = lax.axis_size(axis)
    size = cells.shape[dim]
    head = lax.slice_in_dim(cells, 0, width, axis=dim)
    tail = lax.slice_in_dim(cells, size - width, size, axis=dim)
    even = lax.axis_index(axis) % 2 == 0
    from_low = jnp.zeros_like(tail)
    from_high = jnp.zeros_like(head)
    for first in (0, 1):
        pairs = []
        for i in range(first, count - 1, 2):
            pairs += [(i, i + 1), (i + 1, i)]
        if not pairs:
            continue
        lower_is_even = first == 0
        send = row_major(jnp.where(even == lower_is_even, tail, head))
        got = row_major(lax.ppermute(send, axis, pairs))
        from_high = jnp.where(even == lower_is_even, got, from_high)
        from_low = jnp.where(even == lower_is_even, from_low, got)
    return jnp.concatenate([from_low, cells, from_high], axis=dim)


def row_major(x):
    return with_layout_constraint(x, Layout(major_to_minor=tuple(range(x.ndim))))


def sweep_all(shot_ext, sigma_ext, inside, outer):
    kappa = K_FREQ * sigma_ext
    delta = K_FREQ * (sigma_ext - 1.0)
    rhs = source_term(shot_ext, delta)
    field = jnp.where(inside, jnp.where(outer, shot_ext, jacobi(rhs, kappa)), 0.0)
    for sweep in range(SWEEPS):
        curled = curl_curl(pad_z(field))
        field = shrink(field, 1)
        kappa = shrink(kappa, 1)
        rhs = shrink(rhs, 1)
        inside = shrink(inside, 1)
        real_part = curled[..., 0, :, :, :, :] - kappa * field[..., 1, :, :, :, :]
        imag_part = curled[..., 1, :, :, :, :] + kappa * field[..., 0, :, :, :, :]
        applied = jnp.stack([real_part, imag_part], axis=-5)
        field = field + RELAX * jacobi(rhs - applied, kappa)
        if sweep < SWEEPS - 1:
            field = jnp.where(inside, field, 0.0)
    return field


def rolled_sweeps(shot_ext, sigma_ext, inside, outer, rows, lanes):
    def nxt(f, axis):
        return pltpu.roll(f, (lanes if axis == -1 else rows) - 1, axis=f.ndim + axis)

    def prv(f, axis):
        return pltpu.roll(f, 1, axis=f.ndim + axis)

    def curl(field):
        padded = pad_z(field)
        above = padded[..., 1:, :, :]
        here = padded[..., :-1, :, :]

        def dz(c):
            return above[..., c, :, :, :] - here[..., c, :, :, :]

        def dx(c):
            return nxt(here[..., c, :, :, :], -2) - here[..., c, :, :, :]

        def dy(c):
            return nxt(here[..., c, :, :, :], -1) - here[..., c, :, :, :]

        h_x = dy(2) - dz(1)
        h_y = dz(0) - dx(2)
        h_z = dx(1) - dy(0)

        def bz(g):
            return g[..., 1:, :, :] - g[..., :-1, :, :]

        def bx(g):
            return g[..., 1:, :, :] - prv(g[..., 1:, :, :], -2)

        def by(g):
            return g[..., 1:, :, :] - prv(g[..., 1:, :, :], -1)

        c_x = by(h_z) - bz(h_y)
        c_y = bz(h_x) - bx(h_z)
        c_z = bx(h_y) - by(h_x)
        return jnp.stack([c_x, c_y, c_z], axis=-4)

    kappa = K_FREQ * sigma_ext
    delta = K_FREQ * (sigma_ext - 1.0)
    rhs = source_term(shot_ext, delta)
    field = jnp.where(inside, jnp.where(outer, shot_ext, jacobi(rhs, kappa)), 0.0)
    for sweep in range(SWEEPS):
        curled = curl(field)
        real_part = curled[..., 0, :, :, :, :] - kappa * field[..., 1, :, :, :, :]
        imag_part = curled[..., 1, :, :, :, :] + kappa * field[..., 0, :, :, :, :]
        applied = jnp.stack([real_part, imag_part], axis=-5)
        field = field + RELAX * jacobi(rhs - applied, kappa)
        if sweep < SWEEPS - 1:
            field = jnp.where(inside, field, 0.0)
    return field


def encode_weights(group_part, sign_part, rows):
    picked = group_part[None, :] == rows[:, None]
    return jnp.where(picked, sign_part[None, :], 0).astype(jnp.float32).astype(jnp.bfloat16)


def body(primaries, conductivity, group_of, sign_of):
    nt_local = primaries.shape[0]
    depth = primaries.shape[3]
    width_x = primaries.shape[4]
    width_y = primaries.shape[5]
    n_tx = lax.axis_size("tx")
    tx_index = lax.axis_index("tx")
    other = (tx_index + 1) % n_tx
    mine = lax.broadcasted_iota(jnp.int32, (n_tx, nt_local), 0) == tx_index
    own_groups = jnp.sum(jnp.where(mine, group_of.reshape(n_tx, nt_local), 0), axis=0)
    own_signs = jnp.sum(jnp.where(mine, sign_of.reshape(n_tx, nt_local), 0), axis=0)
    rows = jnp.stack([other, tx_index]).astype(jnp.int32)
    weights = encode_weights(own_groups, own_signs, rows)
    partial = lax.dot_general(
        weights, primaries, (((1,), (0,)), ((), ())), preferred_element_type=jnp.float32
    )
    tx_ring = [(i, (i + 1) % n_tx) for i in range(n_tx)]
    got = lax.ppermute(partial[0], "tx", tx_ring)
    sigma_other = lax.ppermute(conductivity, "tx", tx_ring)
    shot_planes = partial.shape[1] * partial.shape[2] * depth
    ext_x = width_x + 2 * SWEEPS
    ext_y = width_y + 2 * SWEEPS
    w = SWEEPS
    x_rounds = list(swap_rounds("xb"))
    y_rounds = list(swap_rounds("yb"))
    n_x = len(x_rounds)
    n_y = len(y_rounds)
    flags = jnp.stack(
        [(tx_index == 0).astype(jnp.int32), (lax.axis_index("xb") % 2 == 0).astype(jnp.int32)]
        + [lower.astype(jnp.int32) for _, lower in x_rounds]
        + [lower.astype(jnp.int32) for _, lower in y_rounds]
    )
    pieces = (partial[1], got, conductivity, sigma_other)
    n_planes = shot_planes + 2 * conductivity.shape[0] * conductivity.shape[1]
    vmem = pl.BlockSpec(memory_space=pltpu.VMEM)
    smem = pl.BlockSpec(memory_space=pltpu.SMEM)

    def planes_of(flags_ref, own_ref, got_ref, sigma_ref, other_ref):
        shot = (own_ref[...] + got_ref[...]).reshape(shot_planes, width_x, width_y)
        mine = sigma_ref[...]
        theirs = other_ref[...]
        sigma = jnp.where(
            flags_ref[0] == 1,
            jnp.concatenate([mine, theirs], axis=1),
            jnp.concatenate([theirs, mine], axis=1),
        ).reshape(-1, width_x, width_y)
        return jnp.concatenate([shot, sigma], axis=0)

    row_shot = primaries.shape[1:3] + (depth, 1, width_y)
    payload_planes = n_planes * (w - 1) + shot_planes

    def field0_row(row):
        shot = row[:shot_planes].reshape(row_shot)
        sigma = row[shot_planes:].reshape(-1, depth, 1, width_y)
        rhs = source_term(shot, K_FREQ * (sigma - 1.0))
        return jacobi(rhs, K_FREQ * sigma).reshape(shot_planes, 1, width_y)

    def send_kernel(flags_ref, own_ref, got_ref, sigma_ref, other_ref, *send_refs):
        cells = planes_of(flags_ref, own_ref, got_ref, sigma_ref, other_ref)

        def payload(inner_rows, outer_row):
            parts = [cells[:, r, :] for r in inner_rows]
            parts.append(field0_row(cells[:, outer_row:outer_row + 1]).reshape(shot_planes, width_y))
            return jnp.concatenate(parts, axis=0)

        head = payload(range(0, w - 1), w - 1)
        tail = payload(range(width_x - w + 1, width_x), width_x - w)
        for k in range(n_x):
            send_refs[k][...] = jnp.where(flags_ref[2 + k] == 1, tail, head)

    x_sends = pl.pallas_call(
        send_kernel,
        out_shape=[jax.ShapeDtypeStruct((payload_planes, width_y), jnp.float32)] * n_x,
        in_specs=[smem] + [vmem] * 4,
        out_specs=[vmem] * n_x,
    )(flags, *pieces)
    x_gots = [
        row_major(lax.ppermute(row_major(send), "xb", pairs))
        for send, (pairs, _) in zip(x_sends, x_rounds)
    ]
    face_shape = (w, n_planes * ext_x)

    def decode(payload, outer_first):
        inner = [payload[k * n_planes:(k + 1) * n_planes].reshape(n_planes, 1, width_y) for k in range(w - 1)]
        field0 = payload[n_planes * (w - 1):].reshape(shot_planes, 1, width_y)
        filler = jnp.zeros((n_planes - shot_planes, 1, width_y), payload.dtype)
        outer = jnp.concatenate([field0, filler], axis=0)
        return jnp.concatenate([outer] + inner if outer_first else inner + [outer], axis=1)

    def x_cells(flags_ref, own_ref, got_ref, sigma_ref, other_ref, got_refs):
        if n_x == 1:
            low = high = got_refs[0][...]
        else:
            even = flags_ref[1] == 1
            high = jnp.where(even, got_refs[0][...], got_refs[1][...])
            low = jnp.where(even, got_refs[1][...], got_refs[0][...])
        low = decode(low, True)
        high = decode(high, False)
        middle = planes_of(flags_ref, own_ref, got_ref, sigma_ref, other_ref)
        return jnp.concatenate([low, middle, high], axis=1)

    def x_kernel(flags_ref, own_ref, got_ref, sigma_ref, other_ref, *refs):
        got_refs = refs[:n_x]
        send_refs = refs[n_x:]
        cells = x_cells(flags_ref, own_ref, got_ref, sigma_ref, other_ref, got_refs)
        columns = cells.reshape(n_planes * ext_x, width_y).T
        head = columns[:w]
        tail = columns[width_y - w:]
        for k in range(n_y):
            send_refs[k][...] = jnp.where(flags_ref[2 + n_x + k] == 1, tail, head)

    y_sends = pl.pallas_call(
        x_kernel,
        out_shape=[jax.ShapeDtypeStruct(face_shape, jnp.float32)] * n_y,
        in_specs=[smem] + [vmem] * (4 + n_x),
        out_specs=[vmem] * n_y,
    )(flags, *pieces, *x_gots)
    y_gots = [
        row_major(lax.ppermute(row_major(send), "yb", pairs))
        for send, (pairs, _) in zip(y_sends, y_rounds)
    ]
    if n_y == 1:
        y_low = y_high = y_gots[0]
    else:
        even_y = lax.axis_index("yb") % 2 == 0
        y_high = jnp.where(even_y, y_gots[0], y_gots[1])
        y_low = jnp.where(even_y, y_gots[1], y_gots[0])
    lanes = 2 * width_y
    gx = lax.axis_index("xb") * width_x - SWEEPS + lax.broadcasted_iota(jnp.int32, (ext_x, lanes), 0)
    lane = lax.broadcasted_iota(jnp.int32, (ext_x, lanes), 1)
    local_y = jnp.where(lane >= lanes - SWEEPS, lane - lanes, lane)
    gy = lax.axis_index("yb") * width_y + local_y
    inside = (gx >= 0) & (gx < width_x * lax.axis_size("xb")) & (gy >= 0) & (gy < width_y * lax.axis_size("yb"))
    inside = inside & (local_y < width_y + SWEEPS)
    shot_shape = primaries.shape[1:3]
    out_shape = shot_shape + (depth, width_x, width_y)

    def unflip(face):
        filler = jnp.zeros((width_y - w, face.shape[1]), face.dtype)
        back = jnp.concatenate([face, filler], axis=0).T.reshape(n_planes, ext_x, width_y)
        return back[:, :, :w]

    def sweeps_kernel(flags_ref, own_ref, got_ref, sigma_ref, other_ref, *refs):
        got_refs = refs[:n_x]
        low_ref, high_ref, inside_ref, out_ref = refs[n_x:]
        cells = x_cells(flags_ref, own_ref, got_ref, sigma_ref, other_ref, got_refs)
        gap = jnp.zeros((lanes - width_y - 2 * w, n_planes * ext_x), jnp.float32)
        upper = jnp.concatenate([high_ref[...], gap, low_ref[...]], axis=0)
        upper = upper.T.reshape(n_planes, ext_x, lanes - width_y)
        ext = jnp.concatenate([cells, upper], axis=2)
        shot_ext = ext[:shot_planes].reshape(shot_shape + (depth, ext_x, lanes))
        sigma_ext = ext[shot_planes:].reshape(-1, depth, ext_x, lanes)
        keep = inside_ref[...] > 0.5
        row = lax.broadcasted_iota(jnp.int32, (ext_x, lanes), 0)
        outer = (row == 0) | (row == ext_x - 1)
        field = rolled_sweeps(shot_ext, sigma_ext, keep, outer, ext_x, lanes)
        out_ref[...] = field[..., w:w + width_x, :width_y]

    field = pl.pallas_call(
        sweeps_kernel,
        out_shape=jax.ShapeDtypeStruct(out_shape, jnp.float32),
        in_specs=[smem] + [vmem] * (4 + n_x + 3),
        out_specs=vmem,
    )(flags, *pieces, *x_gots, y_low, y_high, inside.astype(jnp.float32))
    return field[None]


def solution(mesh):
    in_specs = (
        P(("survey", "tx"), None, None, None, "xb", "yb"),
        P("survey", "tx", "xb", "yb"),
        P("survey"),
        P("survey"),
    )
    out_specs = P(("survey", "tx"), None, None, None, "xb", "yb")
    return jax.shard_map(body, mesh=mesh, in_specs=in_specs, out_specs=out_specs, check_vma=False)
```
